128 devices in a mesh: req: 32 (over x, z, core), head: 4 (over y).
Axes of the slice: x: 4, y: 4, z: 4, core: 2. Of those that a mesh axis runs over, the one named last changes fastest.
Arguments:
- tokens: bfloat16 [32768, 1536], P(('req', 'head')), may hold values from -6 to 6
- norm1_gain: float32 [1536], replicated, may hold values from 0.1 to 1.9
- query_key_value_weight: bfloat16 [1536, 2048], replicated, may hold values from -0.15625 to 0.15625
- w_out: bfloat16 [1536, 1536], replicated, may hold values from -0.15625 to 0.15625
- norm2_gain: float32 [1536], replicated, may hold values from 0.1 to 1.9
- router_weight: float32 [1536, 32], replicated, may hold values from -0.078125 to 0.078125
- w_gate_up: bfloat16 [32, 1536, 1536], P('req'), may hold values from -0.15625 to 0.15625
- w_down: bfloat16 [32, 768, 1536], P('req'), may hold values from -0.21875 to 0.21875
- routes: int32 [32768, 4], P(('req', 'head')), may hold values from 0 to 31, all different within a row; in each aligned block of 256 rows (0 to 255, 256 to 511, ...) at most 48 rows name the same one
- key_page_store: bfloat16 [1024, 128, 256], P('req'), may hold values from -100 to 100
- value_page_store: bfloat16 [1024, 128, 256], P('req'), may hold values from -6 to 6
- page_table: int32 [64, 16], P('req'), may hold values from 0 to 31, as said below
- cached_pages: int32 [64], replicated, may hold values from 0 to 16
- anchor: int32 [64], replicated, may hold values from 0 to 63, as said below
Outputs:
- mixed: bfloat16 [32768, 1536], P(('req', 'head'))
- appended: bfloat16 [32768, 512], P(('req', 'head'))
The draws below stay inside these ranges and needn't reach their ends.
Inputs may be any that keep to these rules, and one draw needn't show every extreme that they name: `page_table`: row o lists the pages of request o of the previous placement, as page numbers of the pool of index o // 2 of req; the rows of one index of req use distinct pages; entries past cached_pages[o] are not part of the cache. A permutation. Either anchor[i] = i, or request i and request anchor[i] lie on two indices of req that differ only in the lowest bit and trade places with each other; an index of req gives and takes at most one request.
All inputs are finite; a program needn't handle non-finite values.
Results may differ from the reference program's by a relative error of at most 0.011.
Values may be sent and summed in bfloat16 or wider, within the bound.
No kernel may reach another device: no remote copies, remote signals or barrier semaphores. Data moves between devices by JAX's collectives and lax.ppermute only.
A program may use at most 128 MiB of HBM per device.

```python
import math
import jax
import jax.numpy as jnp
import numpy as np
from jax import lax

MODEL_WIDTH = 1536
QUERY_HEADS = 12
KEY_VALUE_HEADS = 2
HEAD_SIZE = 128
FE = 768
TOPK = 4
NE = 32
REQ_DEV = 2
REQUEST_TOKENS = 512
PAGE_TOKENS = 128
MAXP = 16
REQS = 64
TOK_DEV = 256
NEW_TOKEN_COUNT = 32768
POOL_DEV = 32
TOTAL_PAGES = 1024
CAP = 48
N_REQ = 32
N_HEAD = 4


def layout_parts(key):
    key_rows = jax.random.split(jax.random.fold_in(key, 41), 8)
    first_draw = jax.random.randint(key_rows[0], (REQS,), 0, MAXP + 1)
    second_draw = jax.random.randint(key_rows[1], (REQS,), 0, MAXP + 1)
    longest = jax.random.randint(key_rows[2], (), 0, REQS)
    pair_count = REQS // (2 * REQ_DEV)
    trades = jax.random.randint(key_rows[3], (pair_count,), 0, 2).at[0].set(1)
    left_pick = jax.random.randint(key_rows[4], (pair_count,), 0, REQ_DEV)
    right_pick = jax.random.randint(key_rows[5], (pair_count,), 0, REQ_DEV)
    pair_ids = jnp.arange(pair_count, dtype=jnp.int32)
    left_slot = (2 * pair_ids * REQ_DEV + left_pick).astype(jnp.int32)
    right_slot = ((2 * pair_ids + 1) * REQ_DEV + right_pick).astype(jnp.int32)
    cached = (first_draw * second_draw // MAXP).at[longest].set(MAXP)
    cached = cached.at[left_slot[0]].set(MAXP).at[right_slot[0]].set(MAXP).astype(jnp.int32)
    anchor = jnp.arange(REQS, dtype=jnp.int32)
    anchor = anchor.at[left_slot].set(jnp.where(trades == 1, right_slot, left_slot))
    anchor = anchor.at[right_slot].set(jnp.where(trades == 1, left_slot, right_slot))
    device_keys = jax.random.split(key_rows[7], REQS // REQ_DEV)
    table = jax.vmap(lambda one_key: jax.random.permutation(one_key, REQ_DEV * MAXP))(device_keys)
    table = table.reshape(REQS, MAXP).astype(jnp.int32)
    return (cached, anchor, table)


def draw_cached_pages(key, part):
    return layout_parts(key)[0]


def draw_anchor(key, part):
    return layout_parts(key)[1]


def draw_page_table(key, part):
    return layout_parts(key)[2]


def draw_key_page_store(key, part):
    full_shape = (TOTAL_PAGES, PAGE_TOKENS, KEY_VALUE_HEADS * HEAD_SIZE)
    key_rows = jax.random.split(jax.random.fold_in(key, 43), 1)
    drawn = jnp.clip(jax.random.normal(key_rows[0], full_shape, jnp.float32), -6.0, 6.0)
    return drawn.astype(jnp.bfloat16)


def block_levels(key, extent, cuts, low, high):
    def one(dim, shards_of):
        steps = jax.random.uniform(jax.random.fold_in(jax.random.fold_in(key, 6), dim), (shards_of,), jnp.float32, low / len(cuts), high / len(cuts))
        return jnp.repeat(jnp.exp(steps), extent[dim] // shards_of).reshape((-1,) + (1,) * (len(extent) - dim - 1))

    gain = one(*cuts[0])
    for cut in cuts[1:]:
        gain = gain * one(*cut)
    return gain


def routed_block(key, own, number, rows, number_of, top, limit, skew):
    sequence = jax.random.permutation(key, number_of)
    packed, ordinary = load_shares(number_of, rows * top, limit, skew, True), load_shares(number_of, rows * top, limit, skew, False)
    places = jnp.arange(number_of)

    def named(lengths, offset_by):
        used = int((lengths > 0).sum())
        fixed = max(1, used // 4)
        passed = fixed + (places - fixed + offset_by * (used - fixed)) % max(1, number_of - fixed)
        return jnp.zeros((number_of,), jnp.int32).at[sequence[jnp.where(places < fixed, places, passed)]].set(jnp.asarray(lengths, jnp.int32))

    lengths = jnp.where(number % 4 == 0, named(packed, number // 4), named(ordinary, number - number // 4 - 1))
    mixed = jax.random.permutation(jax.random.fold_in(own, 3), number_of)
    giver, taker = mixed[0:number_of // 2 * 2:2], mixed[1:number_of // 2 * 2:2]
    room = jnp.minimum(lengths[giver] - 1, limit - lengths[taker]) // 2
    room = jnp.where((giver == sequence[0]) | (taker == sequence[0]) | (lengths[taker] == 0), 0, jnp.maximum(room, 0))
    passed = jax.random.randint(jax.random.fold_in(own, 4), (number_of // 2,), 0, 1 << 20) % (room + 1)
    lengths = lengths.at[giver].add(-passed).at[taker].add(passed)
    labels = jnp.searchsorted(jnp.cumsum(lengths), jnp.arange(rows * top), side="right").astype(jnp.int32)
    table = labels.reshape(top, rows).T
    table = table[jax.random.permutation(jax.random.fold_in(own, 1), rows)]
    offset_by = jax.random.randint(jax.random.fold_in(own, 2), (rows, 1), 0, top)
    return jnp.take_along_axis(table, (jnp.arange(top)[None, :] + offset_by) % top, axis=1)


def load_shares(number_of, total, most, skew, full):
    loads = [(1 << 20) // math.isqrt(rank ** skew) + 1 for rank in range(1, number_of + 1)]
    largest = most if full else min(most, max(-(-total // number_of), total * loads[0] // sum(loads)))
    least = 1 if total - largest >= number_of - 1 else 0
    given, rest = [largest] + [least] * (number_of - 1), total - largest - least * (number_of - 1)
    while rest > 0:
        free = [i for i in range(1, number_of) if given[i] < largest] or [i for i in range(1, number_of) if given[i] < most]
        whole, remaining = sum([loads[i] for i in free]), rest
        for i in free:
            more = min(most - given[i], max(1, remaining * loads[i] // whole), rest)
            given[i] = given[i] + more
            rest = rest - more
    return np.array(given)


def scatter_about(rng, extent, deviation, limit, shards=(), held_as=jnp.bfloat16):
    array = deviation * jax.random.normal(rng, extent, jnp.float32)
    if shards:
        array = array * block_levels(rng, extent, shards, -0.22, 0.18)
    return jnp.clip(array, -limit, limit).astype(held_as)


def setup_inputs(seed: int = 0) -> dict:
    arg_keys = jax.random.split(jax.random.key(seed), 15)
    tokens = scatter_about(arg_keys[0], (NEW_TOKEN_COUNT, MODEL_WIDTH), 1.0, 6.0, ((0, 128),))
    norm1_gain = jnp.clip(1.0 + 0.18 * jax.random.normal(arg_keys[1], (MODEL_WIDTH,), jnp.float32), 0.1, 1.9)
    query_key_value_weight = scatter_about(arg_keys[2], (MODEL_WIDTH, (QUERY_HEADS + 2 * KEY_VALUE_HEADS) * HEAD_SIZE), MODEL_WIDTH ** -0.5, 0.15625)
    w_out = scatter_about(arg_keys[3], (QUERY_HEADS * HEAD_SIZE, MODEL_WIDTH), (QUERY_HEADS * HEAD_SIZE) ** -0.5, 0.15625)
    norm2_gain = jnp.clip(1.0 + 0.18 * jax.random.normal(arg_keys[4], (MODEL_WIDTH,), jnp.float32), 0.1, 1.9)
    router_weight = scatter_about(arg_keys[5], (MODEL_WIDTH, NE), (4 * MODEL_WIDTH) ** -0.5, 0.078125, (), jnp.float32)
    w_gate_up = scatter_about(arg_keys[6], (NE, MODEL_WIDTH, 2 * FE), MODEL_WIDTH ** -0.5, 0.15625, ((0, 32),))
    w_down = scatter_about(arg_keys[7], (NE, FE, MODEL_WIDTH), FE ** -0.5, 0.21875, ((0, 32),))
    routes_keys = jax.random.split(jax.random.fold_in(arg_keys[8], 1), NEW_TOKEN_COUNT // TOK_DEV)
    routes_turns = jax.random.permutation(jax.random.fold_in(arg_keys[8], 3), NEW_TOKEN_COUNT // TOK_DEV)
    routes = jax.vmap(lambda own, number: routed_block(jax.random.fold_in(arg_keys[8], 2), own, number, TOK_DEV, NE, TOPK, CAP, 2))(routes_keys, routes_turns).reshape((NEW_TOKEN_COUNT, TOPK))
    key_page_store = draw_key_page_store(jax.random.fold_in(arg_keys[14], 71), 0)
    value_page_store = scatter_about(arg_keys[10], (TOTAL_PAGES, PAGE_TOKENS, KEY_VALUE_HEADS * HEAD_SIZE), 1.0, 6.0, ((0, 32),))
    page_table = draw_page_table(jax.random.fold_in(arg_keys[14], 71), 0)
    cached_pages = draw_cached_pages(jax.random.fold_in(arg_keys[14], 71), 0)
    anchor = draw_anchor(jax.random.fold_in(arg_keys[14], 71), 0)
    return {"tokens": tokens, "norm1_gain": norm1_gain, "query_key_value_weight": query_key_value_weight, "w_out": w_out, "norm2_gain": norm2_gain, "router_weight": router_weight, "w_gate_up": w_gate_up, "w_down": w_down, "routes": routes, "key_page_store": key_page_store, "value_page_store": value_page_store, "page_table": page_table, "cached_pages": cached_pages, "anchor": anchor}


EPS = 1e-06
THETA = 1000000.0

def rms_scale(values, gain_vector):
    mean_sq = lax.optimization_barrier(jnp.mean(values * values, axis=-1, keepdims=True))
    return values * lax.rsqrt(mean_sq + EPS) * gain_vector

def apply_rotary(values, where_at):
    half_dim = values.shape[-1] // 2
    frequency = jnp.exp(-jnp.log(jnp.float32(THETA)) * jnp.arange(half_dim, dtype=jnp.float32) * 2.0 / values.shape[-1])
    angles = where_at.astype(jnp.float32)[:, None] * frequency[None, :]
    cosine = jnp.cos(angles)[:, None, :]
    sines = jnp.sin(angles)[:, None, :]
    first_half = values[..., :half_dim]
    second = values[..., half_dim:]
    return jnp.concatenate([first_half * cosine - second * sines, second * cosine + first_half * sines], axis=-1)

def reference(tokens, norm1_gain, query_key_value_weight, w_out, norm2_gain, router_weight, w_gate_up, w_down, routes, key_page_store, value_page_store, page_table, cached_pages, anchor):
    row_ids = jnp.arange(NEW_TOKEN_COUNT, dtype=jnp.int32)
    request_of = row_ids // REQUEST_TOKENS
    token_positions = cached_pages[anchor[request_of]] * PAGE_TOKENS + row_ids % REQUEST_TOKENS
    normed = rms_scale(tokens.astype(jnp.float32), norm1_gain).astype(jnp.bfloat16)
    projected_rows = jnp.dot(normed, query_key_value_weight, preferred_element_type=jnp.float32)
    q_all = apply_rotary(projected_rows[:, :QUERY_HEADS * HEAD_SIZE].reshape(NEW_TOKEN_COUNT, QUERY_HEADS, HEAD_SIZE), token_positions).astype(jnp.bfloat16)
    every_key = apply_rotary(projected_rows[:, QUERY_HEADS * HEAD_SIZE:(QUERY_HEADS + KEY_VALUE_HEADS) * HEAD_SIZE].reshape(NEW_TOKEN_COUNT, KEY_VALUE_HEADS, HEAD_SIZE), token_positions).astype(jnp.bfloat16)
    every_value = projected_rows[:, (QUERY_HEADS + KEY_VALUE_HEADS) * HEAD_SIZE:].astype(jnp.bfloat16)
    appended = jnp.concatenate([every_key.reshape(NEW_TOKEN_COUNT, KEY_VALUE_HEADS * HEAD_SIZE), every_value], axis=1)
    value_heads = every_value.reshape(NEW_TOKEN_COUNT, KEY_VALUE_HEADS, HEAD_SIZE)
    cache_length = MAXP * PAGE_TOKENS
    group_width = QUERY_HEADS // KEY_VALUE_HEADS

    def one_request(request_id):
        old_id = anchor[request_id]
        cached_len = cached_pages[old_id] * PAGE_TOKENS
        page_numbers = old_id // REQ_DEV * POOL_DEV + page_table[old_id]
        cached_key_rows = key_page_store[page_numbers].reshape(cache_length, KEY_VALUE_HEADS, HEAD_SIZE)
        cached_value_rows = value_page_store[page_numbers].reshape(cache_length, KEY_VALUE_HEADS, HEAD_SIZE)
        start_row = (request_id * REQUEST_TOKENS).astype(jnp.int32)
        fresh_queries = lax.dynamic_slice_in_dim(q_all, start_row, REQUEST_TOKENS, 0)
        new_keys = lax.dynamic_slice_in_dim(every_key, start_row, REQUEST_TOKENS, 0)
        new_values = lax.dynamic_slice_in_dim(value_heads, start_row, REQUEST_TOKENS, 0)
        all_keys = jnp.concatenate([cached_key_rows, new_keys], axis=0).astype(jnp.float32)
        all_values = jnp.concatenate([cached_value_rows, new_values], axis=0).astype(jnp.float32)
        key_ids = jnp.arange(cache_length + REQUEST_TOKENS, dtype=jnp.int32)
        span_pos = jnp.arange(REQUEST_TOKENS, dtype=jnp.int32)
        visible = jnp.where(key_ids[None, :] < cache_length, key_ids[None, :] < cached_len, key_ids[None, :] - cache_length <= span_pos[:, None])
        grouped_queries = fresh_queries.astype(jnp.float32).reshape(REQUEST_TOKENS, KEY_VALUE_HEADS, group_width, HEAD_SIZE)
        scores = jnp.einsum('tkgd,ckd->kgtc', grouped_queries, all_keys) * HEAD_SIZE ** (-0.5)
        scores = jnp.where(visible[None, None, :, :], scores, -jnp.inf)
        row_max = lax.optimization_barrier(jnp.max(scores, axis=-1, keepdims=True))
        weights = jnp.exp(scores - row_max)
        row_sums = lax.optimization_barrier(jnp.sum(weights, axis=-1))
        rounded = lax.optimization_barrier(weights.astype(jnp.bfloat16)).astype(jnp.float32)
        summed = jnp.einsum('kgtc,ckd->tkgd', rounded, all_values)
        result = summed / jnp.transpose(row_sums, (2, 0, 1))[..., None]
        return result.reshape(REQUEST_TOKENS, QUERY_HEADS * HEAD_SIZE).astype(jnp.bfloat16)
    attention = lax.map(one_request, jnp.arange(REQS, dtype=jnp.int32)).reshape(NEW_TOKEN_COUNT, QUERY_HEADS * HEAD_SIZE)
    residual = tokens.astype(jnp.float32) + jnp.dot(attention, w_out, preferred_element_type=jnp.float32)
    normed_moe = rms_scale(residual, norm2_gain).astype(jnp.bfloat16)
    logits = jnp.dot(normed_moe.astype(jnp.float32), router_weight, precision=lax.Precision.HIGHEST)
    chosen = jnp.take_along_axis(logits, routes, axis=1)
    sigmoids = jax.nn.sigmoid(chosen)
    route_gates = sigmoids / lax.optimization_barrier(jnp.sum(sigmoids, axis=1, keepdims=True))
    flat_ids = routes.reshape(-1)
    flat_gates = route_gates.reshape(-1)
    sorted_rows = jnp.argsort(flat_ids, stable=True).astype(jnp.int32)
    counts = lax.optimization_barrier(jnp.sum((flat_ids[None, :] == jnp.arange(NE, dtype=jnp.int32)[:, None]).astype(jnp.int32), axis=1))
    starts = (jnp.cumsum(counts) - counts).astype(jnp.int32)
    cap_total = CAP * N_REQ * N_HEAD
    padded_rows = jnp.concatenate([sorted_rows, jnp.zeros((cap_total,), jnp.int32)])

    def expert_step(accumulated, expert_id):
        picked_rows = lax.dynamic_slice_in_dim(padded_rows, starts[expert_id], cap_total, 0)
        valid = jnp.arange(cap_total, dtype=jnp.int32) < counts[expert_id]
        token_ids = picked_rows // TOPK
        inputs = normed_moe[token_ids]
        gate_up = jnp.dot(inputs, w_gate_up[expert_id], preferred_element_type=jnp.float32)
        hidden = (jax.nn.relu(gate_up[:, :FE]) * gate_up[:, FE:]).astype(jnp.bfloat16)
        outputs = jnp.dot(hidden, w_down[expert_id], preferred_element_type=jnp.float32).astype(jnp.bfloat16)
        contrib = jnp.where(valid[:, None], flat_gates[picked_rows][:, None] * outputs.astype(jnp.float32), 0.0)
        return (accumulated.at[token_ids].add(contrib), None)
    expert_sum, _ = lax.scan(expert_step, jnp.zeros((NEW_TOKEN_COUNT, MODEL_WIDTH), jnp.float32), jnp.arange(NE, dtype=jnp.int32))
    mixed = (residual + expert_sum).astype(jnp.bfloat16)
    return (mixed, appended)
```

```python
import functools

import jax
import jax.numpy as jnp
from jax import lax
from jax.experimental import pallas as pl
from jax.experimental.pallas import tpu as pltpu
from jax.sharding import PartitionSpec as P

MODEL_WIDTH = 1536
QUERY_HEADS = 12
KEY_VALUE_HEADS = 2
HEAD_SIZE = 128
FE = 768
TOPK = 4
REQUEST_TOKENS = 512


EPS = 1e-06
THETA = 1000000.0


def rms_scale(values, gain_vector):
    mean_sq = jnp.mean(values * values, axis=-1, keepdims=True)
    return values * lax.rsqrt(mean_sq + EPS) * gain_vector


def apply_rotary(values, where_at):
    half_dim = values.shape[-1] // 2
    frequency = jnp.exp(
        -jnp.log(jnp.float32(THETA))
        * jnp.arange(half_dim, dtype=jnp.float32)
        * 2.0
        / values.shape[-1]
    )
    angles = where_at.astype(jnp.float32)[:, None] * frequency[None, :]
    cosine = jnp.cos(angles)[:, None, :]
    sines = jnp.sin(angles)[:, None, :]
    first_half = values[..., :half_dim]
    second = values[..., half_dim:]
    return jnp.concatenate(
        [first_half * cosine - second * sines, second * cosine + first_half * sines], axis=-1
    )


def attention_kernel(
    meta_ref, page_ref, q_ref, kn_ref, vn_ref, kl_ref, vl_ref, kr_ref, vr_ref,
    o_ref, m_sc, l_sc, acc_sc, *, group, tokens
):
    j = pl.program_id(1)
    count = meta_ref[0]
    moved = meta_ref[1]
    half = meta_ref[2]
    scaling = HEAD_SIZE ** (-0.5)
    contract = (((1,), (1,)), ((), ()))

    def stacked_queries():
        q = q_ref[...]
        return jnp.concatenate(
            [q[:, g * HEAD_SIZE : (g + 1) * HEAD_SIZE] for g in range(group)], axis=0
        )

    @pl.when(j == 0)
    def _():
        qa = stacked_queries()
        s = lax.dot_general(qa, kn_ref[...], contract, preferred_element_type=jnp.float32)
        s = s * scaling
        rows = group * tokens
        t = lax.broadcasted_iota(jnp.int32, (group, tokens, s.shape[1]), 1).reshape(rows, -1)
        v = lax.broadcasted_iota(jnp.int32, s.shape, 1)
        s = jnp.where(v <= t + half * tokens, s, -jnp.inf)
        m = jnp.max(s, axis=1, keepdims=True)
        p = jnp.exp(s - m)
        l_sc[...] = jnp.sum(p, axis=1, keepdims=True)
        m_sc[...] = m
        acc_sc[...] = jnp.dot(
            p.astype(jnp.bfloat16), vn_ref[...], preferred_element_type=jnp.float32
        )

    @pl.when((j > 0) & (j - 1 < count))
    def _():
        qa = stacked_queries()
        k = jnp.where(moved == 1, kr_ref[0], kl_ref[0])
        vv = jnp.where(moved == 1, vr_ref[0], vl_ref[0])
        s = lax.dot_general(qa, k, contract, preferred_element_type=jnp.float32) * scaling
        m_old = m_sc[...]
        m_new = jnp.maximum(m_old, jnp.max(s, axis=1, keepdims=True))
        factor = jnp.exp(m_old - m_new)
        p = jnp.exp(s - m_new)
        l_sc[...] = l_sc[...] * factor + jnp.sum(p, axis=1, keepdims=True)
        acc_sc[...] = acc_sc[...] * factor + jnp.dot(
            p.astype(jnp.bfloat16), vv, preferred_element_type=jnp.float32
        )
        m_sc[...] = m_new

    @pl.when(j == pl.num_programs(1) - 1)
    def _():
        res = acc_sc[...] / l_sc[...]
        o_ref[...] = jnp.concatenate(
            [res[g * tokens : (g + 1) * tokens] for g in range(group)], axis=1
        ).astype(jnp.bfloat16)


def attend(meta, page_ids, queries, new_keys, new_values, k_pool, v_pool, k_got, v_got):
    tokens = queries.shape[0]
    group = QUERY_HEADS // KEY_VALUE_HEADS
    width = group * HEAD_SIZE
    span = new_keys.shape[0]
    page_size = k_pool.shape[1]
    max_pages = page_ids.shape[0]

    def page_at(j, meta_ref):
        return jnp.maximum(jnp.minimum(j - 1, meta_ref[0] - 1), 0)

    def local_map(c, j, meta_ref, page_ref):
        return (page_ref[page_at(j, meta_ref)] * (1 - meta_ref[1]), 0, c)

    def got_map(c, j, meta_ref, page_ref):
        return (page_at(j, meta_ref) * meta_ref[1], 0, c)

    page_block = (1, page_size, HEAD_SIZE)
    grid_spec = pltpu.PrefetchScalarGridSpec(
        num_scalar_prefetch=2,
        grid=(KEY_VALUE_HEADS, max_pages + 1),
        in_specs=[
            pl.BlockSpec((tokens, width), lambda c, j, m, p: (0, c)),
            pl.BlockSpec((span, HEAD_SIZE), lambda c, j, m, p: (0, c)),
            pl.BlockSpec((span, HEAD_SIZE), lambda c, j, m, p: (0, c)),
            pl.BlockSpec(page_block, local_map),
            pl.BlockSpec(page_block, local_map),
            pl.BlockSpec(page_block, got_map),
            pl.BlockSpec(page_block, got_map),
        ],
        out_specs=pl.BlockSpec((tokens, width), lambda c, j, m, p: (0, c)),
        scratch_shapes=[
            pltpu.VMEM((group * tokens, 1), jnp.float32),
            pltpu.VMEM((group * tokens, 1), jnp.float32),
            pltpu.VMEM((group * tokens, HEAD_SIZE), jnp.float32),
        ],
    )
    return pl.pallas_call(
        functools.partial(attention_kernel, group=group, tokens=tokens),
        grid_spec=grid_spec,
        out_shape=jax.ShapeDtypeStruct((tokens, QUERY_HEADS * HEAD_SIZE), jnp.bfloat16),
        compiler_params=pltpu.CompilerParams(dimension_semantics=("arbitrary", "arbitrary")),
    )(meta, page_ids, queries, new_keys, new_values, k_pool, v_pool, k_got, v_got)


def on_device(
    tokens,
    norm1_gain,
    query_key_value_weight,
    w_out,
    norm2_gain,
    router_weight,
    w_gate_up,
    w_down,
    routes,
    key_page_store,
    value_page_store,
    page_table,
    cached_pages,
    anchor,
):
    req_index = lax.axis_index("req")
    head_index = lax.axis_index("head")
    count_of_heads = lax.axis_size("head")
    req_count = lax.axis_size("req")
    tokens_per_device = tokens.shape[0]
    req_dev = page_table.shape[0]
    page_size = key_page_store.shape[1]
    share = REQUEST_TOKENS // tokens_per_device
    kv_width = KEY_VALUE_HEADS * HEAD_SIZE

    request = (req_index * count_of_heads + head_index) // share
    half = head_index % share
    slot = request % req_dev
    old_id = anchor[request]
    place = half * tokens_per_device + jnp.arange(tokens_per_device, dtype=jnp.int32)
    token_positions = cached_pages[old_id] * page_size + place

    normed = rms_scale(tokens.astype(jnp.float32), norm1_gain).astype(jnp.bfloat16)
    projected_rows = jnp.dot(normed, query_key_value_weight, preferred_element_type=jnp.float32)
    queries = apply_rotary(
        projected_rows[:, : QUERY_HEADS * HEAD_SIZE].reshape(
            tokens_per_device, QUERY_HEADS, HEAD_SIZE
        ),
        token_positions,
    ).astype(jnp.bfloat16)
    fresh_keys = apply_rotary(
        projected_rows[
            :, QUERY_HEADS * HEAD_SIZE : (QUERY_HEADS + KEY_VALUE_HEADS) * HEAD_SIZE
        ].reshape(tokens_per_device, KEY_VALUE_HEADS, HEAD_SIZE),
        token_positions,
    ).astype(jnp.bfloat16)
    fresh_values = projected_rows[:, (QUERY_HEADS + KEY_VALUE_HEADS) * HEAD_SIZE :].astype(
        jnp.bfloat16
    )
    appended = jnp.concatenate(
        [fresh_keys.reshape(tokens_per_device, kv_width), fresh_values], axis=1
    )

    forward_pairs = [
        (h, h + 1) for h in range(count_of_heads) if h % share != share - 1
    ]
    earlier = lax.ppermute(appended, "head", forward_pairs)
    is_second = half == 1
    span_rows = jnp.where(
        is_second,
        jnp.concatenate([earlier, appended], axis=0),
        jnp.concatenate([appended, earlier], axis=0),
    )
    new_keys = span_rows[:, :kv_width]
    new_values = span_rows[:, kv_width:]

    partner = req_index ^ 1
    partner_anchor = lax.dynamic_slice_in_dim(anchor, partner * req_dev, req_dev, 0)
    leaving = partner_anchor // req_dev == req_index
    out_row = jnp.sum(jnp.where(leaving, partner_anchor, 0)) % req_dev
    sent_pages = page_table[out_row]
    sent = (
        jnp.take(key_page_store, sent_pages, axis=0),
        jnp.take(value_page_store, sent_pages, axis=0),
    )
    pairs = [(source, source ^ 1) for source in range(req_count)]
    k_got, v_got = lax.ppermute(sent, "req", pairs)

    moved_in = (old_id // req_dev != req_index).astype(jnp.int32)
    page_ids = page_table[old_id % req_dev]
    meta = jnp.stack([cached_pages[old_id], moved_in, half.astype(jnp.int32)]).astype(jnp.int32)
    attention = attend(
        meta, page_ids, queries.reshape(tokens_per_device, QUERY_HEADS * HEAD_SIZE),
        new_keys, new_values, key_page_store, value_page_store, k_got, v_got,
    )
    del slot

    residual = tokens.astype(jnp.float32) + jnp.dot(
        attention, w_out, preferred_element_type=jnp.float32
    )
    normed_moe = rms_scale(residual, norm2_gain).astype(jnp.bfloat16)
    logits = jnp.dot(normed_moe.astype(jnp.float32), router_weight, precision=lax.Precision.HIGHEST)
    chosen = jnp.take_along_axis(logits, routes, axis=1)
    sigmoids = jax.nn.sigmoid(chosen)
    route_gates = sigmoids / jnp.sum(sigmoids, axis=1, keepdims=True)

    exp_dev = w_gate_up.shape[0]
    expert_total = exp_dev * req_count
    capacity = max(2, 3 * tokens_per_device * TOPK // (2 * expert_total))
    slot_total = expert_total * capacity
    flat_ids = routes.reshape(-1)
    route_rows = flat_ids.shape[0]
    one_hot = (flat_ids[:, None] == jnp.arange(expert_total, dtype=jnp.int32)[None, :]).astype(
        jnp.bfloat16
    )
    row_i = lax.broadcasted_iota(jnp.int32, (route_rows, route_rows), 0)
    col_i = lax.broadcasted_iota(jnp.int32, (route_rows, route_rows), 1)
    before = (col_i < row_i).astype(jnp.bfloat16)
    earlier_counts = jnp.dot(before, one_hot, preferred_element_type=jnp.float32)
    slot_ranks = jnp.sum(earlier_counts * one_hot.astype(jnp.float32), axis=1).astype(jnp.int32)
    slot_ids = (flat_ids * capacity + slot_ranks).reshape(tokens_per_device, TOPK)

    slot_iota = jnp.arange(slot_total, dtype=jnp.int32)
    hits = slot_ids[None, :, :] == slot_iota[:, None, None]
    gather_matrix = jnp.any(hits, axis=2).astype(jnp.bfloat16)
    dispatch = jnp.dot(gather_matrix, normed_moe, preferred_element_type=jnp.float32).astype(
        jnp.bfloat16
    )
    dispatch = dispatch.reshape(req_count, exp_dev, capacity, MODEL_WIDTH)
    gate_up = jnp.einsum(
        "nekd,edf->nekf",
        lax.all_to_all(dispatch, "req", split_axis=0, concat_axis=0, tiled=True),
        w_gate_up,
        preferred_element_type=jnp.float32,
    )
    hidden = (jax.nn.relu(gate_up[..., :FE]) * gate_up[..., FE:]).astype(jnp.bfloat16)
    result = jnp.einsum(
        "nekf,efd->nekd", hidden, w_down, preferred_element_type=jnp.float32
    ).astype(jnp.bfloat16)
    results = lax.all_to_all(result, "req", split_axis=0, concat_axis=0, tiled=True)
    flat_results = results.reshape(slot_total, MODEL_WIDTH)

    token_hits = slot_ids[:, :, None] == slot_iota[None, None, :]
    combine = jnp.sum(jnp.where(token_hits, route_gates[:, :, None], 0.0), axis=1)
    combine_hi = combine.astype(jnp.bfloat16)
    combine_lo = (combine - combine_hi.astype(jnp.float32)).astype(jnp.bfloat16)
    expert_sum = jnp.dot(combine_hi, flat_results, preferred_element_type=jnp.float32) + jnp.dot(
        combine_lo, flat_results, preferred_element_type=jnp.float32
    )
    mixed_out = (residual + expert_sum).astype(jnp.bfloat16)
    return (mixed_out, appended)


def solution(mesh):
    return jax.shard_map(
        on_device,
        mesh=mesh,
        in_specs=(
            P(("req", "head"), None),
            P(),
            P(),
            P(),
            P(),
            P(),
            P("req", None, None),
            P("req", None, None),
            P(("req", "head"), None),
            P("req", None, None),
            P("req", None, None),
            P("req", None),
            P(),
            P(),
        ),
        out_specs=(P(("req", "head"), None), P(("req", "head"), None)),
        check_vma=False,
    )
```

```python
import functools

import jax
import jax.numpy as jnp
from jax import lax
from jax.experimental import pallas as pl
from jax.experimental.pallas import tpu as pltpu
from jax.sharding import PartitionSpec as P

MODEL_WIDTH = 1536
QUERY_HEADS = 12
KEY_VALUE_HEADS = 2
HEAD_SIZE = 128
FE = 768
TOPK = 4
REQUEST_TOKENS = 512
PAGE_CHUNK = 128


EPS = 1e-06
THETA = 1000000.0


def rms_scale(values, gain_vector):
    mean_sq = jnp.mean(values * values, axis=-1, keepdims=True)
    return values * lax.rsqrt(mean_sq + EPS) * gain_vector


def apply_rotary(values, where_at):
    half_dim = values.shape[-1] // 2
    frequency = jnp.exp(
        -jnp.log(jnp.float32(THETA))
        * jnp.arange(half_dim, dtype=jnp.float32)
        * 2.0
        / values.shape[-1]
    )
    angles = where_at.astype(jnp.float32)[:, None] * frequency[None, :]
    cosine = jnp.cos(angles)[:, None, :]
    sines = jnp.sin(angles)[:, None, :]
    first_half = values[..., :half_dim]
    second = values[..., half_dim:]
    return jnp.concatenate(
        [first_half * cosine - second * sines, second * cosine + first_half * sines], axis=-1
    )


def attention_kernel(
    meta_ref, q_ref, kn_ref, vn_ref, k_ref, v_ref, o_ref, q_sc, m_sc, l_sc, acc_sc, *, group, tokens
):
    count = meta_ref[0]
    half = meta_ref[1]
    scaling = HEAD_SIZE ** (-0.5)
    contract = (((1,), (1,)), ((), ()))
    chunk = 2 * PAGE_CHUNK

    q = q_ref[...]
    q_sc[...] = jnp.concatenate(
        [q[:, g * HEAD_SIZE : (g + 1) * HEAD_SIZE] for g in range(group)], axis=0
    )
    s = lax.dot_general(q_sc[...], kn_ref[...], contract, preferred_element_type=jnp.float32)
    s = s * scaling
    rows = group * tokens
    t = lax.broadcasted_iota(jnp.int32, (group, tokens, s.shape[1]), 1).reshape(rows, -1)
    v = lax.broadcasted_iota(jnp.int32, s.shape, 1)
    s = jnp.where(v <= t + half * tokens, s, -jnp.inf)
    m = jnp.max(s, axis=1, keepdims=True)
    p = jnp.exp(s - m)
    l_sc[...] = jnp.sum(p, axis=1, keepdims=True)
    m_sc[...] = m
    acc_sc[...] = jnp.dot(p.astype(jnp.bfloat16), vn_ref[...], preferred_element_type=jnp.float32)
    limit = count * PAGE_CHUNK

    def visit(i, carry):
        first = pl.multiple_of(i * chunk, chunk)
        k = k_ref[pl.ds(first, chunk), :]
        vv = v_ref[pl.ds(first, chunk), :]
        s = lax.dot_general(q_sc[...], k, contract, preferred_element_type=jnp.float32) * scaling
        key_ids = first + lax.broadcasted_iota(jnp.int32, s.shape, 1)
        s = jnp.where(key_ids < limit, s, -jnp.inf)
        m_old = m_sc[...]
        m_new = jnp.maximum(m_old, jnp.max(s, axis=1, keepdims=True))
        factor = jnp.exp(m_old - m_new)
        p = jnp.exp(s - m_new)
        l_sc[...] = l_sc[...] * factor + jnp.sum(p, axis=1, keepdims=True)
        acc_sc[...] = acc_sc[...] * factor + jnp.dot(
            p.astype(jnp.bfloat16), vv, preferred_element_type=jnp.float32
        )
        m_sc[...] = m_new
        return carry

    lax.fori_loop(0, (count + 1) // 2, visit, 0)
    res = acc_sc[...] / l_sc[...]
    o_ref[...] = jnp.concatenate(
        [res[g * tokens : (g + 1) * tokens] for g in range(group)], axis=1
    ).astype(jnp.bfloat16)


def attend(meta, queries, new_keys, new_values, cache_keys, cache_values):
    tokens = queries.shape[0]
    group = QUERY_HEADS // KEY_VALUE_HEADS
    width = group * HEAD_SIZE
    span = new_keys.shape[0]
    cache_rows = cache_keys.shape[0]
    grid_spec = pltpu.PrefetchScalarGridSpec(
        num_scalar_prefetch=1,
        grid=(KEY_VALUE_HEADS,),
        in_specs=[
            pl.BlockSpec((tokens, width), lambda c, m: (0, c)),
            pl.BlockSpec((span, HEAD_SIZE), lambda c, m: (0, c)),
            pl.BlockSpec((span, HEAD_SIZE), lambda c, m: (0, c)),
            pl.BlockSpec((cache_rows, HEAD_SIZE), lambda c, m: (0, c)),
            pl.BlockSpec((cache_rows, HEAD_SIZE), lambda c, m: (0, c)),
        ],
        out_specs=pl.BlockSpec((tokens, width), lambda c, m: (0, c)),
        scratch_shapes=[
            pltpu.VMEM((group * tokens, HEAD_SIZE), jnp.bfloat16),
            pltpu.VMEM((group * tokens, 1), jnp.float32),
            pltpu.VMEM((group * tokens, 1), jnp.float32),
            pltpu.VMEM((group * tokens, HEAD_SIZE), jnp.float32),
        ],
    )
    return pl.pallas_call(
        functools.partial(attention_kernel, group=group, tokens=tokens),
        grid_spec=grid_spec,
        out_shape=jax.ShapeDtypeStruct((tokens, QUERY_HEADS * HEAD_SIZE), jnp.bfloat16),
        compiler_params=pltpu.CompilerParams(dimension_semantics=("arbitrary",)),
    )(meta, queries, new_keys, new_values, cache_keys, cache_values)


def on_device(
    tokens,
    norm1_gain,
    query_key_value_weight,
    w_out,
    norm2_gain,
    router_weight,
    w_gate_up,
    w_down,
    routes,
    key_page_store,
    value_page_store,
    page_table,
    cached_pages,
    anchor,
):
    req_index = lax.axis_index("req")
    head_index = lax.axis_index("head")
    count_of_heads = lax.axis_size("head")
    req_count = lax.axis_size("req")
    tokens_per_device = tokens.shape[0]
    req_dev = page_table.shape[0]
    page_size = key_page_store.shape[1]
    share = REQUEST_TOKENS // tokens_per_device
    kv_width = KEY_VALUE_HEADS * HEAD_SIZE

    request = (req_index * count_of_heads + head_index) // share
    half = head_index % share
    slot = request % req_dev
    old_id = anchor[request]
    place = half * tokens_per_device + jnp.arange(tokens_per_device, dtype=jnp.int32)
    token_positions = cached_pages[old_id] * page_size + place

    normed = rms_scale(tokens.astype(jnp.float32), norm1_gain).astype(jnp.bfloat16)
    projected_rows = jnp.dot(normed, query_key_value_weight, preferred_element_type=jnp.float32)
    queries = apply_rotary(
        projected_rows[:, : QUERY_HEADS * HEAD_SIZE].reshape(
            tokens_per_device, QUERY_HEADS, HEAD_SIZE
        ),
        token_positions,
    ).astype(jnp.bfloat16)
    fresh_keys = apply_rotary(
        projected_rows[
            :, QUERY_HEADS * HEAD_SIZE : (QUERY_HEADS + KEY_VALUE_HEADS) * HEAD_SIZE
        ].reshape(tokens_per_device, KEY_VALUE_HEADS, HEAD_SIZE),
        token_positions,
    ).astype(jnp.bfloat16)
    fresh_values = projected_rows[:, (QUERY_HEADS + KEY_VALUE_HEADS) * HEAD_SIZE :].astype(
        jnp.bfloat16
    )
    appended = jnp.concatenate(
        [fresh_keys.reshape(tokens_per_device, kv_width), fresh_values], axis=1
    )

    forward_pairs = [
        (h, h + 1) for h in range(count_of_heads) if h % share != share - 1
    ]
    earlier = lax.ppermute(appended, "head", forward_pairs)
    is_second = half == 1
    span_rows = jnp.where(
        is_second,
        jnp.concatenate([earlier, appended], axis=0),
        jnp.concatenate([appended, earlier], axis=0),
    )
    new_keys = span_rows[:, :kv_width]
    new_values = span_rows[:, kv_width:]

    partner = req_index ^ 1
    partner_anchor = lax.dynamic_slice_in_dim(anchor, partner * req_dev, req_dev, 0)
    leaving = partner_anchor // req_dev == req_index
    out_row = jnp.sum(jnp.where(leaving, partner_anchor, 0)) % req_dev
    sent_pages = page_table[out_row]
    sent = (
        jnp.take(key_page_store, sent_pages, axis=0),
        jnp.take(value_page_store, sent_pages, axis=0),
    )
    pairs = [(source, source ^ 1) for source in range(req_count)]
    k_got, v_got = lax.ppermute(sent, "req", pairs)

    moved_in = old_id // req_dev != req_index
    page_ids = page_table[old_id % req_dev]
    cache_rows = page_ids.shape[0] * page_size
    cache_keys = jnp.where(moved_in, k_got, jnp.take(key_page_store, page_ids, axis=0))
    cache_values = jnp.where(moved_in, v_got, jnp.take(value_page_store, page_ids, axis=0))
    meta = jnp.stack([cached_pages[old_id], half.astype(jnp.int32)]).astype(jnp.int32)
    attention = attend(
        meta, queries.reshape(tokens_per_device, QUERY_HEADS * HEAD_SIZE),
        new_keys, new_values,
        cache_keys.reshape(cache_rows, kv_width), cache_values.reshape(cache_rows, kv_width),
    )
    del slot

    residual = tokens.astype(jnp.float32) + jnp.dot(
        attention, w_out, preferred_element_type=jnp.float32
    )
    normed_moe = rms_scale(residual, norm2_gain).astype(jnp.bfloat16)
    logits = jnp.dot(normed_moe.astype(jnp.float32), router_weight, precision=lax.Precision.HIGHEST)
    route_match = routes[:, :, None] == jnp.arange(logits.shape[1], dtype=jnp.int32)[None, None, :]
    chosen = jnp.sum(jnp.where(route_match, logits[:, None, :], 0.0), axis=2)
    sigmoids = jax.nn.sigmoid(chosen)
    route_gates = sigmoids / jnp.sum(sigmoids, axis=1, keepdims=True)

    exp_dev = w_gate_up.shape[0]
    expert_total = exp_dev * req_count
    capacity = max(2, 3 * tokens_per_device * TOPK // (2 * expert_total))
    slot_total = expert_total * capacity
    flat_ids = routes.reshape(-1)
    route_rows = flat_ids.shape[0]
    one_hot = (flat_ids[:, None] == jnp.arange(expert_total, dtype=jnp.int32)[None, :]).astype(
        jnp.bfloat16
    )
    row_i = lax.broadcasted_iota(jnp.int32, (route_rows, route_rows), 0)
    col_i = lax.broadcasted_iota(jnp.int32, (route_rows, route_rows), 1)
    before = (col_i < row_i).astype(jnp.bfloat16)
    earlier_counts = jnp.dot(before, one_hot, preferred_element_type=jnp.float32)
    slot_ranks = jnp.sum(earlier_counts * one_hot.astype(jnp.float32), axis=1).astype(jnp.int32)
    slot_ids = (flat_ids * capacity + slot_ranks).reshape(tokens_per_device, TOPK)

    slot_iota = jnp.arange(slot_total, dtype=jnp.int32)
    hits = slot_ids[None, :, :] == slot_iota[:, None, None]
    gather_matrix = jnp.any(hits, axis=2).astype(jnp.bfloat16)
    dispatch = jnp.dot(gather_matrix, normed_moe, preferred_element_type=jnp.float32).astype(
        jnp.bfloat16
    )
    dispatch = dispatch.reshape(req_count, exp_dev, capacity, MODEL_WIDTH)
    gate_up = jnp.einsum(
        "nekd,edf->nekf",
        lax.all_to_all(dispatch, "req", split_axis=0, concat_axis=0, tiled=True),
        w_gate_up,
        preferred_element_type=jnp.float32,
    )
    hidden = (jax.nn.relu(gate_up[..., :FE]) * gate_up[..., FE:]).astype(jnp.bfloat16)
    result = jnp.einsum(
        "nekf,efd->nekd", hidden, w_down, preferred_element_type=jnp.float32
    ).astype(jnp.bfloat16)
    results = lax.all_to_all(result, "req", split_axis=0, concat_axis=0, tiled=True)
    flat_results = results.reshape(slot_total, MODEL_WIDTH)

    token_hits = slot_ids[:, :, None] == slot_iota[None, None, :]
    combine = jnp.sum(jnp.where(token_hits, route_gates[:, :, None], 0.0), axis=1)
    combine_hi = combine.astype(jnp.bfloat16)
    combine_lo = (combine - combine_hi.astype(jnp.float32)).astype(jnp.bfloat16)
    expert_sum = jnp.dot(combine_hi, flat_results, preferred_element_type=jnp.float32) + jnp.dot(
        combine_lo, flat_results, preferred_element_type=jnp.float32
    )
    mixed_out = (residual + expert_sum).astype(jnp.bfloat16)
    return (mixed_out, appended)


def solution(mesh):
    return jax.shard_map(
        on_device,
        mesh=mesh,
        in_specs=(
            P(("req", "head"), None),
            P(),
            P(),
            P(),
            P(),
            P(),
            P("req", None, None),
            P("req", None, None),
            P(("req", "head"), None),
            P("req", None, None),
            P("req", None, None),
            P("req", None),
            P(),
            P(),
        ),
        out_specs=(P(("req", "head"), None), P(("req", "head"), None)),
        check_vma=False,
    )
```

```python
import functools

import jax
import jax.numpy as jnp
from jax import lax
from jax.experimental import pallas as pl
from jax.experimental.pallas import tpu as pltpu
from jax.sharding import PartitionSpec as P

MODEL_WIDTH = 1536
QUERY_HEADS = 12
KEY_VALUE_HEADS = 2
HEAD_SIZE = 128
FE = 768
TOPK = 4
REQUEST_TOKENS = 512
PAGE_CHUNK = 128
STACK = 6


EPS = 1e-06
THETA = 1000000.0


def rms_scale(values, gain_vector):
    mean_sq = jnp.mean(values * values, axis=-1, keepdims=True)
    return values * lax.rsqrt(mean_sq + EPS) * gain_vector


def apply_rotary(values, where_at):
    half_dim = values.shape[-1] // 2
    frequency = jnp.exp(
        -jnp.log(jnp.float32(THETA))
        * jnp.arange(half_dim, dtype=jnp.float32)
        * 2.0
        / values.shape[-1]
    )
    angles = where_at.astype(jnp.float32)[:, None] * frequency[None, :]
    cosine = jnp.cos(angles)[:, None, :]
    sines = jnp.sin(angles)[:, None, :]
    first_half = values[..., :half_dim]
    second = values[..., half_dim:]
    return jnp.concatenate(
        [first_half * cosine - second * sines, second * cosine + first_half * sines], axis=-1
    )


def attention_kernel(
    meta_ref, q_ref, kn_ref, vn_ref, k_ref, v_ref, o_ref, m_sc, l_sc, acc_sc, *, group, tokens
):
    count = meta_ref[0]
    half = meta_ref[1]
    scaling = HEAD_SIZE ** (-0.5)
    contract = (((1,), (1,)), ((), ()))
    lanes = HEAD_SIZE

    def absorb(qg, k, v):
        s = lax.dot_general(qg, k, contract, preferred_element_type=jnp.float32) * scaling
        m_prev = m_sc[...]
        m_next = jnp.maximum(m_prev, jnp.max(s, axis=1, keepdims=True))
        repeat = s.shape[1] // lanes
        wide = m_next if repeat == 1 else jnp.concatenate([m_next] * repeat, axis=1)
        p = jnp.exp(s - wide)
        alpha = jnp.exp(m_prev - m_next)
        l_sc[...] = alpha * l_sc[...] + jnp.sum(p, axis=1, keepdims=True)
        acc_sc[...] = acc_sc[...] * alpha + jnp.dot(
            p.astype(jnp.bfloat16), v, preferred_element_type=jnp.float32
        )
        m_sc[...] = m_next

    for b in range(group // STACK):
        qg = jnp.concatenate(
            [q_ref[:, g * HEAD_SIZE : (g + 1) * HEAD_SIZE] for g in range(b * STACK, (b + 1) * STACK)],
            axis=0,
        )
        s = lax.dot_general(qg, kn_ref[...], contract, preferred_element_type=jnp.float32)
        s = s * scaling
        t = lax.broadcasted_iota(jnp.int32, s.shape, 0) % tokens
        key_pos = lax.broadcasted_iota(jnp.int32, s.shape, 1)
        s = jnp.where(key_pos <= t + half * tokens, s, -jnp.inf)
        m = jnp.max(s, axis=1, keepdims=True)
        p = jnp.exp(s - m)
        l_sc[...] = jnp.broadcast_to(jnp.sum(p, axis=1, keepdims=True), l_sc.shape)
        m_sc[...] = jnp.broadcast_to(m, m_sc.shape)
        acc_sc[...] = jnp.dot(
            p.astype(jnp.bfloat16), vn_ref[...], preferred_element_type=jnp.float32
        )

        def visit(i, carry):
            first = pl.multiple_of(i * (2 * PAGE_CHUNK), 2 * PAGE_CHUNK)
            absorb(qg, k_ref[pl.ds(first, 2 * PAGE_CHUNK), :], v_ref[pl.ds(first, 2 * PAGE_CHUNK), :])
            return carry

        lax.fori_loop(0, count // 2, visit, 0)

        @pl.when(count % 2 == 1)
        def _():
            first = pl.multiple_of((count - 1) * PAGE_CHUNK, PAGE_CHUNK)
            absorb(qg, k_ref[pl.ds(first, PAGE_CHUNK), :], v_ref[pl.ds(first, PAGE_CHUNK), :])

        res = (acc_sc[...] / l_sc[...]).astype(jnp.bfloat16)
        for i in range(STACK):
            g = b * STACK + i
            o_ref[:, g * HEAD_SIZE : (g + 1) * HEAD_SIZE] = res[i * tokens : (i + 1) * tokens]


def attend(meta, queries, new_keys, new_values, cache_keys, cache_values):
    tokens = queries.shape[0]
    group = QUERY_HEADS // KEY_VALUE_HEADS
    width = group * HEAD_SIZE
    span = new_keys.shape[0]
    cache_rows = cache_keys.shape[0]
    grid_spec = pltpu.PrefetchScalarGridSpec(
        num_scalar_prefetch=1,
        grid=(KEY_VALUE_HEADS,),
        in_specs=[
            pl.BlockSpec((tokens, width), lambda c, m: (0, c)),
            pl.BlockSpec((span, HEAD_SIZE), lambda c, m: (0, c)),
            pl.BlockSpec((span, HEAD_SIZE), lambda c, m: (0, c)),
            pl.BlockSpec((cache_rows, HEAD_SIZE), lambda c, m: (0, c)),
            pl.BlockSpec((cache_rows, HEAD_SIZE), lambda c, m: (0, c)),
        ],
        out_specs=pl.BlockSpec((tokens, width), lambda c, m: (0, c)),
        scratch_shapes=[
            pltpu.VMEM((STACK * tokens, HEAD_SIZE), jnp.float32),
            pltpu.VMEM((STACK * tokens, HEAD_SIZE), jnp.float32),
            pltpu.VMEM((STACK * tokens, HEAD_SIZE), jnp.float32),
        ],
    )
    return pl.pallas_call(
        functools.partial(attention_kernel, group=group, tokens=tokens),
        grid_spec=grid_spec,
        out_shape=jax.ShapeDtypeStruct((tokens, QUERY_HEADS * HEAD_SIZE), jnp.bfloat16),
        compiler_params=pltpu.CompilerParams(dimension_semantics=("arbitrary",)),
    )(meta, queries, new_keys, new_values, cache_keys, cache_values)


def on_device(
    tokens,
    norm1_gain,
    query_key_value_weight,
    w_out,
    norm2_gain,
    router_weight,
    w_gate_up,
    w_down,
    routes,
    key_page_store,
    value_page_store,
    page_table,
    cached_pages,
    anchor,
):
    req_index = lax.axis_index("req")
    head_index = lax.axis_index("head")
    count_of_heads = lax.axis_size("head")
    req_count = lax.axis_size("req")
    tokens_per_device = tokens.shape[0]
    req_dev = page_table.shape[0]
    page_size = key_page_store.shape[1]
    share = REQUEST_TOKENS // tokens_per_device
    kv_width = KEY_VALUE_HEADS * HEAD_SIZE

    request = (req_index * count_of_heads + head_index) // share
    half = head_index % share
    slot = request % req_dev
    old_id = anchor[request]
    place = half * tokens_per_device + jnp.arange(tokens_per_device, dtype=jnp.int32)
    token_positions = cached_pages[old_id] * page_size + place

    normed = rms_scale(tokens.astype(jnp.float32), norm1_gain).astype(jnp.bfloat16)
    projected_rows = jnp.dot(normed, query_key_value_weight, preferred_element_type=jnp.float32)
    queries = apply_rotary(
        projected_rows[:, : QUERY_HEADS * HEAD_SIZE].reshape(
            tokens_per_device, QUERY_HEADS, HEAD_SIZE
        ),
        token_positions,
    ).astype(jnp.bfloat16)
    fresh_keys = apply_rotary(
        projected_rows[
            :, QUERY_HEADS * HEAD_SIZE : (QUERY_HEADS + KEY_VALUE_HEADS) * HEAD_SIZE
        ].reshape(tokens_per_device, KEY_VALUE_HEADS, HEAD_SIZE),
        token_positions,
    ).astype(jnp.bfloat16)
    fresh_values = projected_rows[:, (QUERY_HEADS + KEY_VALUE_HEADS) * HEAD_SIZE :].astype(
        jnp.bfloat16
    )
    appended = jnp.concatenate(
        [fresh_keys.reshape(tokens_per_device, kv_width), fresh_values], axis=1
    )

    forward_pairs = [
        (h, h + 1) for h in range(count_of_heads) if h % share != share - 1
    ]
    earlier = lax.ppermute(appended, "head", forward_pairs)
    is_second = half == 1
    span_rows = jnp.where(
        is_second,
        jnp.concatenate([earlier, appended], axis=0),
        jnp.concatenate([appended, earlier], axis=0),
    )
    new_keys = span_rows[:, :kv_width]
    new_values = span_rows[:, kv_width:]

    partner = req_index ^ 1
    partner_anchor = lax.dynamic_slice_in_dim(anchor, partner * req_dev, req_dev, 0)
    leaving = partner_anchor // req_dev == req_index
    out_row = jnp.sum(jnp.where(leaving, partner_anchor, 0)) % req_dev
    sent_pages = page_table[out_row]
    sent = (
        jnp.take(key_page_store, sent_pages, axis=0),
        jnp.take(value_page_store, sent_pages, axis=0),
    )
    pairs = [(source, source ^ 1) for source in range(req_count)]
    k_got, v_got = lax.ppermute(sent, "req", pairs)

    moved_in = old_id // req_dev != req_index
    page_ids = page_table[old_id % req_dev]
    cache_rows = page_ids.shape[0] * page_size
    cache_keys = jnp.where(moved_in, k_got, jnp.take(key_page_store, page_ids, axis=0))
    cache_values = jnp.where(moved_in, v_got, jnp.take(value_page_store, page_ids, axis=0))
    meta = jnp.stack([cached_pages[old_id], half.astype(jnp.int32)]).astype(jnp.int32)
    attention = attend(
        meta, queries.reshape(tokens_per_device, QUERY_HEADS * HEAD_SIZE),
        new_keys, new_values,
        cache_keys.reshape(cache_rows, kv_width), cache_values.reshape(cache_rows, kv_width),
    )
    del slot

    residual = tokens.astype(jnp.float32) + jnp.dot(
        attention, w_out, preferred_element_type=jnp.float32
    )
    normed_moe = rms_scale(residual, norm2_gain).astype(jnp.bfloat16)
    logits = jnp.dot(normed_moe.astype(jnp.float32), router_weight, precision=lax.Precision.HIGHEST)
    route_match = routes[:, :, None] == jnp.arange(logits.shape[1], dtype=jnp.int32)[None, None, :]
    chosen = jnp.sum(jnp.where(route_match, logits[:, None, :], 0.0), axis=2)
    sigmoids = jax.nn.sigmoid(chosen)
    route_gates = sigmoids / jnp.sum(sigmoids, axis=1, keepdims=True)

    exp_dev = w_gate_up.shape[0]
    expert_total = exp_dev * req_count
    capacity = max(2, 3 * tokens_per_device * TOPK // (2 * expert_total))
    slot_total = expert_total * capacity
    flat_ids = routes.reshape(-1)
    route_rows = flat_ids.shape[0]
    one_hot = (flat_ids[:, None] == jnp.arange(expert_total, dtype=jnp.int32)[None, :]).astype(
        jnp.bfloat16
    )
    row_i = lax.broadcasted_iota(jnp.int32, (route_rows, route_rows), 0)
    col_i = lax.broadcasted_iota(jnp.int32, (route_rows, route_rows), 1)
    before = (col_i < row_i).astype(jnp.bfloat16)
    earlier_counts = jnp.dot(before, one_hot, preferred_element_type=jnp.float32)
    slot_ranks = jnp.sum(earlier_counts * one_hot.astype(jnp.float32), axis=1).astype(jnp.int32)
    slot_ids = (flat_ids * capacity + slot_ranks).reshape(tokens_per_device, TOPK)

    slot_iota = jnp.arange(slot_total, dtype=jnp.int32)
    hits = slot_ids[None, :, :] == slot_iota[:, None, None]
    gather_matrix = jnp.any(hits, axis=2).astype(jnp.bfloat16)
    dispatch = jnp.dot(gather_matrix, normed_moe, preferred_element_type=jnp.float32).astype(
        jnp.bfloat16
    )
    dispatch = dispatch.reshape(req_count, exp_dev, capacity, MODEL_WIDTH)
    gate_up = jnp.einsum(
        "nekd,edf->nekf",
        lax.all_to_all(dispatch, "req", split_axis=0, concat_axis=0, tiled=True),
        w_gate_up,
        preferred_element_type=jnp.float32,
    )
    hidden = (jax.nn.relu(gate_up[..., :FE]) * gate_up[..., FE:]).astype(jnp.bfloat16)
    result = jnp.einsum(
        "nekf,efd->nekd", hidden, w_down, preferred_element_type=jnp.float32
    ).astype(jnp.bfloat16)
    results = lax.all_to_all(result, "req", split_axis=0, concat_axis=0, tiled=True)
    flat_results = results.reshape(slot_total, MODEL_WIDTH)

    token_hits = slot_ids[:, :, None] == slot_iota[None, None, :]
    combine = jnp.sum(jnp.where(token_hits, route_gates[:, :, None], 0.0), axis=1)
    combine_hi = combine.astype(jnp.bfloat16)
    combine_lo = (combine - combine_hi.astype(jnp.float32)).astype(jnp.bfloat16)
    expert_sum = jnp.dot(combine_hi, flat_results, preferred_element_type=jnp.float32) + jnp.dot(
        combine_lo, flat_results, preferred_element_type=jnp.float32
    )
    mixed_out = (residual + expert_sum).astype(jnp.bfloat16)
    return (mixed_out, appended)


def solution(mesh):
    return jax.shard_map(
        on_device,
        mesh=mesh,
        in_specs=(
            P(("req", "head"), None),
            P(),
            P(),
            P(),
            P(),
            P(),
            P("req", None, None),
            P("req", None, None),
            P(("req", "head"), None),
            P("req", None, None),
            P("req", None, None),
            P("req", None),
            P(),
            P(),
        ),
        out_specs=(P(("req", "head"), None), P(("req", "head"), None)),
        check_vma=False,
    )
```

```python
import functools

import jax
import jax.numpy as jnp
from jax import lax
from jax.experimental import pallas as pl
from jax.experimental.pallas import tpu as pltpu
from jax.sharding import PartitionSpec as P

MODEL_WIDTH = 1536
QUERY_HEADS = 12
KEY_VALUE_HEADS = 2
HEAD_SIZE = 128
FE = 768
TOPK = 4
REQUEST_TOKENS = 512
PAGE_CHUNK = 128


EPS = 1e-06
THETA = 1000000.0


def rms_scale(values, gain_vector):
    mean_sq = jnp.mean(values * values, axis=-1, keepdims=True)
    return values * lax.rsqrt(mean_sq + EPS) * gain_vector


def apply_rotary(values, where_at):
    half_dim = values.shape[-1] // 2
    frequency = jnp.exp(
        -jnp.log(jnp.float32(THETA))
        * jnp.arange(half_dim, dtype=jnp.float32)
        * 2.0
        / values.shape[-1]
    )
    angles = where_at.astype(jnp.float32)[:, None] * frequency[None, :]
    cosine = jnp.cos(angles)[:, None, :]
    sines = jnp.sin(angles)[:, None, :]
    first_half = values[..., :half_dim]
    second = values[..., half_dim:]
    return jnp.concatenate(
        [first_half * cosine - second * sines, second * cosine + first_half * sines], axis=-1
    )


def attention_kernel(
    meta_ref, page_ref, q_ref, kn_ref, vn_ref, k_own, v_own, k_got, v_got,
    o_ref, k_buf, v_buf, sems, m_sc, l_sc, acc_sc, *, group, tokens
):
    count = meta_ref[0]
    half = meta_ref[1]
    moved = meta_ref[2]
    scaling = HEAD_SIZE ** (-0.5)
    contract = (((1,), (1,)), ((), ()))
    lanes = HEAD_SIZE

    def page_copies(c, j, k_pool, v_pool):
        page = page_ref[j]
        rows = pl.ds(pl.multiple_of(j * PAGE_CHUNK, PAGE_CHUNK), PAGE_CHUNK)
        cols = pl.ds(c * HEAD_SIZE, HEAD_SIZE)
        return (
            pltpu.make_async_copy(k_pool.at[page, :, cols], k_buf.at[c, rows, :], sems.at[0, c, j]),
            pltpu.make_async_copy(v_pool.at[page, :, cols], v_buf.at[c, rows, :], sems.at[1, c, j]),
        )

    def start_all(k_pool, v_pool):
        for c in range(KEY_VALUE_HEADS):
            def body(j, carry):
                for copy in page_copies(c, j, k_pool, v_pool):
                    copy.start()
                return carry
            lax.fori_loop(0, count, body, 0)

    @pl.when(moved == 1)
    def _():
        start_all(k_got, v_got)

    @pl.when(moved == 0)
    def _():
        start_all(k_own, v_own)

    def absorb(qg, k, v):
        s = lax.dot_general(qg, k, contract, preferred_element_type=jnp.float32) * scaling
        m_prev = m_sc[...]
        m_next = jnp.maximum(m_prev, jnp.max(s, axis=1, keepdims=True))
        repeat = s.shape[1] // lanes
        wide = m_next if repeat == 1 else jnp.concatenate([m_next] * repeat, axis=1)
        p = jnp.exp(s - wide)
        alpha = jnp.exp(m_prev - m_next)
        l_sc[...] = alpha * l_sc[...] + jnp.sum(p, axis=1, keepdims=True)
        acc_sc[...] = acc_sc[...] * alpha + jnp.dot(
            p.astype(jnp.bfloat16), v, preferred_element_type=jnp.float32
        )
        m_sc[...] = m_next

    for c in range(KEY_VALUE_HEADS):
        heads = range(c * group, (c + 1) * group)
        qg = jnp.concatenate(
            [q_ref[:, g * HEAD_SIZE : (g + 1) * HEAD_SIZE] for g in heads], axis=0
        )
        kn = kn_ref[:, c * HEAD_SIZE : (c + 1) * HEAD_SIZE]
        vn = vn_ref[:, c * HEAD_SIZE : (c + 1) * HEAD_SIZE]
        s = lax.dot_general(qg, kn, contract, preferred_element_type=jnp.float32)
        s = s * scaling
        t = lax.broadcasted_iota(jnp.int32, s.shape, 0) % tokens
        key_pos = lax.broadcasted_iota(jnp.int32, s.shape, 1)
        s = jnp.where(key_pos <= t + half * tokens, s, -jnp.inf)
        m = jnp.max(s, axis=1, keepdims=True)
        p = jnp.exp(s - m)
        l_sc[...] = jnp.broadcast_to(jnp.sum(p, axis=1, keepdims=True), l_sc.shape)
        m_sc[...] = jnp.broadcast_to(m, m_sc.shape)
        acc_sc[...] = jnp.dot(p.astype(jnp.bfloat16), vn, preferred_element_type=jnp.float32)

        def wait_page(j, carry):
            for copy in page_copies(c, j, k_own, v_own):
                copy.wait()
            return carry

        lax.fori_loop(0, count, wait_page, 0)

        def visit(i, carry):
            first = pl.multiple_of(i * (2 * PAGE_CHUNK), 2 * PAGE_CHUNK)
            absorb(
                qg,
                k_buf[c, pl.ds(first, 2 * PAGE_CHUNK), :],
                v_buf[c, pl.ds(first, 2 * PAGE_CHUNK), :],
            )
            return carry

        lax.fori_loop(0, count // 2, visit, 0)

        @pl.when(count % 2 == 1)
        def _():
            first = pl.multiple_of((count - 1) * PAGE_CHUNK, PAGE_CHUNK)
            absorb(
                qg,
                k_buf[c, pl.ds(first, PAGE_CHUNK), :],
                v_buf[c, pl.ds(first, PAGE_CHUNK), :],
            )

        res = (acc_sc[...] / l_sc[...]).astype(jnp.bfloat16)
        for i, g in enumerate(heads):
            o_ref[:, g * HEAD_SIZE : (g + 1) * HEAD_SIZE] = res[i * tokens : (i + 1) * tokens]


def attend(meta, page_ids, queries, new_keys, new_values, k_own, v_own, k_got, v_got):
    tokens = queries.shape[0]
    group = QUERY_HEADS // KEY_VALUE_HEADS
    max_pages = page_ids.shape[0]
    cache_rows = max_pages * PAGE_CHUNK
    smem = pltpu.MemorySpace.SMEM if hasattr(pltpu, "MemorySpace") else pltpu.SMEM
    vmem_spec = pl.BlockSpec(memory_space=pltpu.VMEM)
    any_spec = pl.BlockSpec(memory_space=pl.ANY)
    return pl.pallas_call(
        functools.partial(attention_kernel, group=group, tokens=tokens),
        in_specs=[
            pl.BlockSpec(memory_space=smem),
            pl.BlockSpec(memory_space=smem),
            vmem_spec,
            vmem_spec,
            vmem_spec,
            any_spec,
            any_spec,
            any_spec,
            any_spec,
        ],
        out_specs=vmem_spec,
        out_shape=jax.ShapeDtypeStruct((tokens, QUERY_HEADS * HEAD_SIZE), jnp.bfloat16),
        scratch_shapes=[
            pltpu.VMEM((KEY_VALUE_HEADS, cache_rows, HEAD_SIZE), jnp.bfloat16),
            pltpu.VMEM((KEY_VALUE_HEADS, cache_rows, HEAD_SIZE), jnp.bfloat16),
            pltpu.SemaphoreType.DMA((2, KEY_VALUE_HEADS, max_pages)),
            pltpu.VMEM((group * tokens, HEAD_SIZE), jnp.float32),
            pltpu.VMEM((group * tokens, HEAD_SIZE), jnp.float32),
            pltpu.VMEM((group * tokens, HEAD_SIZE), jnp.float32),
        ],
    )(meta, page_ids, queries, new_keys, new_values, k_own, v_own, k_got, v_got)


def on_device(
    tokens,
    norm1_gain,
    query_key_value_weight,
    w_out,
    norm2_gain,
    router_weight,
    w_gate_up,
    w_down,
    routes,
    key_page_store,
    value_page_store,
    page_table,
    cached_pages,
    anchor,
):
    req_index = lax.axis_index("req")
    head_index = lax.axis_index("head")
    count_of_heads = lax.axis_size("head")
    req_count = lax.axis_size("req")
    tokens_per_device = tokens.shape[0]
    req_dev = page_table.shape[0]
    page_size = key_page_store.shape[1]
    share = REQUEST_TOKENS // tokens_per_device
    kv_width = KEY_VALUE_HEADS * HEAD_SIZE

    request = (req_index * count_of_heads + head_index) // share
    half = head_index % share
    old_id = anchor[request]
    place = half * tokens_per_device + jnp.arange(tokens_per_device, dtype=jnp.int32)
    token_positions = cached_pages[old_id] * page_size + place

    normed = rms_scale(tokens.astype(jnp.float32), norm1_gain).astype(jnp.bfloat16)
    projected_rows = jnp.dot(normed, query_key_value_weight, preferred_element_type=jnp.float32)
    queries = apply_rotary(
        projected_rows[:, : QUERY_HEADS * HEAD_SIZE].reshape(
            tokens_per_device, QUERY_HEADS, HEAD_SIZE
        ),
        token_positions,
    ).astype(jnp.bfloat16)
    fresh_keys = apply_rotary(
        projected_rows[
            :, QUERY_HEADS * HEAD_SIZE : (QUERY_HEADS + KEY_VALUE_HEADS) * HEAD_SIZE
        ].reshape(tokens_per_device, KEY_VALUE_HEADS, HEAD_SIZE),
        token_positions,
    ).astype(jnp.bfloat16)
    fresh_values = projected_rows[:, (QUERY_HEADS + KEY_VALUE_HEADS) * HEAD_SIZE :].astype(
        jnp.bfloat16
    )
    appended = jnp.concatenate(
        [fresh_keys.reshape(tokens_per_device, kv_width), fresh_values], axis=1
    )

    forward_pairs = [
        (h, h + 1) for h in range(count_of_heads) if h % share != share - 1
    ]
    earlier = lax.ppermute(appended, "head", forward_pairs)
    is_second = half == 1
    span_rows = jnp.where(
        is_second,
        jnp.concatenate([earlier, appended], axis=0),
        jnp.concatenate([appended, earlier], axis=0),
    )
    new_keys = span_rows[:, :kv_width]
    new_values = span_rows[:, kv_width:]

    pairs = [(source, source ^ 1) for source in range(req_count)]
    k_got, v_got, table_got = lax.ppermute(
        (key_page_store, value_page_store, page_table), "req", pairs
    )
    moved_in = old_id // req_dev != req_index
    page_ids = jnp.where(moved_in, table_got[old_id % req_dev], page_table[old_id % req_dev])
    meta = jnp.stack(
        [cached_pages[old_id], half.astype(jnp.int32), moved_in.astype(jnp.int32)]
    ).astype(jnp.int32)
    attention = attend(
        meta, page_ids, queries.reshape(tokens_per_device, QUERY_HEADS * HEAD_SIZE),
        new_keys, new_values, key_page_store, value_page_store, k_got, v_got,
    )

    residual = tokens.astype(jnp.float32) + jnp.dot(
        attention, w_out, preferred_element_type=jnp.float32
    )
    normed_moe = rms_scale(residual, norm2_gain).astype(jnp.bfloat16)
    logits = jnp.dot(normed_moe.astype(jnp.float32), router_weight, precision=lax.Precision.HIGHEST)
    route_match = routes[:, :, None] == jnp.arange(logits.shape[1], dtype=jnp.int32)[None, None, :]
    chosen = jnp.sum(jnp.where(route_match, logits[:, None, :], 0.0), axis=2)
    sigmoids = jax.nn.sigmoid(chosen)
    route_gates = sigmoids / jnp.sum(sigmoids, axis=1, keepdims=True)

    exp_dev = w_gate_up.shape[0]
    expert_total = exp_dev * req_count
    capacity = max(2, 3 * tokens_per_device * TOPK // (2 * expert_total))
    slot_total = expert_total * capacity
    flat_ids = routes.reshape(-1)
    route_rows = flat_ids.shape[0]
    one_hot = (flat_ids[:, None] == jnp.arange(expert_total, dtype=jnp.int32)[None, :]).astype(
        jnp.bfloat16
    )
    row_i = lax.broadcasted_iota(jnp.int32, (route_rows, route_rows), 0)
    col_i = lax.broadcasted_iota(jnp.int32, (route_rows, route_rows), 1)
    before = (col_i < row_i).astype(jnp.bfloat16)
    earlier_counts = jnp.dot(before, one_hot, preferred_element_type=jnp.float32)
    slot_ranks = jnp.sum(earlier_counts * one_hot.astype(jnp.float32), axis=1).astype(jnp.int32)
    slot_ids = (flat_ids * capacity + slot_ranks).reshape(tokens_per_device, TOPK)

    slot_iota = jnp.arange(slot_total, dtype=jnp.int32)
    hits = slot_ids[None, :, :] == slot_iota[:, None, None]
    gather_matrix = jnp.any(hits, axis=2).astype(jnp.bfloat16)
    dispatch = jnp.dot(gather_matrix, normed_moe, preferred_element_type=jnp.float32).astype(
        jnp.bfloat16
    )
    dispatch = dispatch.reshape(req_count, exp_dev, capacity, MODEL_WIDTH)
    gate_up = jnp.einsum(
        "nekd,edf->nekf",
        lax.all_to_all(dispatch, "req", split_axis=0, concat_axis=0, tiled=True),
        w_gate_up,
        preferred_element_type=jnp.float32,
    )
    hidden = (jax.nn.relu(gate_up[..., :FE]) * gate_up[..., FE:]).astype(jnp.bfloat16)
    result = jnp.einsum(
        "nekf,efd->nekd", hidden, w_down, preferred_element_type=jnp.float32
    ).astype(jnp.bfloat16)
    results = lax.all_to_all(result, "req", split_axis=0, concat_axis=0, tiled=True)
    flat_results = results.reshape(slot_total, MODEL_WIDTH)

    token_hits = slot_ids[:, :, None] == slot_iota[None, None, :]
    combine = jnp.sum(jnp.where(token_hits, route_gates[:, :, None], 0.0), axis=1)
    combine_hi = combine.astype(jnp.bfloat16)
    combine_lo = (combine - combine_hi.astype(jnp.float32)).astype(jnp.bfloat16)
    expert_sum = jnp.dot(combine_hi, flat_results, preferred_element_type=jnp.float32) + jnp.dot(
        combine_lo, flat_results, preferred_element_type=jnp.float32
    )
    mixed_out = (residual + expert_sum).astype(jnp.bfloat16)
    return (mixed_out, appended)


def solution(mesh):
    return jax.shard_map(
        on_device,
        mesh=mesh,
        in_specs=(
            P(("req", "head"), None),
            P(),
            P(),
            P(),
            P(),
            P(),
            P("req", None, None),
            P("req", None, None),
            P(("req", "head"), None),
            P("req", None, None),
            P("req", None, None),
            P("req", None),
            P(),
            P(),
        ),
        out_specs=(P(("req", "head"), None), P(("req", "head"), None)),
        check_vma=False,
    )
```

```python
import functools

import jax
import jax.numpy as jnp
from jax import lax
from jax.experimental import pallas as pl
from jax.experimental.pallas import tpu as pltpu
from jax.sharding import PartitionSpec as P

MODEL_WIDTH = 1536
QUERY_HEADS = 12
KEY_VALUE_HEADS = 2
HEAD_SIZE = 128
FE = 768
TOPK = 4
REQUEST_TOKENS = 512
PAGE_CHUNK = 128


EPS = 1e-06
THETA = 1000000.0


def rms_scale(values, gain_vector):
    mean_sq = jnp.mean(values * values, axis=-1, keepdims=True)
    return values * lax.rsqrt(mean_sq + EPS) * gain_vector


def apply_rotary(values, where_at):
    half_dim = values.shape[-1] // 2
    frequency = jnp.exp(
        -jnp.log(jnp.float32(THETA))
        * jnp.arange(half_dim, dtype=jnp.float32)
        * 2.0
        / values.shape[-1]
    )
    angles = where_at.astype(jnp.float32)[:, None] * frequency[None, :]
    cosine = jnp.cos(angles)[:, None, :]
    sines = jnp.sin(angles)[:, None, :]
    first_half = values[..., :half_dim]
    second = values[..., half_dim:]
    return jnp.concatenate(
        [first_half * cosine - second * sines, second * cosine + first_half * sines], axis=-1
    )


def rotate_flat(values, cosine, sines):
    half_dim = cosine.shape[1]
    heads = values.shape[1] // (2 * half_dim)
    cos_full = jnp.tile(jnp.concatenate([cosine, cosine], axis=1), (1, heads))
    sin_signed = jnp.tile(jnp.concatenate([-sines, sines], axis=1), (1, heads))
    parts = []
    for h in range(heads):
        base = 2 * half_dim * h
        parts += [values[:, base + half_dim : base + 2 * half_dim], values[:, base : base + half_dim]]
    return values * cos_full + jnp.concatenate(parts, axis=1) * sin_signed


def attention_kernel(
    meta_ref, page_ref, q_ref, kn_ref, vn_ref, k_own, v_own, k_got, v_got,
    o_ref, k_buf, v_buf, sems, m_sc, l_sc, acc_sc, *, group, tokens
):
    count = meta_ref[0]
    half = meta_ref[1]
    moved = meta_ref[2]
    scaling = HEAD_SIZE ** (-0.5)
    contract = (((1,), (1,)), ((), ()))
    lanes = HEAD_SIZE

    def page_copies(c, j, k_pool, v_pool):
        page = page_ref[j]
        rows = pl.ds(pl.multiple_of(j * PAGE_CHUNK, PAGE_CHUNK), PAGE_CHUNK)
        cols = pl.ds(c * HEAD_SIZE, HEAD_SIZE)
        return (
            pltpu.make_async_copy(k_pool.at[page, :, cols], k_buf.at[c, rows, :], sems.at[0, c, j]),
            pltpu.make_async_copy(v_pool.at[page, :, cols], v_buf.at[c, rows, :], sems.at[1, c, j]),
        )

    def start_all(k_pool, v_pool):
        for c in range(KEY_VALUE_HEADS):
            def body(j, carry):
                for copy in page_copies(c, j, k_pool, v_pool):
                    copy.start()
                return carry
            lax.fori_loop(0, count, body, 0)

    @pl.when(moved == 1)
    def _():
        start_all(k_got, v_got)

    @pl.when(moved == 0)
    def _():
        start_all(k_own, v_own)

    def absorb(qg, k, v):
        s = lax.dot_general(qg, k, contract, preferred_element_type=jnp.float32) * scaling
        m_prev = m_sc[...]
        m_next = jnp.maximum(m_prev, jnp.max(s, axis=1, keepdims=True))
        repeat = s.shape[1] // lanes
        wide = m_next if repeat == 1 else jnp.concatenate([m_next] * repeat, axis=1)
        p = jnp.exp(s - wide)
        alpha = jnp.exp(m_prev - m_next)
        l_sc[...] = alpha * l_sc[...] + jnp.sum(p, axis=1, keepdims=True)
        acc_sc[...] = acc_sc[...] * alpha + jnp.dot(
            p.astype(jnp.bfloat16), v, preferred_element_type=jnp.float32
        )
        m_sc[...] = m_next

    for c in range(KEY_VALUE_HEADS):
        heads = range(c * group, (c + 1) * group)
        qg = jnp.concatenate(
            [q_ref[:, g * HEAD_SIZE : (g + 1) * HEAD_SIZE] for g in heads], axis=0
        )
        key_cols = slice(c * HEAD_SIZE, (c + 1) * HEAD_SIZE)
        value_cols = slice((KEY_VALUE_HEADS + c) * HEAD_SIZE, (KEY_VALUE_HEADS + c + 1) * HEAD_SIZE)
        s = lax.dot_general(qg, kn_ref[:, key_cols], contract, preferred_element_type=jnp.float32)
        s = s * scaling
        t = lax.broadcasted_iota(jnp.int32, s.shape, 0) % tokens
        key_pos = lax.broadcasted_iota(jnp.int32, s.shape, 1)
        s = jnp.where(key_pos <= t, s, -jnp.inf)
        m = jnp.max(s, axis=1, keepdims=True)
        p = jnp.exp(s - m)
        l_sc[...] = jnp.broadcast_to(jnp.sum(p, axis=1, keepdims=True), l_sc.shape)
        m_sc[...] = jnp.broadcast_to(m, m_sc.shape)
        acc_sc[...] = jnp.dot(
            p.astype(jnp.bfloat16), kn_ref[:, value_cols], preferred_element_type=jnp.float32
        )

        @pl.when(half == 1)
        def _():
            absorb(qg, vn_ref[:, key_cols], vn_ref[:, value_cols])

        def wait_page(j, carry):
            for copy in page_copies(c, j, k_own, v_own):
                copy.wait()
            return carry

        lax.fori_loop(0, count, wait_page, 0)

        def visit(i, carry):
            first = pl.multiple_of(i * (2 * PAGE_CHUNK), 2 * PAGE_CHUNK)
            absorb(
                qg,
                k_buf[c, pl.ds(first, 2 * PAGE_CHUNK), :],
                v_buf[c, pl.ds(first, 2 * PAGE_CHUNK), :],
            )
            return carry

        lax.fori_loop(0, count // 2, visit, 0)

        @pl.when(count % 2 == 1)
        def _():
            first = pl.multiple_of((count - 1) * PAGE_CHUNK, PAGE_CHUNK)
            absorb(
                qg,
                k_buf[c, pl.ds(first, PAGE_CHUNK), :],
                v_buf[c, pl.ds(first, PAGE_CHUNK), :],
            )

        res = (acc_sc[...] / l_sc[...]).astype(jnp.bfloat16)
        for i, g in enumerate(heads):
            o_ref[:, g * HEAD_SIZE : (g + 1) * HEAD_SIZE] = res[i * tokens : (i + 1) * tokens]


def attend(meta, page_ids, queries, new_keys, new_values, k_own, v_own, k_got, v_got):
    tokens = queries.shape[0]
    group = QUERY_HEADS // KEY_VALUE_HEADS
    max_pages = page_ids.shape[0]
    cache_rows = max_pages * PAGE_CHUNK
    smem = pltpu.MemorySpace.SMEM if hasattr(pltpu, "MemorySpace") else pltpu.SMEM
    vmem_spec = pl.BlockSpec(memory_space=pltpu.VMEM)
    any_spec = pl.BlockSpec(memory_space=pl.ANY)
    return pl.pallas_call(
        functools.partial(attention_kernel, group=group, tokens=tokens),
        in_specs=[
            pl.BlockSpec(memory_space=smem),
            pl.BlockSpec(memory_space=smem),
            vmem_spec,
            vmem_spec,
            vmem_spec,
            any_spec,
            any_spec,
            any_spec,
            any_spec,
        ],
        out_specs=vmem_spec,
        out_shape=jax.ShapeDtypeStruct((tokens, QUERY_HEADS * HEAD_SIZE), jnp.bfloat16),
        scratch_shapes=[
            pltpu.VMEM((KEY_VALUE_HEADS, cache_rows, HEAD_SIZE), jnp.bfloat16),
            pltpu.VMEM((KEY_VALUE_HEADS, cache_rows, HEAD_SIZE), jnp.bfloat16),
            pltpu.SemaphoreType.DMA((2, KEY_VALUE_HEADS, max_pages)),
            pltpu.VMEM((group * tokens, HEAD_SIZE), jnp.float32),
            pltpu.VMEM((group * tokens, HEAD_SIZE), jnp.float32),
            pltpu.VMEM((group * tokens, HEAD_SIZE), jnp.float32),
        ],
    )(meta, page_ids, queries, new_keys, new_values, k_own, v_own, k_got, v_got)


def on_device(
    tokens,
    norm1_gain,
    query_key_value_weight,
    w_out,
    norm2_gain,
    router_weight,
    w_gate_up,
    w_down,
    routes,
    key_page_store,
    value_page_store,
    page_table,
    cached_pages,
    anchor,
):
    req_index = lax.axis_index("req")
    head_index = lax.axis_index("head")
    count_of_heads = lax.axis_size("head")
    req_count = lax.axis_size("req")
    tokens_per_device = tokens.shape[0]
    req_dev = page_table.shape[0]
    page_size = key_page_store.shape[1]
    share = REQUEST_TOKENS // tokens_per_device
    kv_width = KEY_VALUE_HEADS * HEAD_SIZE

    request = (req_index * count_of_heads + head_index) // share
    half = head_index % share
    old_id = anchor[request]
    place = half * tokens_per_device + jnp.arange(tokens_per_device, dtype=jnp.int32)
    token_positions = cached_pages[old_id] * page_size + place

    normed = rms_scale(tokens.astype(jnp.float32), norm1_gain).astype(jnp.bfloat16)
    projected_rows = jnp.dot(normed, query_key_value_weight, preferred_element_type=jnp.float32)
    half_dim = HEAD_SIZE // 2
    frequency = jnp.exp(
        -jnp.log(jnp.float32(THETA))
        * jnp.arange(half_dim, dtype=jnp.float32)
        * 2.0
        / HEAD_SIZE
    )
    angles = token_positions.astype(jnp.float32)[:, None] * frequency[None, :]
    rotated = rotate_flat(
        projected_rows[:, : (QUERY_HEADS + KEY_VALUE_HEADS) * HEAD_SIZE],
        jnp.cos(angles),
        jnp.sin(angles),
    ).astype(jnp.bfloat16)
    queries = rotated[:, : QUERY_HEADS * HEAD_SIZE]
    fresh_values = projected_rows[:, (QUERY_HEADS + KEY_VALUE_HEADS) * HEAD_SIZE :].astype(
        jnp.bfloat16
    )
    appended = jnp.concatenate([rotated[:, QUERY_HEADS * HEAD_SIZE :], fresh_values], axis=1)

    forward_pairs = [
        (h, h + 1) for h in range(count_of_heads) if h % share != share - 1
    ]
    earlier = lax.ppermute(appended, "head", forward_pairs)
    pairs = [(source, source ^ 1) for source in range(req_count)]
    k_got, v_got, table_got = lax.ppermute(
        (key_page_store, value_page_store, page_table), "req", pairs
    )
    moved_in = old_id // req_dev != req_index
    page_ids = jnp.where(moved_in, table_got[old_id % req_dev], page_table[old_id % req_dev])
    meta = jnp.stack(
        [cached_pages[old_id], half.astype(jnp.int32), moved_in.astype(jnp.int32)]
    ).astype(jnp.int32)
    attention = attend(
        meta, page_ids, queries, appended, earlier, key_page_store, value_page_store, k_got, v_got,
    )

    residual = tokens.astype(jnp.float32) + jnp.dot(
        attention, w_out, preferred_element_type=jnp.float32
    )
    normed_moe = rms_scale(residual, norm2_gain).astype(jnp.bfloat16)
    logits = jnp.dot(normed_moe.astype(jnp.float32), router_weight, precision=lax.Precision.HIGHEST)
    route_match = routes[:, :, None] == jnp.arange(logits.shape[1], dtype=jnp.int32)[None, None, :]
    chosen = jnp.sum(jnp.where(route_match, logits[:, None, :], 0.0), axis=2)
    sigmoids = jax.nn.sigmoid(chosen)
    route_gates = sigmoids / jnp.sum(sigmoids, axis=1, keepdims=True)

    exp_dev = w_gate_up.shape[0]
    expert_total = exp_dev * req_count
    capacity = max(2, 3 * tokens_per_device * TOPK // (2 * expert_total))
    slot_total = expert_total * capacity
    flat_ids = routes.reshape(-1)
    route_rows = flat_ids.shape[0]
    one_hot = (flat_ids[:, None] == jnp.arange(expert_total, dtype=jnp.int32)[None, :]).astype(
        jnp.bfloat16
    )
    row_i = lax.broadcasted_iota(jnp.int32, (route_rows, route_rows), 0)
    col_i = lax.broadcasted_iota(jnp.int32, (route_rows, route_rows), 1)
    before = (col_i < row_i).astype(jnp.bfloat16)
    earlier_counts = jnp.dot(before, one_hot, preferred_element_type=jnp.float32)
    slot_ranks = jnp.sum(earlier_counts * one_hot.astype(jnp.float32), axis=1).astype(jnp.int32)
    slot_ids = (flat_ids * capacity + slot_ranks).reshape(tokens_per_device, TOPK)

    slot_iota = jnp.arange(slot_total, dtype=jnp.int32)
    hits = slot_ids[None, :, :] == slot_iota[:, None, None]
    gather_matrix = jnp.any(hits, axis=2).astype(jnp.bfloat16)
    dispatch = jnp.dot(gather_matrix, normed_moe, preferred_element_type=jnp.float32).astype(
        jnp.bfloat16
    )
    dispatch = dispatch.reshape(req_count, exp_dev, capacity, MODEL_WIDTH)
    gate_up = jnp.einsum(
        "nekd,edf->nekf",
        lax.all_to_all(dispatch, "req", split_axis=0, concat_axis=0, tiled=True),
        w_gate_up,
        preferred_element_type=jnp.float32,
    )
    hidden = (jax.nn.relu(gate_up[..., :FE]) * gate_up[..., FE:]).astype(jnp.bfloat16)
    result = jnp.einsum(
        "nekf,efd->nekd", hidden, w_down, preferred_element_type=jnp.float32
    ).astype(jnp.bfloat16)
    results = lax.all_to_all(result, "req", split_axis=0, concat_axis=0, tiled=True)
    flat_results = results.reshape(slot_total, MODEL_WIDTH)

    token_hits = slot_ids[:, :, None] == slot_iota[None, None, :]
    combine = jnp.sum(jnp.where(token_hits, route_gates[:, :, None], 0.0), axis=1)
    expert_sum = jnp.dot(
        combine.astype(jnp.bfloat16), flat_results, preferred_element_type=jnp.float32
    )
    mixed_out = (residual + expert_sum).astype(jnp.bfloat16)
    return (mixed_out, appended)


def solution(mesh):
    return jax.shard_map(
        on_device,
        mesh=mesh,
        in_specs=(
            P(("req", "head"), None),
            P(),
            P(),
            P(),
            P(),
            P(),
            P("req", None, None),
            P("req", None, None),
            P(("req", "head"), None),
            P("req", None, None),
            P("req", None, None),
            P("req", None),
            P(),
            P(),
        ),
        out_specs=(P(("req", "head"), None), P(("req", "head"), None)),
        check_vma=False,
    )
```

```python
import functools

import jax
import jax.numpy as jnp
from jax import lax
from jax.experimental import pallas as pl
from jax.experimental.pallas import tpu as pltpu
from jax.sharding import PartitionSpec as P

MODEL_WIDTH = 1536
QUERY_HEADS = 12
KEY_VALUE_HEADS = 2
HEAD_SIZE = 128
FE = 768
TOPK = 4
REQUEST_TOKENS = 512
PAGE_CHUNK = 128


EPS = 1e-06
THETA = 1000000.0


def rms_scale(values, gain_vector):
    mean_sq = jnp.mean(values * values, axis=-1, keepdims=True)
    return values * lax.rsqrt(mean_sq + EPS) * gain_vector


def apply_rotary(values, where_at):
    half_dim = values.shape[-1] // 2
    frequency = jnp.exp(
        -jnp.log(jnp.float32(THETA))
        * jnp.arange(half_dim, dtype=jnp.float32)
        * 2.0
        / values.shape[-1]
    )
    angles = where_at.astype(jnp.float32)[:, None] * frequency[None, :]
    cosine = jnp.cos(angles)[:, None, :]
    sines = jnp.sin(angles)[:, None, :]
    first_half = values[..., :half_dim]
    second = values[..., half_dim:]
    return jnp.concatenate(
        [first_half * cosine - second * sines, second * cosine + first_half * sines], axis=-1
    )


def rotary_kernel(proj_ref, cos_ref, sin_ref, q_ref, app_ref):
    cosine = cos_ref[...]
    sines = sin_ref[...]
    for h in range(QUERY_HEADS + KEY_VALUE_HEADS):
        x = proj_ref[:, h * HEAD_SIZE : (h + 1) * HEAD_SIZE]
        swapped = pltpu.roll(x, HEAD_SIZE // 2, 1)
        r = (x * cosine + swapped * sines).astype(jnp.bfloat16)
        if h < QUERY_HEADS:
            q_ref[:, h * HEAD_SIZE : (h + 1) * HEAD_SIZE] = r
        else:
            k = h - QUERY_HEADS
            app_ref[:, k * HEAD_SIZE : (k + 1) * HEAD_SIZE] = r
    base = (QUERY_HEADS + KEY_VALUE_HEADS) * HEAD_SIZE
    width = KEY_VALUE_HEADS * HEAD_SIZE
    app_ref[:, width : 2 * width] = proj_ref[:, base : base + width].astype(jnp.bfloat16)


def rotate(projected_rows, cosine, sines):
    tokens = projected_rows.shape[0]
    vmem_spec = pl.BlockSpec(memory_space=pltpu.VMEM)
    return pl.pallas_call(
        rotary_kernel,
        in_specs=[vmem_spec, vmem_spec, vmem_spec],
        out_specs=(vmem_spec, vmem_spec),
        out_shape=(
            jax.ShapeDtypeStruct((tokens, QUERY_HEADS * HEAD_SIZE), jnp.bfloat16),
            jax.ShapeDtypeStruct((tokens, 2 * KEY_VALUE_HEADS * HEAD_SIZE), jnp.bfloat16),
        ),
    )(projected_rows, cosine, sines)


def attention_kernel(
    meta_ref, page_ref, q_ref, kn_ref, vn_ref, k_own, v_own, k_got, v_got,
    o_ref, k_buf, v_buf, sems, m_sc, l_sc, acc_sc, *, group, tokens
):
    count = meta_ref[0]
    half = meta_ref[1]
    moved = meta_ref[2]
    scaling = HEAD_SIZE ** (-0.5)
    contract = (((1,), (1,)), ((), ()))
    lanes = HEAD_SIZE

    def page_copies(c, j, k_pool, v_pool):
        page = page_ref[j]
        rows = pl.ds(pl.multiple_of(j * PAGE_CHUNK, PAGE_CHUNK), PAGE_CHUNK)
        cols = pl.ds(c * HEAD_SIZE, HEAD_SIZE)
        return (
            pltpu.make_async_copy(k_pool.at[page, :, cols], k_buf.at[c, rows, :], sems.at[0, c, j]),
            pltpu.make_async_copy(v_pool.at[page, :, cols], v_buf.at[c, rows, :], sems.at[1, c, j]),
        )

    def start_all(k_pool, v_pool):
        for c in range(KEY_VALUE_HEADS):
            def body(j, carry):
                for copy in page_copies(c, j, k_pool, v_pool):
                    copy.start()
                return carry
            lax.fori_loop(0, count, body, 0)

    @pl.when(moved == 1)
    def _():
        start_all(k_got, v_got)

    @pl.when(moved == 0)
    def _():
        start_all(k_own, v_own)

    def absorb(qg, k, v):
        s = lax.dot_general(qg, k, contract, preferred_element_type=jnp.float32) * scaling
        m_prev = m_sc[...]
        m_next = jnp.maximum(m_prev, jnp.max(s, axis=1, keepdims=True))
        repeat = s.shape[1] // lanes
        wide = m_next if repeat == 1 else jnp.concatenate([m_next] * repeat, axis=1)
        p = jnp.exp(s - wide)
        alpha = jnp.exp(m_prev - m_next)
        l_sc[...] = alpha * l_sc[...] + jnp.sum(p, axis=1, keepdims=True)
        acc_sc[...] = acc_sc[...] * alpha + jnp.dot(
            p.astype(jnp.bfloat16), v, preferred_element_type=jnp.float32
        )
        m_sc[...] = m_next

    for c in range(KEY_VALUE_HEADS):
        heads = range(c * group, (c + 1) * group)
        qg = jnp.concatenate(
            [q_ref[:, g * HEAD_SIZE : (g + 1) * HEAD_SIZE] for g in heads], axis=0
        )
        key_cols = slice(c * HEAD_SIZE, (c + 1) * HEAD_SIZE)
        value_cols = slice((KEY_VALUE_HEADS + c) * HEAD_SIZE, (KEY_VALUE_HEADS + c + 1) * HEAD_SIZE)
        s = lax.dot_general(qg, kn_ref[:, key_cols], contract, preferred_element_type=jnp.float32)
        s = s * scaling
        t = lax.broadcasted_iota(jnp.int32, s.shape, 0) % tokens
        key_pos = lax.broadcasted_iota(jnp.int32, s.shape, 1)
        s = jnp.where(key_pos <= t, s, -jnp.inf)
        m = jnp.max(s, axis=1, keepdims=True)
        p = jnp.exp(s - m)
        l_sc[...] = jnp.broadcast_to(jnp.sum(p, axis=1, keepdims=True), l_sc.shape)
        m_sc[...] = jnp.broadcast_to(m, m_sc.shape)
        acc_sc[...] = jnp.dot(
            p.astype(jnp.bfloat16), kn_ref[:, value_cols], preferred_element_type=jnp.float32
        )

        @pl.when(half == 1)
        def _():
            absorb(qg, vn_ref[:, key_cols], vn_ref[:, value_cols])

        def wait_page(j, carry):
            for copy in page_copies(c, j, k_own, v_own):
                copy.wait()
            return carry

        lax.fori_loop(0, count, wait_page, 0)

        def visit(i, carry):
            first = pl.multiple_of(i * (2 * PAGE_CHUNK), 2 * PAGE_CHUNK)
            absorb(
                qg,
                k_buf[c, pl.ds(first, 2 * PAGE_CHUNK), :],
                v_buf[c, pl.ds(first, 2 * PAGE_CHUNK), :],
            )
            return carry

        lax.fori_loop(0, count // 2, visit, 0)

        @pl.when(count % 2 == 1)
        def _():
            first = pl.multiple_of((count - 1) * PAGE_CHUNK, PAGE_CHUNK)
            absorb(
                qg,
                k_buf[c, pl.ds(first, PAGE_CHUNK), :],
                v_buf[c, pl.ds(first, PAGE_CHUNK), :],
            )

        res = (acc_sc[...] / l_sc[...]).astype(jnp.bfloat16)
        for i, g in enumerate(heads):
            o_ref[:, g * HEAD_SIZE : (g + 1) * HEAD_SIZE] = res[i * tokens : (i + 1) * tokens]


def attend(meta, page_ids, queries, new_keys, new_values, k_own, v_own, k_got, v_got):
    tokens = queries.shape[0]
    group = QUERY_HEADS // KEY_VALUE_HEADS
    max_pages = page_ids.shape[0]
    cache_rows = max_pages * PAGE_CHUNK
    smem = pltpu.MemorySpace.SMEM if hasattr(pltpu, "MemorySpace") else pltpu.SMEM
    vmem_spec = pl.BlockSpec(memory_space=pltpu.VMEM)
    any_spec = pl.BlockSpec(memory_space=pl.ANY)
    return pl.pallas_call(
        functools.partial(attention_kernel, group=group, tokens=tokens),
        in_specs=[
            pl.BlockSpec(memory_space=smem),
            pl.BlockSpec(memory_space=smem),
            vmem_spec,
            vmem_spec,
            vmem_spec,
            any_spec,
            any_spec,
            any_spec,
            any_spec,
        ],
        out_specs=vmem_spec,
        out_shape=jax.ShapeDtypeStruct((tokens, QUERY_HEADS * HEAD_SIZE), jnp.bfloat16),
        scratch_shapes=[
            pltpu.VMEM((KEY_VALUE_HEADS, cache_rows, HEAD_SIZE), jnp.bfloat16),
            pltpu.VMEM((KEY_VALUE_HEADS, cache_rows, HEAD_SIZE), jnp.bfloat16),
            pltpu.SemaphoreType.DMA((2, KEY_VALUE_HEADS, max_pages)),
            pltpu.VMEM((group * tokens, HEAD_SIZE), jnp.float32),
            pltpu.VMEM((group * tokens, HEAD_SIZE), jnp.float32),
            pltpu.VMEM((group * tokens, HEAD_SIZE), jnp.float32),
        ],
    )(meta, page_ids, queries, new_keys, new_values, k_own, v_own, k_got, v_got)


def on_device(
    tokens,
    norm1_gain,
    query_key_value_weight,
    w_out,
    norm2_gain,
    router_weight,
    w_gate_up,
    w_down,
    routes,
    key_page_store,
    value_page_store,
    page_table,
    cached_pages,
    anchor,
):
    req_index = lax.axis_index("req")
    head_index = lax.axis_index("head")
    count_of_heads = lax.axis_size("head")
    req_count = lax.axis_size("req")
    tokens_per_device = tokens.shape[0]
    req_dev = page_table.shape[0]
    page_size = key_page_store.shape[1]
    share = REQUEST_TOKENS // tokens_per_device
    kv_width = KEY_VALUE_HEADS * HEAD_SIZE

    request = (req_index * count_of_heads + head_index) // share
    half = head_index % share
    old_id = anchor[request]
    place = half * tokens_per_device + jnp.arange(tokens_per_device, dtype=jnp.int32)
    token_positions = cached_pages[old_id] * page_size + place

    normed = rms_scale(tokens.astype(jnp.float32), norm1_gain).astype(jnp.bfloat16)
    projected_rows = jnp.dot(normed, query_key_value_weight, preferred_element_type=jnp.float32)
    half_dim = HEAD_SIZE // 2
    frequency = jnp.exp(
        -jnp.log(jnp.float32(THETA))
        * jnp.arange(half_dim, dtype=jnp.float32)
        * 2.0
        / HEAD_SIZE
    )
    angles = token_positions.astype(jnp.float32)[:, None] * frequency[None, :]
    cosine = jnp.cos(angles)
    sines = jnp.sin(angles)
    queries, appended = rotate(
        projected_rows,
        jnp.concatenate([cosine, cosine], axis=1),
        jnp.concatenate([-sines, sines], axis=1),
    )

    forward_pairs = [
        (h, h + 1) for h in range(count_of_heads) if h % share != share - 1
    ]
    earlier = lax.ppermute(appended, "head", forward_pairs)
    pairs = [(source, source ^ 1) for source in range(req_count)]
    k_got, v_got, table_got = lax.ppermute(
        (key_page_store, value_page_store, page_table), "req", pairs
    )
    moved_in = old_id // req_dev != req_index
    page_ids = jnp.where(moved_in, table_got[old_id % req_dev], page_table[old_id % req_dev])
    meta = jnp.stack(
        [cached_pages[old_id], half.astype(jnp.int32), moved_in.astype(jnp.int32)]
    ).astype(jnp.int32)
    attention = attend(
        meta, page_ids, queries, appended, earlier, key_page_store, value_page_store, k_got, v_got,
    )

    residual = tokens.astype(jnp.float32) + jnp.dot(
        attention, w_out, preferred_element_type=jnp.float32
    )
    normed_moe = rms_scale(residual, norm2_gain).astype(jnp.bfloat16)
    logits = jnp.dot(normed_moe.astype(jnp.float32), router_weight, precision=lax.Precision.HIGHEST)
    route_match = routes[:, :, None] == jnp.arange(logits.shape[1], dtype=jnp.int32)[None, None, :]
    chosen = jnp.sum(jnp.where(route_match, logits[:, None, :], 0.0), axis=2)
    sigmoids = jax.nn.sigmoid(chosen)
    route_gates = sigmoids / jnp.sum(sigmoids, axis=1, keepdims=True)

    exp_dev = w_gate_up.shape[0]
    expert_total = exp_dev * req_count
    capacity = max(2, 3 * tokens_per_device * TOPK // (2 * expert_total))
    slot_total = expert_total * capacity
    flat_ids = routes.reshape(-1)
    route_rows = flat_ids.shape[0]
    one_hot = (flat_ids[:, None] == jnp.arange(expert_total, dtype=jnp.int32)[None, :]).astype(
        jnp.bfloat16
    )
    row_i = lax.broadcasted_iota(jnp.int32, (route_rows, route_rows), 0)
    col_i = lax.broadcasted_iota(jnp.int32, (route_rows, route_rows), 1)
    before = (col_i < row_i).astype(jnp.bfloat16)
    earlier_counts = jnp.dot(before, one_hot, preferred_element_type=jnp.float32)
    slot_ranks = jnp.sum(earlier_counts * one_hot.astype(jnp.float32), axis=1).astype(jnp.int32)
    slot_ids = (flat_ids * capacity + slot_ranks).reshape(tokens_per_device, TOPK)

    slot_iota = jnp.arange(slot_total, dtype=jnp.int32)
    hits = slot_ids[None, :, :] == slot_iota[:, None, None]
    gather_matrix = jnp.any(hits, axis=2).astype(jnp.bfloat16)
    dispatch = jnp.dot(gather_matrix, normed_moe, preferred_element_type=jnp.float32).astype(
        jnp.bfloat16
    )
    dispatch = dispatch.reshape(req_count, exp_dev, capacity, MODEL_WIDTH)
    gate_up = jnp.einsum(
        "nekd,edf->nekf",
        lax.all_to_all(dispatch, "req", split_axis=0, concat_axis=0, tiled=True),
        w_gate_up,
        preferred_element_type=jnp.float32,
    )
    hidden = (jax.nn.relu(gate_up[..., :FE]) * gate_up[..., FE:]).astype(jnp.bfloat16)
    result = jnp.einsum(
        "nekf,efd->nekd", hidden, w_down, preferred_element_type=jnp.float32
    ).astype(jnp.bfloat16)
    results = lax.all_to_all(result, "req", split_axis=0, concat_axis=0, tiled=True)
    flat_results = results.reshape(slot_total, MODEL_WIDTH)

    token_hits = slot_ids[:, :, None] == slot_iota[None, None, :]
    combine = jnp.sum(jnp.where(token_hits, route_gates[:, :, None], 0.0), axis=1)
    expert_sum = jnp.dot(
        combine.astype(jnp.bfloat16), flat_results, preferred_element_type=jnp.float32
    )
    mixed_out = (residual + expert_sum).astype(jnp.bfloat16)
    return (mixed_out, appended)


def solution(mesh):
    return jax.shard_map(
        on_device,
        mesh=mesh,
        in_specs=(
            P(("req", "head"), None),
            P(),
            P(),
            P(),
            P(),
            P(),
            P("req", None, None),
            P("req", None, None),
            P(("req", "head"), None),
            P("req", None, None),
            P("req", None, None),
            P("req", None),
            P(),
            P(),
        ),
        out_specs=(P(("req", "head"), None), P(("req", "head"), None)),
        check_vma=False,
    )
```

```python
import functools

import jax
import jax.numpy as jnp
from jax import lax
from jax.experimental import pallas as pl
from jax.experimental.pallas import tpu as pltpu
from jax.sharding import PartitionSpec as P

MODEL_WIDTH = 1536
QUERY_HEADS = 12
KEY_VALUE_HEADS = 2
HEAD_SIZE = 128
FE = 768
TOPK = 4
REQUEST_TOKENS = 512
PAGE_CHUNK = 128


EPS = 1e-06
THETA = 1000000.0


def rms_scale(values, gain_vector):
    mean_sq = jnp.mean(values * values, axis=-1, keepdims=True)
    return values * lax.rsqrt(mean_sq + EPS) * gain_vector


def apply_rotary(values, where_at):
    half_dim = values.shape[-1] // 2
    frequency = jnp.exp(
        -jnp.log(jnp.float32(THETA))
        * jnp.arange(half_dim, dtype=jnp.float32)
        * 2.0
        / values.shape[-1]
    )
    angles = where_at.astype(jnp.float32)[:, None] * frequency[None, :]
    cosine = jnp.cos(angles)[:, None, :]
    sines = jnp.sin(angles)[:, None, :]
    first_half = values[..., :half_dim]
    second = values[..., half_dim:]
    return jnp.concatenate(
        [first_half * cosine - second * sines, second * cosine + first_half * sines], axis=-1
    )


def rotary_kernel(proj_ref, cos_ref, sin_ref, q_ref, app_ref):
    cosine = cos_ref[...]
    sines = sin_ref[...]
    for h in range(QUERY_HEADS + KEY_VALUE_HEADS):
        x = proj_ref[:, h * HEAD_SIZE : (h + 1) * HEAD_SIZE]
        swapped = pltpu.roll(x, HEAD_SIZE // 2, 1)
        r = (x * cosine + swapped * sines).astype(jnp.bfloat16)
        if h < QUERY_HEADS:
            q_ref[:, h * HEAD_SIZE : (h + 1) * HEAD_SIZE] = r
        else:
            k = h - QUERY_HEADS
            app_ref[:, k * HEAD_SIZE : (k + 1) * HEAD_SIZE] = r
    base = (QUERY_HEADS + KEY_VALUE_HEADS) * HEAD_SIZE
    width = KEY_VALUE_HEADS * HEAD_SIZE
    app_ref[:, width : 2 * width] = proj_ref[:, base : base + width].astype(jnp.bfloat16)


def rotate(projected_rows, cosine, sines):
    tokens = projected_rows.shape[0]
    vmem_spec = pl.BlockSpec(memory_space=pltpu.VMEM)
    return pl.pallas_call(
        rotary_kernel,
        in_specs=[vmem_spec, vmem_spec, vmem_spec],
        out_specs=(vmem_spec, vmem_spec),
        out_shape=(
            jax.ShapeDtypeStruct((tokens, QUERY_HEADS * HEAD_SIZE), jnp.bfloat16),
            jax.ShapeDtypeStruct((tokens, 2 * KEY_VALUE_HEADS * HEAD_SIZE), jnp.bfloat16),
        ),
    )(projected_rows, cosine, sines)


def attention_kernel(
    meta_ref, page_ref, q_ref, kn_ref, vn_ref, k_own, v_own, k_got, v_got,
    o_ref, k_buf, v_buf, sems, m_sc, l_sc, acc_sc, *, group, tokens
):
    count = meta_ref[0]
    half = meta_ref[1]
    moved = meta_ref[2]
    scaling = HEAD_SIZE ** (-0.5)
    contract = (((1,), (1,)), ((), ()))
    lanes = HEAD_SIZE

    def page_copies(c, j, k_pool, v_pool):
        page = page_ref[j]
        rows = pl.ds(pl.multiple_of(j * PAGE_CHUNK, PAGE_CHUNK), PAGE_CHUNK)
        cols = pl.ds(c * HEAD_SIZE, HEAD_SIZE)
        return (
            pltpu.make_async_copy(k_pool.at[page, :, cols], k_buf.at[c, rows, :], sems.at[0, c, j]),
            pltpu.make_async_copy(v_pool.at[page, :, cols], v_buf.at[c, rows, :], sems.at[1, c, j]),
        )

    def start_all(k_pool, v_pool):
        for c in range(KEY_VALUE_HEADS):
            def body(j, carry):
                for copy in page_copies(c, j, k_pool, v_pool):
                    copy.start()
                return carry
            lax.fori_loop(0, count, body, 0)

    @pl.when(moved == 1)
    def _():
        start_all(k_got, v_got)

    @pl.when(moved == 0)
    def _():
        start_all(k_own, v_own)

    def absorb(qg, k, v):
        s = lax.dot_general(qg, k, contract, preferred_element_type=jnp.float32) * scaling
        m_prev = m_sc[...]
        m_next = jnp.maximum(m_prev, jnp.max(s, axis=1, keepdims=True))
        repeat = s.shape[1] // lanes
        wide = m_next if repeat == 1 else jnp.concatenate([m_next] * repeat, axis=1)
        p = jnp.exp(s - wide)
        alpha = jnp.exp(m_prev - m_next)
        l_sc[...] = alpha * l_sc[...] + jnp.sum(p, axis=1, keepdims=True)
        acc_sc[...] = acc_sc[...] * alpha + jnp.dot(
            p.astype(jnp.bfloat16), v, preferred_element_type=jnp.float32
        )
        m_sc[...] = m_next

    for c in range(KEY_VALUE_HEADS):
        heads = range(c * group, (c + 1) * group)
        qg = jnp.concatenate(
            [q_ref[:, g * HEAD_SIZE : (g + 1) * HEAD_SIZE] for g in heads], axis=0
        )
        key_cols = slice(c * HEAD_SIZE, (c + 1) * HEAD_SIZE)
        value_cols = slice((KEY_VALUE_HEADS + c) * HEAD_SIZE, (KEY_VALUE_HEADS + c + 1) * HEAD_SIZE)
        s = lax.dot_general(qg, kn_ref[:, key_cols], contract, preferred_element_type=jnp.float32)
        s = s * scaling
        t = lax.broadcasted_iota(jnp.int32, s.shape, 0) % tokens
        key_pos = lax.broadcasted_iota(jnp.int32, s.shape, 1)
        s = jnp.where(key_pos <= t, s, -jnp.inf)
        m = jnp.max(s, axis=1, keepdims=True)
        p = jnp.exp(s - m)
        l_sc[...] = jnp.broadcast_to(jnp.sum(p, axis=1, keepdims=True), l_sc.shape)
        m_sc[...] = jnp.broadcast_to(m, m_sc.shape)
        acc_sc[...] = jnp.dot(
            p.astype(jnp.bfloat16), kn_ref[:, value_cols], preferred_element_type=jnp.float32
        )

        @pl.when(half == 1)
        def _():
            absorb(qg, vn_ref[:, key_cols], vn_ref[:, value_cols])

        def wait_page(j, carry):
            for copy in page_copies(c, j, k_own, v_own):
                copy.wait()
            return carry

        lax.fori_loop(0, count, wait_page, 0)

        def visit(i, carry):
            first = pl.multiple_of(i * (2 * PAGE_CHUNK), 2 * PAGE_CHUNK)
            absorb(
                qg,
                k_buf[c, pl.ds(first, 2 * PAGE_CHUNK), :],
                v_buf[c, pl.ds(first, 2 * PAGE_CHUNK), :],
            )
            return carry

        lax.fori_loop(0, count // 2, visit, 0)

        @pl.when(count % 2 == 1)
        def _():
            first = pl.multiple_of((count - 1) * PAGE_CHUNK, PAGE_CHUNK)
            absorb(
                qg,
                k_buf[c, pl.ds(first, PAGE_CHUNK), :],
                v_buf[c, pl.ds(first, PAGE_CHUNK), :],
            )

        res = (acc_sc[...] / l_sc[...]).astype(jnp.bfloat16)
        for i, g in enumerate(heads):
            o_ref[:, g * HEAD_SIZE : (g + 1) * HEAD_SIZE] = res[i * tokens : (i + 1) * tokens]


def attend(meta, page_ids, queries, new_keys, new_values, k_own, v_own, k_got, v_got):
    tokens = queries.shape[0]
    group = QUERY_HEADS // KEY_VALUE_HEADS
    max_pages = page_ids.shape[0]
    cache_rows = max_pages * PAGE_CHUNK
    smem = pltpu.MemorySpace.SMEM if hasattr(pltpu, "MemorySpace") else pltpu.SMEM
    vmem_spec = pl.BlockSpec(memory_space=pltpu.VMEM)
    any_spec = pl.BlockSpec(memory_space=pl.ANY)
    return pl.pallas_call(
        functools.partial(attention_kernel, group=group, tokens=tokens),
        in_specs=[
            pl.BlockSpec(memory_space=smem),
            pl.BlockSpec(memory_space=smem),
            vmem_spec,
            vmem_spec,
            vmem_spec,
            any_spec,
            any_spec,
            any_spec,
            any_spec,
        ],
        out_specs=vmem_spec,
        out_shape=jax.ShapeDtypeStruct((tokens, QUERY_HEADS * HEAD_SIZE), jnp.bfloat16),
        scratch_shapes=[
            pltpu.VMEM((KEY_VALUE_HEADS, cache_rows, HEAD_SIZE), jnp.bfloat16),
            pltpu.VMEM((KEY_VALUE_HEADS, cache_rows, HEAD_SIZE), jnp.bfloat16),
            pltpu.SemaphoreType.DMA((2, KEY_VALUE_HEADS, max_pages)),
            pltpu.VMEM((group * tokens, HEAD_SIZE), jnp.float32),
            pltpu.VMEM((group * tokens, HEAD_SIZE), jnp.float32),
            pltpu.VMEM((group * tokens, HEAD_SIZE), jnp.float32),
        ],
    )(meta, page_ids, queries, new_keys, new_values, k_own, v_own, k_got, v_got)


def on_device(
    tokens,
    norm1_gain,
    query_key_value_weight,
    w_out,
    norm2_gain,
    router_weight,
    w_gate_up,
    w_down,
    routes,
    key_page_store,
    value_page_store,
    page_table,
    cached_pages,
    anchor,
):
    req_index = lax.axis_index("req")
    head_index = lax.axis_index("head")
    count_of_heads = lax.axis_size("head")
    req_count = lax.axis_size("req")
    tokens_per_device = tokens.shape[0]
    req_dev = page_table.shape[0]
    page_size = key_page_store.shape[1]
    share = REQUEST_TOKENS // tokens_per_device
    kv_width = KEY_VALUE_HEADS * HEAD_SIZE

    request = (req_index * count_of_heads + head_index) // share
    half = head_index % share
    old_id = anchor[request]
    place = half * tokens_per_device + jnp.arange(tokens_per_device, dtype=jnp.int32)
    token_positions = cached_pages[old_id] * page_size + place

    normed = rms_scale(tokens.astype(jnp.float32), norm1_gain).astype(jnp.bfloat16)
    projected_rows = jnp.dot(normed, query_key_value_weight, preferred_element_type=jnp.float32)
    half_dim = HEAD_SIZE // 2
    frequency = jnp.exp(
        -jnp.log(jnp.float32(THETA))
        * jnp.arange(half_dim, dtype=jnp.float32)
        * 2.0
        / HEAD_SIZE
    )
    angles = token_positions.astype(jnp.float32)[:, None] * frequency[None, :]
    cosine = jnp.cos(angles)
    sines = jnp.sin(angles)
    queries, appended = rotate(
        projected_rows,
        jnp.concatenate([cosine, cosine], axis=1),
        jnp.concatenate([-sines, sines], axis=1),
    )

    forward_pairs = [
        (h, h + 1) for h in range(count_of_heads) if h % share != share - 1
    ]
    earlier = lax.ppermute(appended, "head", forward_pairs)
    pairs = [(source, source ^ 1) for source in range(req_count)]
    k_got, v_got, table_got = lax.ppermute(
        (key_page_store, value_page_store, page_table), "req", pairs
    )
    moved_in = old_id // req_dev != req_index
    page_ids = jnp.where(moved_in, table_got[old_id % req_dev], page_table[old_id % req_dev])
    meta = jnp.stack(
        [cached_pages[old_id], half.astype(jnp.int32), moved_in.astype(jnp.int32)]
    ).astype(jnp.int32)
    attention = attend(
        meta, page_ids, queries, appended, earlier, key_page_store, value_page_store, k_got, v_got,
    )

    residual = tokens.astype(jnp.float32) + jnp.dot(
        attention, w_out, preferred_element_type=jnp.float32
    )
    normed_moe = rms_scale(residual, norm2_gain).astype(jnp.bfloat16)
    logits = jnp.dot(normed_moe.astype(jnp.float32), router_weight, precision=lax.Precision.HIGHEST)
    route_match = routes[:, :, None] == jnp.arange(logits.shape[1], dtype=jnp.int32)[None, None, :]
    chosen = jnp.sum(jnp.where(route_match, logits[:, None, :], 0.0), axis=2)
    sigmoids = jax.nn.sigmoid(chosen)
    route_gates = sigmoids / jnp.sum(sigmoids, axis=1, keepdims=True)

    exp_dev = w_gate_up.shape[0]
    expert_total = exp_dev * req_count
    capacity = max(2, 3 * tokens_per_device * TOPK // (2 * expert_total))
    slot_total = expert_total * capacity
    flat_ids = routes.reshape(-1)
    route_rows = flat_ids.shape[0]
    one_hot = (flat_ids[:, None] == jnp.arange(expert_total, dtype=jnp.int32)[None, :]).astype(
        jnp.bfloat16
    )
    row_i = lax.broadcasted_iota(jnp.int32, (route_rows, route_rows), 0)
    col_i = lax.broadcasted_iota(jnp.int32, (route_rows, route_rows), 1)
    before = (col_i < row_i).astype(jnp.bfloat16)
    earlier_counts = jnp.dot(before, one_hot, preferred_element_type=jnp.float32)
    slot_ranks = jnp.sum(earlier_counts * one_hot.astype(jnp.float32), axis=1).astype(jnp.int32)
    slot_ids = (flat_ids * capacity + slot_ranks).reshape(tokens_per_device, TOPK)

    slot_iota = jnp.arange(slot_total, dtype=jnp.int32)
    hits = slot_ids[None, :, :] == slot_iota[:, None, None]
    gather_matrix = jnp.any(hits, axis=2).astype(jnp.bfloat16)
    dispatch = jnp.dot(gather_matrix, normed_moe, preferred_element_type=jnp.float32).astype(
        jnp.bfloat16
    )
    dispatch = dispatch.reshape(req_count, exp_dev, capacity, MODEL_WIDTH)
    cut = MODEL_WIDTH // 2
    arrived = [
        lax.all_to_all(dispatch[..., :cut], "req", split_axis=0, concat_axis=0, tiled=True),
        lax.all_to_all(dispatch[..., cut:], "req", split_axis=0, concat_axis=0, tiled=True),
    ]
    gate_up = jnp.einsum(
        "nekd,edf->nekf", arrived[0], w_gate_up[:, :cut, :], preferred_element_type=jnp.float32
    ) + jnp.einsum(
        "nekd,edf->nekf", arrived[1], w_gate_up[:, cut:, :], preferred_element_type=jnp.float32
    )
    hidden = (jax.nn.relu(gate_up[..., :FE]) * gate_up[..., FE:]).astype(jnp.bfloat16)
    token_hits = slot_ids[:, :, None] == slot_iota[None, None, :]
    combine = jnp.sum(jnp.where(token_hits, route_gates[:, :, None], 0.0), axis=1)
    combine = combine.astype(jnp.bfloat16)
    sums = []
    for part in range(2):
        result = jnp.einsum(
            "nekf,efd->nekd",
            hidden,
            w_down[:, :, part * cut : (part + 1) * cut],
            preferred_element_type=jnp.float32,
        ).astype(jnp.bfloat16)
        results = lax.all_to_all(result, "req", split_axis=0, concat_axis=0, tiled=True)
        sums.append(
            jnp.dot(
                combine, results.reshape(slot_total, cut), preferred_element_type=jnp.float32
            )
        )
    expert_sum = jnp.concatenate(sums, axis=1)
    mixed_out = (residual + expert_sum).astype(jnp.bfloat16)
    return (mixed_out, appended)


def solution(mesh):
    return jax.shard_map(
        on_device,
        mesh=mesh,
        in_specs=(
            P(("req", "head"), None),
            P(),
            P(),
            P(),
            P(),
            P(),
            P("req", None, None),
            P("req", None, None),
            P(("req", "head"), None),
            P("req", None, None),
            P("req", None, None),
            P("req", None),
            P(),
            P(),
        ),
        out_specs=(P(("req", "head"), None), P(("req", "head"), None)),
        check_vma=False,
    )
```

```python
import functools

import jax
import jax.numpy as jnp
from jax import lax
from jax.experimental import pallas as pl
from jax.experimental.pallas import tpu as pltpu
from jax.sharding import PartitionSpec as P

MODEL_WIDTH = 1536
QUERY_HEADS = 12
KEY_VALUE_HEADS = 2
HEAD_SIZE = 128
FE = 768
TOPK = 4
REQUEST_TOKENS = 512
PAGE_CHUNK = 128


EPS = 1e-06
THETA = 1000000.0


def rms_scale(values, gain_vector):
    mean_sq = jnp.mean(values * values, axis=-1, keepdims=True)
    return values * lax.rsqrt(mean_sq + EPS) * gain_vector


def apply_rotary(values, where_at):
    half_dim = values.shape[-1] // 2
    frequency = jnp.exp(
        -jnp.log(jnp.float32(THETA))
        * jnp.arange(half_dim, dtype=jnp.float32)
        * 2.0
        / values.shape[-1]
    )
    angles = where_at.astype(jnp.float32)[:, None] * frequency[None, :]
    cosine = jnp.cos(angles)[:, None, :]
    sines = jnp.sin(angles)[:, None, :]
    first_half = values[..., :half_dim]
    second = values[..., half_dim:]
    return jnp.concatenate(
        [first_half * cosine - second * sines, second * cosine + first_half * sines], axis=-1
    )


def rotary_kernel(proj_ref, cos_ref, sin_ref, q_ref, app_ref):
    cosine = cos_ref[...]
    sines = sin_ref[...]
    for h in range(QUERY_HEADS + KEY_VALUE_HEADS):
        x = proj_ref[:, h * HEAD_SIZE : (h + 1) * HEAD_SIZE]
        swapped = pltpu.roll(x, HEAD_SIZE // 2, 1)
        r = (x * cosine + swapped * sines).astype(jnp.bfloat16)
        if h < QUERY_HEADS:
            q_ref[:, h * HEAD_SIZE : (h + 1) * HEAD_SIZE] = r
        else:
            k = h - QUERY_HEADS
            app_ref[:, k * HEAD_SIZE : (k + 1) * HEAD_SIZE] = r
    base = (QUERY_HEADS + KEY_VALUE_HEADS) * HEAD_SIZE
    width = KEY_VALUE_HEADS * HEAD_SIZE
    app_ref[:, width : 2 * width] = proj_ref[:, base : base + width].astype(jnp.bfloat16)


def rotate(projected_rows, cosine, sines):
    tokens = projected_rows.shape[0]
    vmem_spec = pl.BlockSpec(memory_space=pltpu.VMEM)
    return pl.pallas_call(
        rotary_kernel,
        in_specs=[vmem_spec, vmem_spec, vmem_spec],
        out_specs=(vmem_spec, vmem_spec),
        out_shape=(
            jax.ShapeDtypeStruct((tokens, QUERY_HEADS * HEAD_SIZE), jnp.bfloat16),
            jax.ShapeDtypeStruct((tokens, 2 * KEY_VALUE_HEADS * HEAD_SIZE), jnp.bfloat16),
        ),
    )(projected_rows, cosine, sines)


def attention_kernel(
    meta_ref, page_ref, q_ref, kn_ref, vn_ref, k_own, v_own, k_got, v_got,
    o_ref, k_buf, v_buf, sems, m_sc, l_sc, acc_sc, *, group, tokens
):
    count = meta_ref[0]
    half = meta_ref[1]
    moved = meta_ref[2]
    scaling = HEAD_SIZE ** (-0.5)
    contract = (((1,), (1,)), ((), ()))
    lanes = HEAD_SIZE

    def page_copies(c, j, k_pool, v_pool):
        page = page_ref[j]
        rows = pl.ds(pl.multiple_of(j * PAGE_CHUNK, PAGE_CHUNK), PAGE_CHUNK)
        cols = pl.ds(c * HEAD_SIZE, HEAD_SIZE)
        return (
            pltpu.make_async_copy(k_pool.at[page, :, cols], k_buf.at[c, rows, :], sems.at[0, c, j]),
            pltpu.make_async_copy(v_pool.at[page, :, cols], v_buf.at[c, rows, :], sems.at[1, c, j]),
        )

    def start_all(k_pool, v_pool):
        for c in range(KEY_VALUE_HEADS):
            def body(j, carry):
                for copy in page_copies(c, j, k_pool, v_pool):
                    copy.start()
                return carry
            lax.fori_loop(0, count, body, 0)

    @pl.when(moved == 1)
    def _():
        start_all(k_got, v_got)

    @pl.when(moved == 0)
    def _():
        start_all(k_own, v_own)

    def absorb(qg, k, v):
        s = lax.dot_general(qg, k, contract, preferred_element_type=jnp.float32) * scaling
        m_prev = m_sc[...]
        m_next = jnp.maximum(m_prev, jnp.max(s, axis=1, keepdims=True))
        repeat = s.shape[1] // lanes
        wide = m_next if repeat == 1 else jnp.concatenate([m_next] * repeat, axis=1)
        p = jnp.exp(s - wide)
        alpha = jnp.exp(m_prev - m_next)
        l_sc[...] = alpha * l_sc[...] + jnp.sum(p, axis=1, keepdims=True)
        acc_sc[...] = acc_sc[...] * alpha + jnp.dot(
            p.astype(jnp.bfloat16), v, preferred_element_type=jnp.float32
        )
        m_sc[...] = m_next

    for c in range(KEY_VALUE_HEADS):
        heads = range(c * group, (c + 1) * group)
        qg = jnp.concatenate(
            [q_ref[:, g * HEAD_SIZE : (g + 1) * HEAD_SIZE] for g in heads], axis=0
        )
        key_cols = slice(c * HEAD_SIZE, (c + 1) * HEAD_SIZE)
        value_cols = slice((KEY_VALUE_HEADS + c) * HEAD_SIZE, (KEY_VALUE_HEADS + c + 1) * HEAD_SIZE)
        s = lax.dot_general(qg, kn_ref[:, key_cols], contract, preferred_element_type=jnp.float32)
        s = s * scaling
        t = lax.broadcasted_iota(jnp.int32, s.shape, 0) % tokens
        key_pos = lax.broadcasted_iota(jnp.int32, s.shape, 1)
        s = jnp.where(key_pos <= t, s, -jnp.inf)
        m = jnp.max(s, axis=1, keepdims=True)
        p = jnp.exp(s - m)
        l_sc[...] = jnp.broadcast_to(jnp.sum(p, axis=1, keepdims=True), l_sc.shape)
        m_sc[...] = jnp.broadcast_to(m, m_sc.shape)
        acc_sc[...] = jnp.dot(
            p.astype(jnp.bfloat16), kn_ref[:, value_cols], preferred_element_type=jnp.float32
        )

        @pl.when(half == 1)
        def _():
            absorb(qg, vn_ref[:, key_cols], vn_ref[:, value_cols])

        def wait_page(j, carry):
            for copy in page_copies(c, j, k_own, v_own):
                copy.wait()
            return carry

        lax.fori_loop(0, count, wait_page, 0)

        def visit(i, carry):
            first = pl.multiple_of(i * (4 * PAGE_CHUNK), 4 * PAGE_CHUNK)
            absorb(
                qg,
                k_buf[c, pl.ds(first, 4 * PAGE_CHUNK), :],
                v_buf[c, pl.ds(first, 4 * PAGE_CHUNK), :],
            )
            return carry

        lax.fori_loop(0, count // 4, visit, 0)

        @pl.when(count % 4 >= 2)
        def _():
            first = pl.multiple_of((count // 4) * (4 * PAGE_CHUNK), 4 * PAGE_CHUNK)
            absorb(
                qg,
                k_buf[c, pl.ds(first, 2 * PAGE_CHUNK), :],
                v_buf[c, pl.ds(first, 2 * PAGE_CHUNK), :],
            )

        @pl.when(count % 2 == 1)
        def _():
            first = pl.multiple_of((count - 1) * PAGE_CHUNK, PAGE_CHUNK)
            absorb(
                qg,
                k_buf[c, pl.ds(first, PAGE_CHUNK), :],
                v_buf[c, pl.ds(first, PAGE_CHUNK), :],
            )

        res = (acc_sc[...] / l_sc[...]).astype(jnp.bfloat16)
        for i, g in enumerate(heads):
            o_ref[:, g * HEAD_SIZE : (g + 1) * HEAD_SIZE] = res[i * tokens : (i + 1) * tokens]


def attend(meta, page_ids, queries, new_keys, new_values, k_own, v_own, k_got, v_got):
    tokens = queries.shape[0]
    group = QUERY_HEADS // KEY_VALUE_HEADS
    max_pages = page_ids.shape[0]
    cache_rows = max_pages * PAGE_CHUNK
    smem = pltpu.MemorySpace.SMEM if hasattr(pltpu, "MemorySpace") else pltpu.SMEM
    vmem_spec = pl.BlockSpec(memory_space=pltpu.VMEM)
    any_spec = pl.BlockSpec(memory_space=pl.ANY)
    return pl.pallas_call(
        functools.partial(attention_kernel, group=group, tokens=tokens),
        in_specs=[
            pl.BlockSpec(memory_space=smem),
            pl.BlockSpec(memory_space=smem),
            vmem_spec,
            vmem_spec,
            vmem_spec,
            any_spec,
            any_spec,
            any_spec,
            any_spec,
        ],
        out_specs=vmem_spec,
        out_shape=jax.ShapeDtypeStruct((tokens, QUERY_HEADS * HEAD_SIZE), jnp.bfloat16),
        scratch_shapes=[
            pltpu.VMEM((KEY_VALUE_HEADS, cache_rows, HEAD_SIZE), jnp.bfloat16),
            pltpu.VMEM((KEY_VALUE_HEADS, cache_rows, HEAD_SIZE), jnp.bfloat16),
            pltpu.SemaphoreType.DMA((2, KEY_VALUE_HEADS, max_pages)),
            pltpu.VMEM((group * tokens, HEAD_SIZE), jnp.float32),
            pltpu.VMEM((group * tokens, HEAD_SIZE), jnp.float32),
            pltpu.VMEM((group * tokens, HEAD_SIZE), jnp.float32),
        ],
    )(meta, page_ids, queries, new_keys, new_values, k_own, v_own, k_got, v_got)


def on_device(
    tokens,
    norm1_gain,
    query_key_value_weight,
    w_out,
    norm2_gain,
    router_weight,
    w_gate_up,
    w_down,
    routes,
    key_page_store,
    value_page_store,
    page_table,
    cached_pages,
    anchor,
):
    req_index = lax.axis_index("req")
    head_index = lax.axis_index("head")
    count_of_heads = lax.axis_size("head")
    req_count = lax.axis_size("req")
    tokens_per_device = tokens.shape[0]
    req_dev = page_table.shape[0]
    page_size = key_page_store.shape[1]
    share = REQUEST_TOKENS // tokens_per_device
    kv_width = KEY_VALUE_HEADS * HEAD_SIZE

    request = (req_index * count_of_heads + head_index) // share
    half = head_index % share
    old_id = anchor[request]
    place = half * tokens_per_device + jnp.arange(tokens_per_device, dtype=jnp.int32)
    token_positions = cached_pages[old_id] * page_size + place

    normed = rms_scale(tokens.astype(jnp.float32), norm1_gain).astype(jnp.bfloat16)
    projected_rows = jnp.dot(normed, query_key_value_weight, preferred_element_type=jnp.float32)
    half_dim = HEAD_SIZE // 2
    frequency = jnp.exp(
        -jnp.log(jnp.float32(THETA))
        * jnp.arange(half_dim, dtype=jnp.float32)
        * 2.0
        / HEAD_SIZE
    )
    angles = token_positions.astype(jnp.float32)[:, None] * frequency[None, :]
    cosine = jnp.cos(angles)
    sines = jnp.sin(angles)
    queries, appended = rotate(
        projected_rows,
        jnp.concatenate([cosine, cosine], axis=1),
        jnp.concatenate([-sines, sines], axis=1),
    )

    forward_pairs = [
        (h, h + 1) for h in range(count_of_heads) if h % share != share - 1
    ]
    earlier = lax.ppermute(appended, "head", forward_pairs)
    pairs = [(source, source ^ 1) for source in range(req_count)]
    k_got, v_got, table_got = lax.ppermute(
        (key_page_store, value_page_store, page_table), "req", pairs
    )
    moved_in = old_id // req_dev != req_index
    page_ids = jnp.where(moved_in, table_got[old_id % req_dev], page_table[old_id % req_dev])
    meta = jnp.stack(
        [cached_pages[old_id], half.astype(jnp.int32), moved_in.astype(jnp.int32)]
    ).astype(jnp.int32)
    attention = attend(
        meta, page_ids, queries, appended, earlier, key_page_store, value_page_store, k_got, v_got,
    )

    residual = tokens.astype(jnp.float32) + jnp.dot(
        attention, w_out, preferred_element_type=jnp.float32
    )
    normed_moe = rms_scale(residual, norm2_gain).astype(jnp.bfloat16)
    logits = jnp.dot(normed_moe.astype(jnp.float32), router_weight, precision=lax.Precision.HIGHEST)
    route_match = routes[:, :, None] == jnp.arange(logits.shape[1], dtype=jnp.int32)[None, None, :]
    chosen = jnp.sum(jnp.where(route_match, logits[:, None, :], 0.0), axis=2)
    sigmoids = jax.nn.sigmoid(chosen)
    route_gates = sigmoids / jnp.sum(sigmoids, axis=1, keepdims=True)

    exp_dev = w_gate_up.shape[0]
    expert_total = exp_dev * req_count
    capacity = max(2, 3 * tokens_per_device * TOPK // (2 * expert_total))
    slot_total = expert_total * capacity
    flat_ids = routes.reshape(-1)
    route_rows = flat_ids.shape[0]
    one_hot = (flat_ids[:, None] == jnp.arange(expert_total, dtype=jnp.int32)[None, :]).astype(
        jnp.bfloat16
    )
    row_i = lax.broadcasted_iota(jnp.int32, (route_rows, route_rows), 0)
    col_i = lax.broadcasted_iota(jnp.int32, (route_rows, route_rows), 1)
    before = (col_i < row_i).astype(jnp.bfloat16)
    earlier_counts = jnp.dot(before, one_hot, preferred_element_type=jnp.float32)
    slot_ranks = jnp.sum(earlier_counts * one_hot.astype(jnp.float32), axis=1).astype(jnp.int32)
    slot_ids = (flat_ids * capacity + slot_ranks).reshape(tokens_per_device, TOPK)

    slot_iota = jnp.arange(slot_total, dtype=jnp.int32)
    hits = slot_ids[None, :, :] == slot_iota[:, None, None]
    gather_matrix = jnp.any(hits, axis=2).astype(jnp.bfloat16)
    dispatch = jnp.dot(gather_matrix, normed_moe, preferred_element_type=jnp.float32).astype(
        jnp.bfloat16
    )
    dispatch = dispatch.reshape(req_count, exp_dev, capacity, MODEL_WIDTH)
    gate_up = jnp.einsum(
        "nekd,edf->nekf",
        lax.all_to_all(dispatch, "req", split_axis=0, concat_axis=0, tiled=True),
        w_gate_up,
        preferred_element_type=jnp.float32,
    )
    hidden = (jax.nn.relu(gate_up[..., :FE]) * gate_up[..., FE:]).astype(jnp.bfloat16)
    result = jnp.einsum(
        "nekf,efd->nekd", hidden, w_down, preferred_element_type=jnp.float32
    ).astype(jnp.bfloat16)
    results = lax.all_to_all(result, "req", split_axis=0, concat_axis=0, tiled=True)
    flat_results = results.reshape(slot_total, MODEL_WIDTH)

    token_hits = slot_ids[:, :, None] == slot_iota[None, None, :]
    combine = jnp.sum(jnp.where(token_hits, route_gates[:, :, None], 0.0), axis=1)
    expert_sum = jnp.dot(
        combine.astype(jnp.bfloat16), flat_results, preferred_element_type=jnp.float32
    )
    mixed_out = (residual + expert_sum).astype(jnp.bfloat16)
    return (mixed_out, appended)


def solution(mesh):
    return jax.shard_map(
        on_device,
        mesh=mesh,
        in_specs=(
            P(("req", "head"), None),
            P(),
            P(),
            P(),
            P(),
            P(),
            P("req", None, None),
            P("req", None, None),
            P(("req", "head"), None),
            P("req", None, None),
            P("req", None, None),
            P("req", None),
            P(),
            P(),
        ),
        out_specs=(P(("req", "head"), None), P(("req", "head"), None)),
        check_vma=False,
    )
```

```python
import functools

import jax
import jax.numpy as jnp
from jax import lax
from jax.experimental import pallas as pl
from jax.experimental.pallas import tpu as pltpu
from jax.sharding import PartitionSpec as P

MODEL_WIDTH = 1536
QUERY_HEADS = 12
KEY_VALUE_HEADS = 2
HEAD_SIZE = 128
FE = 768
TOPK = 4
REQUEST_TOKENS = 512
PAGE_CHUNK = 128


EPS = 1e-06
THETA = 1000000.0


def rms_scale(values, gain_vector):
    mean_sq = jnp.mean(values * values, axis=-1, keepdims=True)
    return values * lax.rsqrt(mean_sq + EPS) * gain_vector


def apply_rotary(values, where_at):
    half_dim = values.shape[-1] // 2
    frequency = jnp.exp(
        -jnp.log(jnp.float32(THETA))
        * jnp.arange(half_dim, dtype=jnp.float32)
        * 2.0
        / values.shape[-1]
    )
    angles = where_at.astype(jnp.float32)[:, None] * frequency[None, :]
    cosine = jnp.cos(angles)[:, None, :]
    sines = jnp.sin(angles)[:, None, :]
    first_half = values[..., :half_dim]
    second = values[..., half_dim:]
    return jnp.concatenate(
        [first_half * cosine - second * sines, second * cosine + first_half * sines], axis=-1
    )


def rotary_kernel(proj_ref, cos_ref, sin_ref, q_ref, app_ref):
    cosine = cos_ref[...]
    sines = sin_ref[...]
    for h in range(QUERY_HEADS + KEY_VALUE_HEADS):
        x = proj_ref[:, h * HEAD_SIZE : (h + 1) * HEAD_SIZE]
        swapped = pltpu.roll(x, HEAD_SIZE // 2, 1)
        r = (x * cosine + swapped * sines).astype(jnp.bfloat16)
        if h < QUERY_HEADS:
            q_ref[:, h * HEAD_SIZE : (h + 1) * HEAD_SIZE] = r
        else:
            k = h - QUERY_HEADS
            app_ref[:, k * HEAD_SIZE : (k + 1) * HEAD_SIZE] = r
    base = (QUERY_HEADS + KEY_VALUE_HEADS) * HEAD_SIZE
    width = KEY_VALUE_HEADS * HEAD_SIZE
    app_ref[:, width : 2 * width] = proj_ref[:, base : base + width].astype(jnp.bfloat16)


def rotate(projected_rows, cosine, sines):
    tokens = projected_rows.shape[0]
    vmem_spec = pl.BlockSpec(memory_space=pltpu.VMEM)
    return pl.pallas_call(
        rotary_kernel,
        in_specs=[vmem_spec, vmem_spec, vmem_spec],
        out_specs=(vmem_spec, vmem_spec),
        out_shape=(
            jax.ShapeDtypeStruct((tokens, QUERY_HEADS * HEAD_SIZE), jnp.bfloat16),
            jax.ShapeDtypeStruct((tokens, 2 * KEY_VALUE_HEADS * HEAD_SIZE), jnp.bfloat16),
        ),
    )(projected_rows, cosine, sines)


def attention_kernel(
    meta_ref, page_ref, q_ref, kn_ref, vn_ref, k_own, v_own, k_got, v_got,
    o_ref, k_buf, v_buf, sems, m_sc, l_sc, acc_sc, *, group, tokens
):
    count = meta_ref[0]
    half = meta_ref[1]
    moved = meta_ref[2]
    scaling = HEAD_SIZE ** (-0.5)
    contract = (((1,), (1,)), ((), ()))
    lanes = HEAD_SIZE

    def page_copies(c, j, k_pool, v_pool):
        page = page_ref[j]
        rows = pl.ds(pl.multiple_of(j * PAGE_CHUNK, PAGE_CHUNK), PAGE_CHUNK)
        cols = pl.ds(c * HEAD_SIZE, HEAD_SIZE)
        return (
            pltpu.make_async_copy(k_pool.at[page, :, cols], k_buf.at[c, rows, :], sems.at[0, c, j]),
            pltpu.make_async_copy(v_pool.at[page, :, cols], v_buf.at[c, rows, :], sems.at[1, c, j]),
        )

    def start_all(k_pool, v_pool):
        for c in range(KEY_VALUE_HEADS):
            def body(j, carry):
                for copy in page_copies(c, j, k_pool, v_pool):
                    copy.start()
                return carry
            lax.fori_loop(0, count, body, 0)

    @pl.when(moved == 1)
    def _():
        start_all(k_got, v_got)

    @pl.when(moved == 0)
    def _():
        start_all(k_own, v_own)

    def absorb(qg, k, v):
        s = lax.dot_general(qg, k, contract, preferred_element_type=jnp.float32)
        m_prev = m_sc[...]
        m_next = jnp.maximum(m_prev, jnp.max(s, axis=1, keepdims=True) * scaling)
        repeat = s.shape[1] // lanes
        wide = m_next if repeat == 1 else jnp.concatenate([m_next] * repeat, axis=1)
        p = jnp.exp(s * scaling - wide)
        alpha = jnp.exp(m_prev - m_next)
        l_sc[...] = alpha * l_sc[...] + jnp.sum(p, axis=1, keepdims=True)
        acc_sc[...] = acc_sc[...] * alpha + jnp.dot(
            p.astype(jnp.bfloat16), v, preferred_element_type=jnp.float32
        )
        m_sc[...] = m_next

    for c in range(KEY_VALUE_HEADS):
        heads = range(c * group, (c + 1) * group)
        qg = jnp.concatenate(
            [q_ref[:, g * HEAD_SIZE : (g + 1) * HEAD_SIZE] for g in heads], axis=0
        )
        key_cols = slice(c * HEAD_SIZE, (c + 1) * HEAD_SIZE)
        value_cols = slice((KEY_VALUE_HEADS + c) * HEAD_SIZE, (KEY_VALUE_HEADS + c + 1) * HEAD_SIZE)
        s = lax.dot_general(qg, kn_ref[:, key_cols], contract, preferred_element_type=jnp.float32)
        t = lax.broadcasted_iota(jnp.int32, s.shape, 0) % tokens
        key_pos = lax.broadcasted_iota(jnp.int32, s.shape, 1)
        s = jnp.where(key_pos <= t, s, -jnp.inf)
        m = jnp.max(s, axis=1, keepdims=True) * scaling
        p = jnp.exp(s * scaling - m)
        l_sc[...] = jnp.broadcast_to(jnp.sum(p, axis=1, keepdims=True), l_sc.shape)
        m_sc[...] = jnp.broadcast_to(m, m_sc.shape)
        acc_sc[...] = jnp.dot(
            p.astype(jnp.bfloat16), kn_ref[:, value_cols], preferred_element_type=jnp.float32
        )

        @pl.when(half == 1)
        def _():
            absorb(qg, vn_ref[:, key_cols], vn_ref[:, value_cols])

        def wait_page(j, carry):
            for copy in page_copies(c, j, k_own, v_own):
                copy.wait()
            return carry

        lax.fori_loop(0, count, wait_page, 0)

        def visit(i, carry):
            first = pl.multiple_of(i * (4 * PAGE_CHUNK), 4 * PAGE_CHUNK)
            absorb(
                qg,
                k_buf[c, pl.ds(first, 4 * PAGE_CHUNK), :],
                v_buf[c, pl.ds(first, 4 * PAGE_CHUNK), :],
            )
            return carry

        lax.fori_loop(0, count // 4, visit, 0)

        @pl.when(count % 4 >= 2)
        def _():
            first = pl.multiple_of((count // 4) * (4 * PAGE_CHUNK), 4 * PAGE_CHUNK)
            absorb(
                qg,
                k_buf[c, pl.ds(first, 2 * PAGE_CHUNK), :],
                v_buf[c, pl.ds(first, 2 * PAGE_CHUNK), :],
            )

        @pl.when(count % 2 == 1)
        def _():
            first = pl.multiple_of((count - 1) * PAGE_CHUNK, PAGE_CHUNK)
            absorb(
                qg,
                k_buf[c, pl.ds(first, PAGE_CHUNK), :],
                v_buf[c, pl.ds(first, PAGE_CHUNK), :],
            )

        res = (acc_sc[...] / l_sc[...]).astype(jnp.bfloat16)
        for i, g in enumerate(heads):
            o_ref[:, g * HEAD_SIZE : (g + 1) * HEAD_SIZE] = res[i * tokens : (i + 1) * tokens]


def attend(meta, page_ids, queries, new_keys, new_values, k_own, v_own, k_got, v_got):
    tokens = queries.shape[0]
    group = QUERY_HEADS // KEY_VALUE_HEADS
    max_pages = page_ids.shape[0]
    cache_rows = max_pages * PAGE_CHUNK
    smem = pltpu.MemorySpace.SMEM if hasattr(pltpu, "MemorySpace") else pltpu.SMEM
    vmem_spec = pl.BlockSpec(memory_space=pltpu.VMEM)
    any_spec = pl.BlockSpec(memory_space=pl.ANY)
    return pl.pallas_call(
        functools.partial(attention_kernel, group=group, tokens=tokens),
        in_specs=[
            pl.BlockSpec(memory_space=smem),
            pl.BlockSpec(memory_space=smem),
            vmem_spec,
            vmem_spec,
            vmem_spec,
            any_spec,
            any_spec,
            any_spec,
            any_spec,
        ],
        out_specs=vmem_spec,
        out_shape=jax.ShapeDtypeStruct((tokens, QUERY_HEADS * HEAD_SIZE), jnp.bfloat16),
        scratch_shapes=[
            pltpu.VMEM((KEY_VALUE_HEADS, cache_rows, HEAD_SIZE), jnp.bfloat16),
            pltpu.VMEM((KEY_VALUE_HEADS, cache_rows, HEAD_SIZE), jnp.bfloat16),
            pltpu.SemaphoreType.DMA((2, KEY_VALUE_HEADS, max_pages)),
            pltpu.VMEM((group * tokens, HEAD_SIZE), jnp.float32),
            pltpu.VMEM((group * tokens, HEAD_SIZE), jnp.float32),
            pltpu.VMEM((group * tokens, HEAD_SIZE), jnp.float32),
        ],
    )(meta, page_ids, queries, new_keys, new_values, k_own, v_own, k_got, v_got)


def on_device(
    tokens,
    norm1_gain,
    query_key_value_weight,
    w_out,
    norm2_gain,
    router_weight,
    w_gate_up,
    w_down,
    routes,
    key_page_store,
    value_page_store,
    page_table,
    cached_pages,
    anchor,
):
    req_index = lax.axis_index("req")
    head_index = lax.axis_index("head")
    count_of_heads = lax.axis_size("head")
    req_count = lax.axis_size("req")
    tokens_per_device = tokens.shape[0]
    req_dev = page_table.shape[0]
    page_size = key_page_store.shape[1]
    share = REQUEST_TOKENS // tokens_per_device
    kv_width = KEY_VALUE_HEADS * HEAD_SIZE

    request = (req_index * count_of_heads + head_index) // share
    half = head_index % share
    old_id = anchor[request]
    place = half * tokens_per_device + jnp.arange(tokens_per_device, dtype=jnp.int32)
    token_positions = cached_pages[old_id] * page_size + place

    normed = rms_scale(tokens.astype(jnp.float32), norm1_gain).astype(jnp.bfloat16)
    projected_rows = jnp.dot(normed, query_key_value_weight, preferred_element_type=jnp.float32)
    half_dim = HEAD_SIZE // 2
    frequency = jnp.exp(
        -jnp.log(jnp.float32(THETA))
        * jnp.arange(half_dim, dtype=jnp.float32)
        * 2.0
        / HEAD_SIZE
    )
    angles = token_positions.astype(jnp.float32)[:, None] * frequency[None, :]
    cosine = jnp.cos(angles)
    sines = jnp.sin(angles)
    queries, appended = rotate(
        projected_rows,
        jnp.concatenate([cosine, cosine], axis=1),
        jnp.concatenate([-sines, sines], axis=1),
    )

    forward_pairs = [
        (h, h + 1) for h in range(count_of_heads) if h % share != share - 1
    ]
    earlier = lax.ppermute(appended, "head", forward_pairs)
    pairs = [(source, source ^ 1) for source in range(req_count)]
    k_got, v_got, table_got = lax.ppermute(
        (key_page_store, value_page_store, page_table), "req", pairs
    )
    moved_in = old_id // req_dev != req_index
    page_ids = jnp.where(moved_in, table_got[old_id % req_dev], page_table[old_id % req_dev])
    meta = jnp.stack(
        [cached_pages[old_id], half.astype(jnp.int32), moved_in.astype(jnp.int32)]
    ).astype(jnp.int32)
    attention = attend(
        meta, page_ids, queries, appended, earlier, key_page_store, value_page_store, k_got, v_got,
    )

    residual = tokens.astype(jnp.float32) + jnp.dot(
        attention, w_out, preferred_element_type=jnp.float32
    )
    normed_moe = rms_scale(residual, norm2_gain).astype(jnp.bfloat16)
    logits = jnp.dot(normed_moe.astype(jnp.float32), router_weight, precision=lax.Precision.HIGHEST)
    route_match = routes[:, :, None] == jnp.arange(logits.shape[1], dtype=jnp.int32)[None, None, :]
    chosen = jnp.sum(jnp.where(route_match, logits[:, None, :], 0.0), axis=2)
    sigmoids = jax.nn.sigmoid(chosen)
    route_gates = sigmoids / jnp.sum(sigmoids, axis=1, keepdims=True)

    exp_dev = w_gate_up.shape[0]
    expert_total = exp_dev * req_count
    capacity = max(2, 3 * tokens_per_device * TOPK // (2 * expert_total))
    slot_total = expert_total * capacity
    flat_ids = routes.reshape(-1)
    route_rows = flat_ids.shape[0]
    one_hot = (flat_ids[:, None] == jnp.arange(expert_total, dtype=jnp.int32)[None, :]).astype(
        jnp.bfloat16
    )
    row_i = lax.broadcasted_iota(jnp.int32, (route_rows, route_rows), 0)
    col_i = lax.broadcasted_iota(jnp.int32, (route_rows, route_rows), 1)
    before = (col_i < row_i).astype(jnp.bfloat16)
    earlier_counts = jnp.dot(before, one_hot, preferred_element_type=jnp.float32)
    slot_ranks = jnp.sum(earlier_counts * one_hot.astype(jnp.float32), axis=1).astype(jnp.int32)
    slot_ids = (flat_ids * capacity + slot_ranks).reshape(tokens_per_device, TOPK)

    slot_iota = jnp.arange(slot_total, dtype=jnp.int32)
    hits = slot_ids[None, :, :] == slot_iota[:, None, None]
    gather_matrix = jnp.any(hits, axis=2).astype(jnp.bfloat16)
    dispatch = jnp.dot(gather_matrix, normed_moe, preferred_element_type=jnp.float32).astype(
        jnp.bfloat16
    )
    dispatch = dispatch.reshape(req_count, exp_dev, capacity, MODEL_WIDTH)
    gate_up = jnp.einsum(
        "nekd,edf->nekf",
        lax.all_to_all(dispatch, "req", split_axis=0, concat_axis=0, tiled=True),
        w_gate_up,
        preferred_element_type=jnp.float32,
    )
    hidden = (jax.nn.relu(gate_up[..., :FE]) * gate_up[..., FE:]).astype(jnp.bfloat16)
    result = jnp.einsum(
        "nekf,efd->nekd", hidden, w_down, preferred_element_type=jnp.float32
    ).astype(jnp.bfloat16)
    results = lax.all_to_all(result, "req", split_axis=0, concat_axis=0, tiled=True)
    flat_results = results.reshape(slot_total, MODEL_WIDTH)

    token_hits = slot_ids[:, :, None] == slot_iota[None, None, :]
    combine = jnp.sum(jnp.where(token_hits, route_gates[:, :, None], 0.0), axis=1)
    expert_sum = jnp.dot(
        combine.astype(jnp.bfloat16), flat_results, preferred_element_type=jnp.float32
    )
    mixed_out = (residual + expert_sum).astype(jnp.bfloat16)
    return (mixed_out, appended)


def solution(mesh):
    return jax.shard_map(
        on_device,
        mesh=mesh,
        in_specs=(
            P(("req", "head"), None),
            P(),
            P(),
            P(),
            P(),
            P(),
            P("req", None, None),
            P("req", None, None),
            P(("req", "head"), None),
            P("req", None, None),
            P("req", None, None),
            P("req", None),
            P(),
            P(),
        ),
        out_specs=(P(("req", "head"), None), P(("req", "head"), None)),
        check_vma=False,
    )
```

```python
import functools

import jax
import jax.numpy as jnp
from jax import lax
from jax.experimental import pallas as pl
from jax.experimental.pallas import tpu as pltpu
from jax.sharding import PartitionSpec as P

MODEL_WIDTH = 1536
QUERY_HEADS = 12
KEY_VALUE_HEADS = 2
HEAD_SIZE = 128
FE = 768
TOPK = 4
REQUEST_TOKENS = 512
PAGE_CHUNK = 128


EPS = 1e-06
THETA = 1000000.0


def rms_scale(values, gain_vector):
    mean_sq = jnp.mean(values * values, axis=-1, keepdims=True)
    return values * lax.rsqrt(mean_sq + EPS) * gain_vector


def apply_rotary(values, where_at):
    half_dim = values.shape[-1] // 2
    frequency = jnp.exp(
        -jnp.log(jnp.float32(THETA))
        * jnp.arange(half_dim, dtype=jnp.float32)
        * 2.0
        / values.shape[-1]
    )
    angles = where_at.astype(jnp.float32)[:, None] * frequency[None, :]
    cosine = jnp.cos(angles)[:, None, :]
    sines = jnp.sin(angles)[:, None, :]
    first_half = values[..., :half_dim]
    second = values[..., half_dim:]
    return jnp.concatenate(
        [first_half * cosine - second * sines, second * cosine + first_half * sines], axis=-1
    )


def rotary_kernel(proj_ref, cos_ref, sin_ref, q_ref, app_ref):
    cosine = cos_ref[...]
    sines = sin_ref[...]
    for h in range(QUERY_HEADS + KEY_VALUE_HEADS):
        x = proj_ref[:, h * HEAD_SIZE : (h + 1) * HEAD_SIZE]
        swapped = pltpu.roll(x, HEAD_SIZE // 2, 1)
        r = (x * cosine + swapped * sines).astype(jnp.bfloat16)
        if h < QUERY_HEADS:
            q_ref[:, h * HEAD_SIZE : (h + 1) * HEAD_SIZE] = r
        else:
            k = h - QUERY_HEADS
            app_ref[:, k * HEAD_SIZE : (k + 1) * HEAD_SIZE] = r
    base = (QUERY_HEADS + KEY_VALUE_HEADS) * HEAD_SIZE
    width = KEY_VALUE_HEADS * HEAD_SIZE
    app_ref[:, width : 2 * width] = proj_ref[:, base : base + width].astype(jnp.bfloat16)


def rotate(projected_rows, cosine, sines):
    tokens = projected_rows.shape[0]
    vmem_spec = pl.BlockSpec(memory_space=pltpu.VMEM)
    return pl.pallas_call(
        rotary_kernel,
        in_specs=[vmem_spec, vmem_spec, vmem_spec],
        out_specs=(vmem_spec, vmem_spec),
        out_shape=(
            jax.ShapeDtypeStruct((tokens, QUERY_HEADS * HEAD_SIZE), jnp.bfloat16),
            jax.ShapeDtypeStruct((tokens, 2 * KEY_VALUE_HEADS * HEAD_SIZE), jnp.bfloat16),
        ),
    )(projected_rows, cosine, sines)


def attention_kernel(
    meta_ref, page_ref, q_ref, kn_ref, vn_ref, k_own, v_own, k_got, v_got,
    o_ref, k_buf, v_buf, sems, m_sc, l_sc, acc_sc, *, group, tokens
):
    count = meta_ref[0]
    half = meta_ref[1]
    moved = meta_ref[2]
    scaling = HEAD_SIZE ** (-0.5)
    contract = (((1,), (1,)), ((), ()))
    lanes = HEAD_SIZE

    def page_copies(c, j, k_pool, v_pool):
        page = page_ref[j]
        rows = pl.ds(pl.multiple_of(j * PAGE_CHUNK, PAGE_CHUNK), PAGE_CHUNK)
        cols = pl.ds(c * HEAD_SIZE, HEAD_SIZE)
        return (
            pltpu.make_async_copy(k_pool.at[page, :, cols], k_buf.at[c, rows, :], sems.at[0, c, j]),
            pltpu.make_async_copy(v_pool.at[page, :, cols], v_buf.at[c, rows, :], sems.at[1, c, j]),
        )

    def start_all(k_pool, v_pool):
        for c in range(KEY_VALUE_HEADS):
            def body(j, carry):
                for copy in page_copies(c, j, k_pool, v_pool):
                    copy.start()
                return carry
            lax.fori_loop(0, count, body, 0)

    @pl.when(moved == 1)
    def _():
        start_all(k_got, v_got)

    @pl.when(moved == 0)
    def _():
        start_all(k_own, v_own)

    def absorb(qg, k, v):
        s = lax.dot_general(qg, k, contract, preferred_element_type=jnp.float32)
        m_prev = m_sc[...]
        m_next = jnp.maximum(m_prev, jnp.max(s, axis=1, keepdims=True) * scaling)
        repeat = s.shape[1] // lanes
        wide = m_next if repeat == 1 else jnp.concatenate([m_next] * repeat, axis=1)
        p = jnp.exp(s * scaling - wide)
        alpha = jnp.exp(m_prev - m_next)
        l_sc[...] = alpha * l_sc[...] + jnp.sum(p, axis=1, keepdims=True)
        acc_sc[...] = acc_sc[...] * alpha + jnp.dot(
            p.astype(jnp.bfloat16), v, preferred_element_type=jnp.float32
        )
        m_sc[...] = m_next

    for c in range(KEY_VALUE_HEADS):
        heads = range(c * group, (c + 1) * group)
        qg = jnp.concatenate(
            [q_ref[:, g * HEAD_SIZE : (g + 1) * HEAD_SIZE] for g in heads], axis=0
        )
        key_cols = slice(c * HEAD_SIZE, (c + 1) * HEAD_SIZE)
        value_cols = slice((KEY_VALUE_HEADS + c) * HEAD_SIZE, (KEY_VALUE_HEADS + c + 1) * HEAD_SIZE)
        s = lax.dot_general(qg, kn_ref[:, key_cols], contract, preferred_element_type=jnp.float32)
        t = lax.broadcasted_iota(jnp.int32, s.shape, 0) % tokens
        key_pos = lax.broadcasted_iota(jnp.int32, s.shape, 1)
        s = jnp.where(key_pos <= t, s, -jnp.inf)
        m = jnp.max(s, axis=1, keepdims=True) * scaling
        p = jnp.exp(s * scaling - m)
        l_sc[...] = jnp.broadcast_to(jnp.sum(p, axis=1, keepdims=True), l_sc.shape)
        m_sc[...] = jnp.broadcast_to(m, m_sc.shape)
        acc_sc[...] = jnp.dot(
            p.astype(jnp.bfloat16), kn_ref[:, value_cols], preferred_element_type=jnp.float32
        )

        @pl.when(half == 1)
        def _():
            absorb(qg, vn_ref[:, key_cols], vn_ref[:, value_cols])

        def wait_page(j, carry):
            for copy in page_copies(c, j, k_own, v_own):
                copy.wait()
            return carry

        lax.fori_loop(0, count, wait_page, 0)

        def visit(i, carry):
            first = pl.multiple_of(i * (4 * PAGE_CHUNK), 4 * PAGE_CHUNK)
            absorb(
                qg,
                k_buf[c, pl.ds(first, 4 * PAGE_CHUNK), :],
                v_buf[c, pl.ds(first, 4 * PAGE_CHUNK), :],
            )
            return carry

        lax.fori_loop(0, count // 4, visit, 0)

        @pl.when(count % 4 >= 2)
        def _():
            first = pl.multiple_of((count // 4) * (4 * PAGE_CHUNK), 4 * PAGE_CHUNK)
            absorb(
                qg,
                k_buf[c, pl.ds(first, 2 * PAGE_CHUNK), :],
                v_buf[c, pl.ds(first, 2 * PAGE_CHUNK), :],
            )

        @pl.when(count % 2 == 1)
        def _():
            first = pl.multiple_of((count - 1) * PAGE_CHUNK, PAGE_CHUNK)
            absorb(
                qg,
                k_buf[c, pl.ds(first, PAGE_CHUNK), :],
                v_buf[c, pl.ds(first, PAGE_CHUNK), :],
            )

        res = (acc_sc[...] / l_sc[...]).astype(jnp.bfloat16)
        for i, g in enumerate(heads):
            o_ref[:, g * HEAD_SIZE : (g + 1) * HEAD_SIZE] = res[i * tokens : (i + 1) * tokens]


def attend(meta, page_ids, queries, new_keys, new_values, k_own, v_own, k_got, v_got):
    tokens = queries.shape[0]
    group = QUERY_HEADS // KEY_VALUE_HEADS
    max_pages = page_ids.shape[0]
    cache_rows = max_pages * PAGE_CHUNK
    smem = pltpu.MemorySpace.SMEM if hasattr(pltpu, "MemorySpace") else pltpu.SMEM
    vmem_spec = pl.BlockSpec(memory_space=pltpu.VMEM)
    any_spec = pl.BlockSpec(memory_space=pl.ANY)
    return pl.pallas_call(
        functools.partial(attention_kernel, group=group, tokens=tokens),
        in_specs=[
            pl.BlockSpec(memory_space=smem),
            pl.BlockSpec(memory_space=smem),
            vmem_spec,
            vmem_spec,
            vmem_spec,
            any_spec,
            any_spec,
            any_spec,
            any_spec,
        ],
        out_specs=vmem_spec,
        out_shape=jax.ShapeDtypeStruct((tokens, QUERY_HEADS * HEAD_SIZE), jnp.bfloat16),
        scratch_shapes=[
            pltpu.VMEM((KEY_VALUE_HEADS, cache_rows, HEAD_SIZE), jnp.bfloat16),
            pltpu.VMEM((KEY_VALUE_HEADS, cache_rows, HEAD_SIZE), jnp.bfloat16),
            pltpu.SemaphoreType.DMA((2, KEY_VALUE_HEADS, max_pages)),
            pltpu.VMEM((group * tokens, HEAD_SIZE), jnp.float32),
            pltpu.VMEM((group * tokens, HEAD_SIZE), jnp.float32),
            pltpu.VMEM((group * tokens, HEAD_SIZE), jnp.float32),
        ],
    )(meta, page_ids, queries, new_keys, new_values, k_own, v_own, k_got, v_got)


def on_device(
    tokens,
    norm1_gain,
    query_key_value_weight,
    w_out,
    norm2_gain,
    router_weight,
    w_gate_up,
    w_down,
    routes,
    key_page_store,
    value_page_store,
    page_table,
    cached_pages,
    anchor,
):
    req_index = lax.axis_index("req")
    head_index = lax.axis_index("head")
    count_of_heads = lax.axis_size("head")
    req_count = lax.axis_size("req")
    tokens_per_device = tokens.shape[0]
    req_dev = page_table.shape[0]
    page_size = key_page_store.shape[1]
    share = REQUEST_TOKENS // tokens_per_device
    kv_width = KEY_VALUE_HEADS * HEAD_SIZE

    request = (req_index * count_of_heads + head_index) // share
    half = head_index % share
    request_ids = jnp.arange(anchor.shape[0], dtype=jnp.int32)
    old_id = jnp.sum(jnp.where(request_ids == request, anchor, 0))
    base_pages = jnp.sum(jnp.where(request_ids == old_id, cached_pages, 0))
    place = half * tokens_per_device + jnp.arange(tokens_per_device, dtype=jnp.int32)
    token_positions = base_pages * page_size + place

    normed = rms_scale(tokens.astype(jnp.float32), norm1_gain).astype(jnp.bfloat16)
    projected_rows = jnp.dot(normed, query_key_value_weight, preferred_element_type=jnp.float32)
    half_dim = HEAD_SIZE // 2
    frequency = jnp.exp(
        -jnp.log(jnp.float32(THETA))
        * jnp.arange(half_dim, dtype=jnp.float32)
        * 2.0
        / HEAD_SIZE
    )
    angles = token_positions.astype(jnp.float32)[:, None] * frequency[None, :]
    cosine = jnp.cos(angles)
    sines = jnp.sin(angles)
    queries, appended = rotate(
        projected_rows,
        jnp.concatenate([cosine, cosine], axis=1),
        jnp.concatenate([-sines, sines], axis=1),
    )

    forward_pairs = [
        (h, h + 1) for h in range(count_of_heads) if h % share != share - 1
    ]
    earlier = lax.ppermute(appended, "head", forward_pairs)
    pairs = [(source, source ^ 1) for source in range(req_count)]
    k_got, v_got, table_got = lax.ppermute(
        (key_page_store, value_page_store, page_table), "req", pairs
    )
    moved_in = old_id // req_dev != req_index
    row_pick = (jnp.arange(req_dev, dtype=jnp.int32) == old_id % req_dev)[:, None]
    page_ids = jnp.sum(jnp.where(row_pick, jnp.where(moved_in, table_got, page_table), 0), axis=0)
    meta = jnp.stack(
        [base_pages, half.astype(jnp.int32), moved_in.astype(jnp.int32)]
    ).astype(jnp.int32)
    attention = attend(
        meta, page_ids, queries, appended, earlier, key_page_store, value_page_store, k_got, v_got,
    )

    residual = tokens.astype(jnp.float32) + jnp.dot(
        attention, w_out, preferred_element_type=jnp.float32
    )
    normed_moe = rms_scale(residual, norm2_gain).astype(jnp.bfloat16)
    logits = jnp.dot(normed_moe.astype(jnp.float32), router_weight, precision=lax.Precision.HIGHEST)
    route_match = routes[:, :, None] == jnp.arange(logits.shape[1], dtype=jnp.int32)[None, None, :]
    chosen = jnp.sum(jnp.where(route_match, logits[:, None, :], 0.0), axis=2)
    sigmoids = jax.nn.sigmoid(chosen)
    route_gates = sigmoids / jnp.sum(sigmoids, axis=1, keepdims=True)

    exp_dev = w_gate_up.shape[0]
    expert_total = exp_dev * req_count
    capacity = max(2, 3 * tokens_per_device * TOPK // (2 * expert_total))
    slot_total = expert_total * capacity
    flat_ids = routes.reshape(-1)
    route_rows = flat_ids.shape[0]
    one_hot = (flat_ids[:, None] == jnp.arange(expert_total, dtype=jnp.int32)[None, :]).astype(
        jnp.bfloat16
    )
    row_i = lax.broadcasted_iota(jnp.int32, (route_rows, route_rows), 0)
    col_i = lax.broadcasted_iota(jnp.int32, (route_rows, route_rows), 1)
    before = (col_i < row_i).astype(jnp.bfloat16)
    earlier_counts = jnp.dot(before, one_hot, preferred_element_type=jnp.float32)
    slot_ranks = jnp.sum(earlier_counts * one_hot.astype(jnp.float32), axis=1).astype(jnp.int32)
    slot_ids = (flat_ids * capacity + slot_ranks).reshape(tokens_per_device, TOPK)

    slot_iota = jnp.arange(slot_total, dtype=jnp.int32)
    hits = slot_ids[None, :, :] == slot_iota[:, None, None]
    gather_matrix = jnp.any(hits, axis=2).astype(jnp.bfloat16)
    dispatch = jnp.dot(gather_matrix, normed_moe, preferred_element_type=jnp.float32).astype(
        jnp.bfloat16
    )
    dispatch = dispatch.reshape(req_count, exp_dev, capacity, MODEL_WIDTH)
    gate_up = jnp.einsum(
        "nekd,edf->nekf",
        lax.all_to_all(dispatch, "req", split_axis=0, concat_axis=0, tiled=True),
        w_gate_up,
        preferred_element_type=jnp.float32,
    )
    hidden = (jax.nn.relu(gate_up[..., :FE]) * gate_up[..., FE:]).astype(jnp.bfloat16)
    result = jnp.einsum(
        "nekf,efd->nekd", hidden, w_down, preferred_element_type=jnp.float32
    ).astype(jnp.bfloat16)
    results = lax.all_to_all(result, "req", split_axis=0, concat_axis=0, tiled=True)
    flat_results = results.reshape(slot_total, MODEL_WIDTH)

    token_hits = slot_ids[:, :, None] == slot_iota[None, None, :]
    combine = jnp.sum(jnp.where(token_hits, route_gates[:, :, None], 0.0), axis=1)
    expert_sum = jnp.dot(
        combine.astype(jnp.bfloat16), flat_results, preferred_element_type=jnp.float32
    )
    mixed_out = (residual + expert_sum).astype(jnp.bfloat16)
    return (mixed_out, appended)


def solution(mesh):
    return jax.shard_map(
        on_device,
        mesh=mesh,
        in_specs=(
            P(("req", "head"), None),
            P(),
            P(),
            P(),
            P(),
            P(),
            P("req", None, None),
            P("req", None, None),
            P(("req", "head"), None),
            P("req", None, None),
            P("req", None, None),
            P("req", None),
            P(),
            P(),
        ),
        out_specs=(P(("req", "head"), None), P(("req", "head"), None)),
        check_vma=False,
    )
```

```python
import functools

import jax
import jax.numpy as jnp
from jax import lax
from jax.experimental import pallas as pl
from jax.experimental.pallas import tpu as pltpu
from jax.sharding import PartitionSpec as P

MODEL_WIDTH = 1536
QUERY_HEADS = 12
KEY_VALUE_HEADS = 2
HEAD_SIZE = 128
FE = 768
TOPK = 4
REQUEST_TOKENS = 512
PAGE_CHUNK = 128


EPS = 1e-06
THETA = 1000000.0


def rms_scale(values, gain_vector):
    mean_sq = jnp.mean(values * values, axis=-1, keepdims=True)
    return values * lax.rsqrt(mean_sq + EPS) * gain_vector


def apply_rotary(values, where_at):
    half_dim = values.shape[-1] // 2
    frequency = jnp.exp(
        -jnp.log(jnp.float32(THETA))
        * jnp.arange(half_dim, dtype=jnp.float32)
        * 2.0
        / values.shape[-1]
    )
    angles = where_at.astype(jnp.float32)[:, None] * frequency[None, :]
    cosine = jnp.cos(angles)[:, None, :]
    sines = jnp.sin(angles)[:, None, :]
    first_half = values[..., :half_dim]
    second = values[..., half_dim:]
    return jnp.concatenate(
        [first_half * cosine - second * sines, second * cosine + first_half * sines], axis=-1
    )


def rotary_kernel(proj_ref, cos_ref, sin_ref, q_ref, app_ref):
    cosine = cos_ref[...]
    sines = sin_ref[...]
    for h in range(QUERY_HEADS + KEY_VALUE_HEADS):
        x = proj_ref[:, h * HEAD_SIZE : (h + 1) * HEAD_SIZE]
        swapped = pltpu.roll(x, HEAD_SIZE // 2, 1)
        r = (x * cosine + swapped * sines).astype(jnp.bfloat16)
        if h < QUERY_HEADS:
            q_ref[:, h * HEAD_SIZE : (h + 1) * HEAD_SIZE] = r
        else:
            k = h - QUERY_HEADS
            app_ref[:, k * HEAD_SIZE : (k + 1) * HEAD_SIZE] = r
    base = (QUERY_HEADS + KEY_VALUE_HEADS) * HEAD_SIZE
    width = KEY_VALUE_HEADS * HEAD_SIZE
    app_ref[:, width : 2 * width] = proj_ref[:, base : base + width].astype(jnp.bfloat16)


def rotate(projected_rows, cosine, sines):
    tokens = projected_rows.shape[0]
    vmem_spec = pl.BlockSpec(memory_space=pltpu.VMEM)
    return pl.pallas_call(
        rotary_kernel,
        in_specs=[vmem_spec, vmem_spec, vmem_spec],
        out_specs=(vmem_spec, vmem_spec),
        out_shape=(
            jax.ShapeDtypeStruct((tokens, QUERY_HEADS * HEAD_SIZE), jnp.bfloat16),
            jax.ShapeDtypeStruct((tokens, 2 * KEY_VALUE_HEADS * HEAD_SIZE), jnp.bfloat16),
        ),
    )(projected_rows, cosine, sines)


def attention_kernel(
    meta_ref, page_ref, q_ref, kn_ref, vn_ref, k_own, v_own, k_got, v_got,
    o_ref, k_buf, v_buf, sems, m_sc, l_sc, acc_sc, *, group, tokens
):
    count = meta_ref[0]
    half = meta_ref[1]
    moved = meta_ref[2]
    scaling = HEAD_SIZE ** (-0.5)
    contract = (((1,), (1,)), ((), ()))
    lanes = HEAD_SIZE

    def page_copies(c, j, k_pool, v_pool):
        page = page_ref[j]
        rows = pl.ds(pl.multiple_of(j * PAGE_CHUNK, PAGE_CHUNK), PAGE_CHUNK)
        cols = pl.ds(c * HEAD_SIZE, HEAD_SIZE)
        return (
            pltpu.make_async_copy(k_pool.at[page, :, cols], k_buf.at[c, rows, :], sems.at[0, c, j]),
            pltpu.make_async_copy(v_pool.at[page, :, cols], v_buf.at[c, rows, :], sems.at[1, c, j]),
        )

    def start_all(k_pool, v_pool):
        for c in range(KEY_VALUE_HEADS):
            def body(j, carry):
                for copy in page_copies(c, j, k_pool, v_pool):
                    copy.start()
                return carry
            lax.fori_loop(0, count, body, 0)

    @pl.when(moved == 1)
    def _():
        start_all(k_got, v_got)

    @pl.when(moved == 0)
    def _():
        start_all(k_own, v_own)

    def absorb(qg, k, v):
        s = lax.dot_general(qg, k, contract, preferred_element_type=jnp.float32) * scaling
        m_prev = m_sc[...]
        m_next = jnp.maximum(m_prev, jnp.max(s, axis=1, keepdims=True))
        repeat = s.shape[1] // lanes
        wide = m_next if repeat == 1 else jnp.concatenate([m_next] * repeat, axis=1)
        p = jnp.exp(s - wide)
        alpha = jnp.exp(m_prev - m_next)
        l_sc[...] = alpha * l_sc[...] + jnp.sum(p, axis=1, keepdims=True)
        acc_sc[...] = acc_sc[...] * alpha + jnp.dot(
            p.astype(jnp.bfloat16), v, preferred_element_type=jnp.float32
        )
        m_sc[...] = m_next

    for c in range(KEY_VALUE_HEADS):
        heads = range(c * group, (c + 1) * group)
        qg = jnp.concatenate(
            [q_ref[:, g * HEAD_SIZE : (g + 1) * HEAD_SIZE] for g in heads], axis=0
        )
        key_cols = slice(c * HEAD_SIZE, (c + 1) * HEAD_SIZE)
        value_cols = slice((KEY_VALUE_HEADS + c) * HEAD_SIZE, (KEY_VALUE_HEADS + c + 1) * HEAD_SIZE)
        s = lax.dot_general(qg, kn_ref[:, key_cols], contract, preferred_element_type=jnp.float32)
        s = s * scaling
        t = lax.broadcasted_iota(jnp.int32, s.shape, 0) % tokens
        key_pos = lax.broadcasted_iota(jnp.int32, s.shape, 1)
        s = jnp.where(key_pos <= t, s, -jnp.inf)
        m = jnp.max(s, axis=1, keepdims=True)
        p = jnp.exp(s - m)
        l_sc[...] = jnp.broadcast_to(jnp.sum(p, axis=1, keepdims=True), l_sc.shape)
        m_sc[...] = jnp.broadcast_to(m, m_sc.shape)
        acc_sc[...] = jnp.dot(
            p.astype(jnp.bfloat16), kn_ref[:, value_cols], preferred_element_type=jnp.float32
        )

        @pl.when(half == 1)
        def _():
            absorb(qg, vn_ref[:, key_cols], vn_ref[:, value_cols])

        def wait_page(j, carry):
            for copy in page_copies(c, j, k_own, v_own):
                copy.wait()
            return carry

        lax.fori_loop(0, count, wait_page, 0)

        def visit(i, carry):
            first = pl.multiple_of(i * (4 * PAGE_CHUNK), 4 * PAGE_CHUNK)
            absorb(
                qg,
                k_buf[c, pl.ds(first, 4 * PAGE_CHUNK), :],
                v_buf[c, pl.ds(first, 4 * PAGE_CHUNK), :],
            )
            return carry

        lax.fori_loop(0, count // 4, visit, 0)

        @pl.when(count % 4 >= 2)
        def _():
            first = pl.multiple_of((count // 4) * (4 * PAGE_CHUNK), 4 * PAGE_CHUNK)
            absorb(
                qg,
                k_buf[c, pl.ds(first, 2 * PAGE_CHUNK), :],
                v_buf[c, pl.ds(first, 2 * PAGE_CHUNK), :],
            )

        @pl.when(count % 2 == 1)
        def _():
            first = pl.multiple_of((count - 1) * PAGE_CHUNK, PAGE_CHUNK)
            absorb(
                qg,
                k_buf[c, pl.ds(first, PAGE_CHUNK), :],
                v_buf[c, pl.ds(first, PAGE_CHUNK), :],
            )

        res = (acc_sc[...] / l_sc[...]).astype(jnp.bfloat16)
        for i, g in enumerate(heads):
            o_ref[:, g * HEAD_SIZE : (g + 1) * HEAD_SIZE] = res[i * tokens : (i + 1) * tokens]


def attend(meta, page_ids, queries, new_keys, new_values, k_own, v_own, k_got, v_got):
    tokens = queries.shape[0]
    group = QUERY_HEADS // KEY_VALUE_HEADS
    max_pages = page_ids.shape[0]
    cache_rows = max_pages * PAGE_CHUNK
    smem = pltpu.MemorySpace.SMEM if hasattr(pltpu, "MemorySpace") else pltpu.SMEM
    vmem_spec = pl.BlockSpec(memory_space=pltpu.VMEM)
    any_spec = pl.BlockSpec(memory_space=pl.ANY)
    return pl.pallas_call(
        functools.partial(attention_kernel, group=group, tokens=tokens),
        in_specs=[
            pl.BlockSpec(memory_space=smem),
            pl.BlockSpec(memory_space=smem),
            vmem_spec,
            vmem_spec,
            vmem_spec,
            any_spec,
            any_spec,
            any_spec,
            any_spec,
        ],
        out_specs=vmem_spec,
        out_shape=jax.ShapeDtypeStruct((tokens, QUERY_HEADS * HEAD_SIZE), jnp.bfloat16),
        scratch_shapes=[
            pltpu.VMEM((KEY_VALUE_HEADS, cache_rows, HEAD_SIZE), jnp.bfloat16),
            pltpu.VMEM((KEY_VALUE_HEADS, cache_rows, HEAD_SIZE), jnp.bfloat16),
            pltpu.SemaphoreType.DMA((2, KEY_VALUE_HEADS, max_pages)),
            pltpu.VMEM((group * tokens, HEAD_SIZE), jnp.float32),
            pltpu.VMEM((group * tokens, HEAD_SIZE), jnp.float32),
            pltpu.VMEM((group * tokens, HEAD_SIZE), jnp.float32),
        ],
    )(meta, page_ids, queries, new_keys, new_values, k_own, v_own, k_got, v_got)


def on_device(
    tokens,
    norm1_gain,
    query_key_value_weight,
    w_out,
    norm2_gain,
    router_weight,
    w_gate_up,
    w_down,
    routes,
    key_page_store,
    value_page_store,
    page_table,
    cached_pages,
    anchor,
):
    req_index = lax.axis_index("req")
    head_index = lax.axis_index("head")
    count_of_heads = lax.axis_size("head")
    req_count = lax.axis_size("req")
    tokens_per_device = tokens.shape[0]
    req_dev = page_table.shape[0]
    page_size = key_page_store.shape[1]
    share = REQUEST_TOKENS // tokens_per_device
    kv_width = KEY_VALUE_HEADS * HEAD_SIZE

    request = (req_index * count_of_heads + head_index) // share
    half = head_index % share
    old_id = anchor[request]
    place = half * tokens_per_device + jnp.arange(tokens_per_device, dtype=jnp.int32)
    token_positions = cached_pages[old_id] * page_size + place

    normed = rms_scale(tokens.astype(jnp.float32), norm1_gain).astype(jnp.bfloat16)
    projected_rows = jnp.dot(normed, query_key_value_weight, preferred_element_type=jnp.float32)
    half_dim = HEAD_SIZE // 2
    frequency = jnp.exp(
        -jnp.log(jnp.float32(THETA))
        * jnp.arange(half_dim, dtype=jnp.float32)
        * 2.0
        / HEAD_SIZE
    )
    angles = token_positions.astype(jnp.float32)[:, None] * frequency[None, :]
    cosine = jnp.cos(angles)
    sines = jnp.sin(angles)
    queries, appended = rotate(
        projected_rows,
        jnp.concatenate([cosine, cosine], axis=1),
        jnp.concatenate([-sines, sines], axis=1),
    )

    forward_pairs = [
        (h, h + 1) for h in range(count_of_heads) if h % share != share - 1
    ]
    earlier = lax.ppermute(appended, "head", forward_pairs)
    pairs = [(source, source ^ 1) for source in range(req_count)]
    k_got, v_got, table_got = lax.ppermute(
        (key_page_store, value_page_store, page_table), "req", pairs
    )
    moved_in = old_id // req_dev != req_index
    page_ids = jnp.where(moved_in, table_got[old_id % req_dev], page_table[old_id % req_dev])
    meta = jnp.stack(
        [cached_pages[old_id], half.astype(jnp.int32), moved_in.astype(jnp.int32)]
    ).astype(jnp.int32)
    attention = attend(
        meta, page_ids, queries, appended, earlier, key_page_store, value_page_store, k_got, v_got,
    )

    residual = tokens.astype(jnp.float32) + jnp.dot(
        attention, w_out, preferred_element_type=jnp.float32
    )
    normed_moe = rms_scale(residual, norm2_gain).astype(jnp.bfloat16)
    logits = jnp.dot(normed_moe.astype(jnp.float32), router_weight, precision=lax.Precision.HIGHEST)
    route_match = routes[:, :, None] == jnp.arange(logits.shape[1], dtype=jnp.int32)[None, None, :]
    chosen = jnp.sum(jnp.where(route_match, logits[:, None, :], 0.0), axis=2)
    sigmoids = jax.nn.sigmoid(chosen)
    route_gates = sigmoids / jnp.sum(sigmoids, axis=1, keepdims=True)

    exp_dev = w_gate_up.shape[0]
    expert_total = exp_dev * req_count
    capacity = max(2, 3 * tokens_per_device * TOPK // (2 * expert_total))
    slot_total = expert_total * capacity
    flat_ids = routes.reshape(-1)
    route_rows = flat_ids.shape[0]
    route_hits = routes[:, :, None] == jnp.arange(expert_total, dtype=jnp.int32)[None, None, :]
    per_token = jnp.sum(route_hits.astype(jnp.int32), axis=1).astype(jnp.bfloat16)
    row_i = lax.broadcasted_iota(jnp.int32, (tokens_per_device, tokens_per_device), 0)
    col_i = lax.broadcasted_iota(jnp.int32, (tokens_per_device, tokens_per_device), 1)
    before = (col_i < row_i).astype(jnp.bfloat16)
    earlier_counts = jnp.dot(before, per_token, preferred_element_type=jnp.float32)
    slot_ranks = jnp.sum(
        jnp.where(route_hits, earlier_counts[:, None, :], 0.0), axis=2
    ).astype(jnp.int32)
    slot_ids = routes * capacity + slot_ranks

    slot_iota = jnp.arange(slot_total, dtype=jnp.int32)
    hits = slot_ids[None, :, :] == slot_iota[:, None, None]
    gather_matrix = jnp.any(hits, axis=2).astype(jnp.bfloat16)
    dispatch = jnp.dot(gather_matrix, normed_moe, preferred_element_type=jnp.float32).astype(
        jnp.bfloat16
    )
    dispatch = dispatch.reshape(req_count, exp_dev, capacity, MODEL_WIDTH)
    gate_up = jnp.einsum(
        "nekd,edf->nekf",
        lax.all_to_all(dispatch, "req", split_axis=0, concat_axis=0, tiled=True),
        w_gate_up,
        preferred_element_type=jnp.float32,
    )
    hidden = (jax.nn.relu(gate_up[..., :FE]) * gate_up[..., FE:]).astype(jnp.bfloat16)
    result = jnp.einsum(
        "nekf,efd->nekd", hidden, w_down, preferred_element_type=jnp.float32
    ).astype(jnp.bfloat16)
    results = lax.all_to_all(result, "req", split_axis=0, concat_axis=0, tiled=True)
    flat_results = results.reshape(slot_total, MODEL_WIDTH)

    token_hits = slot_ids[:, :, None] == slot_iota[None, None, :]
    combine = jnp.sum(jnp.where(token_hits, route_gates[:, :, None], 0.0), axis=1)
    expert_sum = jnp.dot(
        combine.astype(jnp.bfloat16), flat_results, preferred_element_type=jnp.float32
    )
    mixed_out = (residual + expert_sum).astype(jnp.bfloat16)
    return (mixed_out, appended)


def solution(mesh):
    return jax.shard_map(
        on_device,
        mesh=mesh,
        in_specs=(
            P(("req", "head"), None),
            P(),
            P(),
            P(),
            P(),
            P(),
            P("req", None, None),
            P("req", None, None),
            P(("req", "head"), None),
            P("req", None, None),
            P("req", None, None),
            P("req", None),
            P(),
            P(),
        ),
        out_specs=(P(("req", "head"), None), P(("req", "head"), None)),
        check_vma=False,
    )
```

```python
import functools

import jax
import jax.numpy as jnp
from jax import lax
from jax.experimental import pallas as pl
from jax.experimental.pallas import tpu as pltpu
from jax.sharding import PartitionSpec as P

MODEL_WIDTH = 1536
QUERY_HEADS = 12
KEY_VALUE_HEADS = 2
HEAD_SIZE = 128
FE = 768
TOPK = 4
REQUEST_TOKENS = 512
PAGE_CHUNK = 128


EPS = 1e-06
THETA = 1000000.0


def rms_scale(values, gain_vector):
    mean_sq = jnp.mean(values * values, axis=-1, keepdims=True)
    return values * lax.rsqrt(mean_sq + EPS) * gain_vector


def apply_rotary(values, where_at):
    half_dim = values.shape[-1] // 2
    frequency = jnp.exp(
        -jnp.log(jnp.float32(THETA))
        * jnp.arange(half_dim, dtype=jnp.float32)
        * 2.0
        / values.shape[-1]
    )
    angles = where_at.astype(jnp.float32)[:, None] * frequency[None, :]
    cosine = jnp.cos(angles)[:, None, :]
    sines = jnp.sin(angles)[:, None, :]
    first_half = values[..., :half_dim]
    second = values[..., half_dim:]
    return jnp.concatenate(
        [first_half * cosine - second * sines, second * cosine + first_half * sines], axis=-1
    )


def rotary_kernel(proj_ref, cos_ref, sin_ref, q_ref, app_ref):
    cosine = cos_ref[...]
    sines = sin_ref[...]
    for h in range(QUERY_HEADS + KEY_VALUE_HEADS):
        x = proj_ref[:, h * HEAD_SIZE : (h + 1) * HEAD_SIZE]
        swapped = pltpu.roll(x, HEAD_SIZE // 2, 1)
        r = (x * cosine + swapped * sines).astype(jnp.bfloat16)
        if h < QUERY_HEADS:
            q_ref[:, h * HEAD_SIZE : (h + 1) * HEAD_SIZE] = r
        else:
            k = h - QUERY_HEADS
            app_ref[:, k * HEAD_SIZE : (k + 1) * HEAD_SIZE] = r
    base = (QUERY_HEADS + KEY_VALUE_HEADS) * HEAD_SIZE
    width = KEY_VALUE_HEADS * HEAD_SIZE
    app_ref[:, width : 2 * width] = proj_ref[:, base : base + width].astype(jnp.bfloat16)


def rotate(projected_rows, cosine, sines):
    tokens = projected_rows.shape[0]
    vmem_spec = pl.BlockSpec(memory_space=pltpu.VMEM)
    return pl.pallas_call(
        rotary_kernel,
        in_specs=[vmem_spec, vmem_spec, vmem_spec],
        out_specs=(vmem_spec, vmem_spec),
        out_shape=(
            jax.ShapeDtypeStruct((tokens, QUERY_HEADS * HEAD_SIZE), jnp.bfloat16),
            jax.ShapeDtypeStruct((tokens, 2 * KEY_VALUE_HEADS * HEAD_SIZE), jnp.bfloat16),
        ),
    )(projected_rows, cosine, sines)


def attention_kernel(
    meta_ref, page_ref, q_ref, kn_ref, vn_ref, k_own, v_own, k_got, v_got,
    o_ref, k_buf, v_buf, sems, m_sc, l_sc, acc_sc, *, group, tokens
):
    count = meta_ref[0]
    half = meta_ref[1]
    moved = meta_ref[2]
    scaling = HEAD_SIZE ** (-0.5)
    contract = (((1,), (1,)), ((), ()))
    lanes = HEAD_SIZE

    def page_copies(c, j, k_pool, v_pool):
        page = page_ref[j]
        rows = pl.ds(pl.multiple_of(j * PAGE_CHUNK, PAGE_CHUNK), PAGE_CHUNK)
        cols = pl.ds(c * HEAD_SIZE, HEAD_SIZE)
        return (
            pltpu.make_async_copy(k_pool.at[page, :, cols], k_buf.at[c, rows, :], sems.at[0, c, j]),
            pltpu.make_async_copy(v_pool.at[page, :, cols], v_buf.at[c, rows, :], sems.at[1, c, j]),
        )

    def start_all(k_pool, v_pool):
        for c in range(KEY_VALUE_HEADS):
            def body(j, carry):
                for copy in page_copies(c, j, k_pool, v_pool):
                    copy.start()
                return carry
            lax.fori_loop(0, count, body, 0)

    @pl.when(moved == 1)
    def _():
        start_all(k_got, v_got)

    @pl.when(moved == 0)
    def _():
        start_all(k_own, v_own)

    def absorb(qg, k, v):
        s = lax.dot_general(qg, k, contract, preferred_element_type=jnp.float32)
        m_prev = m_sc[...]
        m_next = jnp.maximum(m_prev, jnp.max(s, axis=1, keepdims=True) * scaling)
        repeat = s.shape[1] // lanes
        wide = m_next if repeat == 1 else jnp.concatenate([m_next] * repeat, axis=1)
        p = jnp.exp(s * scaling - wide)
        alpha = jnp.exp(m_prev - m_next)
        l_sc[...] = alpha * l_sc[...] + jnp.sum(p, axis=1, keepdims=True)
        acc_sc[...] = acc_sc[...] * alpha + jnp.dot(
            p.astype(jnp.bfloat16), v, preferred_element_type=jnp.float32
        )
        m_sc[...] = m_next

    for c in range(KEY_VALUE_HEADS):
        heads = range(c * group, (c + 1) * group)
        qg = jnp.concatenate(
            [q_ref[:, g * HEAD_SIZE : (g + 1) * HEAD_SIZE] for g in heads], axis=0
        )
        key_cols = slice(c * HEAD_SIZE, (c + 1) * HEAD_SIZE)
        value_cols = slice((KEY_VALUE_HEADS + c) * HEAD_SIZE, (KEY_VALUE_HEADS + c + 1) * HEAD_SIZE)
        s = lax.dot_general(qg, kn_ref[:, key_cols], contract, preferred_element_type=jnp.float32)
        t = lax.broadcasted_iota(jnp.int32, s.shape, 0) % tokens
        key_pos = lax.broadcasted_iota(jnp.int32, s.shape, 1)
        s = jnp.where(key_pos <= t, s, -jnp.inf)
        m = jnp.max(s, axis=1, keepdims=True) * scaling
        p = jnp.exp(s * scaling - m)
        l_sc[...] = jnp.broadcast_to(jnp.sum(p, axis=1, keepdims=True), l_sc.shape)
        m_sc[...] = jnp.broadcast_to(m, m_sc.shape)
        acc_sc[...] = jnp.dot(
            p.astype(jnp.bfloat16), kn_ref[:, value_cols], preferred_element_type=jnp.float32
        )

        @pl.when(half == 1)
        def _():
            absorb(qg, vn_ref[:, key_cols], vn_ref[:, value_cols])

        def wait_page(j, carry):
            for copy in page_copies(c, j, k_own, v_own):
                copy.wait()
            return carry

        lax.fori_loop(0, count, wait_page, 0)

        def visit(i, carry):
            first = pl.multiple_of(i * (4 * PAGE_CHUNK), 4 * PAGE_CHUNK)
            absorb(
                qg,
                k_buf[c, pl.ds(first, 4 * PAGE_CHUNK), :],
                v_buf[c, pl.ds(first, 4 * PAGE_CHUNK), :],
            )
            return carry

        lax.fori_loop(0, count // 4, visit, 0)

        @pl.when(count % 4 >= 2)
        def _():
            first = pl.multiple_of((count // 4) * (4 * PAGE_CHUNK), 4 * PAGE_CHUNK)
            absorb(
                qg,
                k_buf[c, pl.ds(first, 2 * PAGE_CHUNK), :],
                v_buf[c, pl.ds(first, 2 * PAGE_CHUNK), :],
            )

        @pl.when(count % 2 == 1)
        def _():
            first = pl.multiple_of((count - 1) * PAGE_CHUNK, PAGE_CHUNK)
            absorb(
                qg,
                k_buf[c, pl.ds(first, PAGE_CHUNK), :],
                v_buf[c, pl.ds(first, PAGE_CHUNK), :],
            )

        res = (acc_sc[...] / l_sc[...]).astype(jnp.bfloat16)
        for i, g in enumerate(heads):
            o_ref[:, g * HEAD_SIZE : (g + 1) * HEAD_SIZE] = res[i * tokens : (i + 1) * tokens]


def attend(meta, page_ids, queries, new_keys, new_values, k_own, v_own, k_got, v_got):
    tokens = queries.shape[0]
    group = QUERY_HEADS // KEY_VALUE_HEADS
    max_pages = page_ids.shape[0]
    cache_rows = max_pages * PAGE_CHUNK
    smem = pltpu.MemorySpace.SMEM if hasattr(pltpu, "MemorySpace") else pltpu.SMEM
    vmem_spec = pl.BlockSpec(memory_space=pltpu.VMEM)
    any_spec = pl.BlockSpec(memory_space=pl.ANY)
    return pl.pallas_call(
        functools.partial(attention_kernel, group=group, tokens=tokens),
        in_specs=[
            pl.BlockSpec(memory_space=smem),
            pl.BlockSpec(memory_space=smem),
            vmem_spec,
            vmem_spec,
            vmem_spec,
            any_spec,
            any_spec,
            any_spec,
            any_spec,
        ],
        out_specs=vmem_spec,
        out_shape=jax.ShapeDtypeStruct((tokens, QUERY_HEADS * HEAD_SIZE), jnp.bfloat16),
        scratch_shapes=[
            pltpu.VMEM((KEY_VALUE_HEADS, cache_rows, HEAD_SIZE), jnp.bfloat16),
            pltpu.VMEM((KEY_VALUE_HEADS, cache_rows, HEAD_SIZE), jnp.bfloat16),
            pltpu.SemaphoreType.DMA((2, KEY_VALUE_HEADS, max_pages)),
            pltpu.VMEM((group * tokens, HEAD_SIZE), jnp.float32),
            pltpu.VMEM((group * tokens, HEAD_SIZE), jnp.float32),
            pltpu.VMEM((group * tokens, HEAD_SIZE), jnp.float32),
        ],
    )(meta, page_ids, queries, new_keys, new_values, k_own, v_own, k_got, v_got)


def on_device(
    tokens,
    norm1_gain,
    query_key_value_weight,
    w_out,
    norm2_gain,
    router_weight,
    w_gate_up,
    w_down,
    routes,
    key_page_store,
    value_page_store,
    page_table,
    cached_pages,
    anchor,
):
    req_index = lax.axis_index("req")
    head_index = lax.axis_index("head")
    count_of_heads = lax.axis_size("head")
    req_count = lax.axis_size("req")
    tokens_per_device = tokens.shape[0]
    req_dev = page_table.shape[0]
    page_size = key_page_store.shape[1]
    share = REQUEST_TOKENS // tokens_per_device
    kv_width = KEY_VALUE_HEADS * HEAD_SIZE

    request = (req_index * count_of_heads + head_index) // share
    half = head_index % share
    request_ids = jnp.arange(anchor.shape[0], dtype=jnp.int32)
    old_id = jnp.sum(jnp.where(request_ids == request, anchor, 0))
    base_pages = jnp.sum(jnp.where(request_ids == old_id, cached_pages, 0))
    place = half * tokens_per_device + jnp.arange(tokens_per_device, dtype=jnp.int32)
    token_positions = base_pages * page_size + place

    normed = rms_scale(tokens.astype(jnp.float32), norm1_gain).astype(jnp.bfloat16)
    projected_rows = jnp.dot(normed, query_key_value_weight, preferred_element_type=jnp.float32)
    half_dim = HEAD_SIZE // 2
    frequency = jnp.exp(
        -jnp.log(jnp.float32(THETA))
        * jnp.arange(half_dim, dtype=jnp.float32)
        * 2.0
        / HEAD_SIZE
    )
    angles = token_positions.astype(jnp.float32)[:, None] * frequency[None, :]
    cosine = jnp.cos(angles)
    sines = jnp.sin(angles)
    queries, appended = rotate(
        projected_rows,
        jnp.concatenate([cosine, cosine], axis=1),
        jnp.concatenate([-sines, sines], axis=1),
    )

    forward_pairs = [
        (h, h + 1) for h in range(count_of_heads) if h % share != share - 1
    ]
    earlier = lax.ppermute(appended, "head", forward_pairs)
    pairs = [(source, source ^ 1) for source in range(req_count)]
    k_got, v_got, table_got = lax.ppermute(
        (key_page_store, value_page_store, page_table), "req", pairs
    )
    moved_in = old_id // req_dev != req_index
    row_pick = (jnp.arange(req_dev, dtype=jnp.int32) == old_id % req_dev)[:, None]
    page_ids = jnp.sum(jnp.where(row_pick, jnp.where(moved_in, table_got, page_table), 0), axis=0)
    meta = jnp.stack(
        [base_pages, half.astype(jnp.int32), moved_in.astype(jnp.int32)]
    ).astype(jnp.int32)
    attention = attend(
        meta, page_ids, queries, appended, earlier, key_page_store, value_page_store, k_got, v_got,
    )

    residual = tokens.astype(jnp.float32) + jnp.dot(
        attention, w_out, preferred_element_type=jnp.float32
    )
    normed_moe = rms_scale(residual, norm2_gain).astype(jnp.bfloat16)
    logits = jnp.dot(normed_moe.astype(jnp.float32), router_weight, precision=lax.Precision.HIGHEST)
    route_match = routes[:, :, None] == jnp.arange(logits.shape[1], dtype=jnp.int32)[None, None, :]
    chosen = jnp.sum(jnp.where(route_match, logits[:, None, :], 0.0), axis=2)
    sigmoids = jax.nn.sigmoid(chosen)
    route_gates = sigmoids / jnp.sum(sigmoids, axis=1, keepdims=True)

    exp_dev = w_gate_up.shape[0]
    expert_total = exp_dev * req_count
    capacity = max(2, 3 * tokens_per_device * TOPK // (2 * expert_total))
    slot_total = expert_total * capacity
    flat_ids = routes.reshape(-1)
    route_rows = flat_ids.shape[0]
    route_hits = routes[:, :, None] == jnp.arange(expert_total, dtype=jnp.int32)[None, None, :]
    per_token = jnp.sum(route_hits.astype(jnp.int32), axis=1).astype(jnp.bfloat16)
    row_i = lax.broadcasted_iota(jnp.int32, (tokens_per_device, tokens_per_device), 0)
    col_i = lax.broadcasted_iota(jnp.int32, (tokens_per_device, tokens_per_device), 1)
    before = (col_i < row_i).astype(jnp.bfloat16)
    earlier_counts = jnp.dot(before, per_token, preferred_element_type=jnp.float32)
    slot_ranks = jnp.sum(
        jnp.where(route_hits, earlier_counts[:, None, :], 0.0), axis=2
    ).astype(jnp.int32)
    slot_ids = routes * capacity + slot_ranks

    slot_iota = jnp.arange(slot_total, dtype=jnp.int32)
    hits = slot_ids[None, :, :] == slot_iota[:, None, None]
    gather_matrix = jnp.any(hits, axis=2).astype(jnp.bfloat16)
    dispatch = jnp.dot(gather_matrix, normed_moe, preferred_element_type=jnp.float32).astype(
        jnp.bfloat16
    )
    dispatch = dispatch.reshape(req_count, exp_dev, capacity, MODEL_WIDTH)
    gate_up = jnp.einsum(
        "nekd,edf->nekf",
        lax.all_to_all(dispatch, "req", split_axis=0, concat_axis=0, tiled=True),
        w_gate_up,
        preferred_element_type=jnp.float32,
    )
    hidden = (jax.nn.relu(gate_up[..., :FE]) * gate_up[..., FE:]).astype(jnp.bfloat16)
    result = jnp.einsum(
        "nekf,efd->nekd", hidden, w_down, preferred_element_type=jnp.float32
    ).astype(jnp.bfloat16)
    results = lax.all_to_all(result, "req", split_axis=0, concat_axis=0, tiled=True)
    flat_results = results.reshape(slot_total, MODEL_WIDTH)

    token_hits = slot_ids[:, :, None] == slot_iota[None, None, :]
    combine = jnp.sum(jnp.where(token_hits, route_gates[:, :, None], 0.0), axis=1)
    expert_sum = jnp.dot(
        combine.astype(jnp.bfloat16), flat_results, preferred_element_type=jnp.float32
    )
    mixed_out = (residual + expert_sum).astype(jnp.bfloat16)
    return (mixed_out, appended)


def solution(mesh):
    return jax.shard_map(
        on_device,
        mesh=mesh,
        in_specs=(
            P(("req", "head"), None),
            P(),
            P(),
            P(),
            P(),
            P(),
            P("req", None, None),
            P("req", None, None),
            P(("req", "head"), None),
            P("req", None, None),
            P("req", None, None),
            P("req", None),
            P(),
            P(),
        ),
        out_specs=(P(("req", "head"), None), P(("req", "head"), None)),
        check_vma=False,
    )
```
